256 devices in a mesh: ctx: 32 (over x, y, core), head: 8 (over z).
Axes of the slice: x: 4, y: 4, z: 8, core: 2. Of those that a mesh axis runs over, the one named last changes fastest.
Arguments:
- mixer_input: bfloat16 [4096, 16384], P('ctx', 'head'), may hold values from -1200 to 1200
- gate: bfloat16 [4096, 16384], P('ctx', 'head'), may hold values from -6 to 6
- in_b: bfloat16 [4096, 2048], P('ctx', 'head'), may hold values from -6 to 6
- in_c: bfloat16 [4096, 2048], P('ctx', 'head'), may hold values from -0.375 to 0.375
- step_size: float32 [256, 4096], P('head', 'ctx'), may hold values from 0.5 to 2
- log_decay: float32 [256, 4096], P('head', 'ctx'), may hold values from -0.7 to 0
- skip_gain: float32 [256], P('head'), may hold values from 1 to 4
- norm_gain: float32 [16384], P('head'), may hold values from 0.5 to 1.5
- query_weight: bfloat16 [8, 2048, 1024], P('head'), may hold values from -0.125 to 0.125
- keys: bfloat16 [4096, 1024], P('ctx', 'head'), may hold values from -500 to 500
- values: bfloat16 [4096, 1024], P('ctx', 'head'), may hold values from -6 to 6
- doc_lengths: int32 [16], replicated, may hold values from 1 to 2176, 4096 in all
Outputs:
- mixer_out: bfloat16 [4096, 16384], P('ctx', 'head')
- attn_out: bfloat16 [4096, 8192], P('ctx', 'head')
The draws below stay inside these ranges and needn't reach their ends.
Inputs may be any that keep to these rules, and one draw needn't show every extreme that they name: `doc_lengths`: the documents lie end to end in token order, sum to 4096 tokens, and the longest has exactly 2176 tokens.
All inputs are finite; a program needn't handle non-finite values.
Results may differ from the reference program's by a relative error of at most 0.0151.
The reference program's roundings to bfloat16 on the way count: a program that leaves them out, or rounds other values in their place, can miss the bound.
Values may be sent and summed in bfloat16 or wider, within the bound.
No kernel may reach another device: no remote copies, remote signals or barrier semaphores. Data moves between devices by JAX's collectives and lax.ppermute only.
A program may use at most 192 MiB of HBM per device.

```python
import math
import jax
import jax.numpy as jnp
import numpy as np
from jax import lax

MIXER_HEADS = 256
HEAD_DIM = 64
STATE = 256
GROUPS = 8
QHEADS = 64
ATT_DIM = 128
TOK_DEV = 128
DOCS = 16
PACK_TOKENS = 4096
MOST = 2176


def draw_mixer_input(key, part):
    width = MIXER_HEADS * HEAD_DIM
    first_key = jax.random.fold_in(key, 0)
    normal_part = jnp.clip(jax.random.normal(first_key, (PACK_TOKENS, width), jnp.float32), -4.0, 4.0)
    column = jnp.arange(width, dtype=jnp.float32) / (width - 1)
    column_scale = (3.0 ** (0.5 * column))[None, :]
    return (normal_part * column_scale).astype(jnp.bfloat16)


def draw_log_decay(key, part):
    random_key_list = jax.random.split(key, 7)
    slow_share = 0.5
    slow_heads = jax.random.uniform(random_key_list[0], (MIXER_HEADS, 1), jnp.float32) < slow_share
    slow_rate = jax.random.uniform(random_key_list[1], (MIXER_HEADS, 1), jnp.float32, 0.1, 0.3) / PACK_TOKENS
    fast_rate = jax.random.uniform(random_key_list[2], (MIXER_HEADS, 1), jnp.float32, 0.04, 0.08)
    head_decay_rate = jnp.where(slow_heads, slow_rate, fast_rate)
    random_perturbation = jax.random.uniform(random_key_list[3], (MIXER_HEADS, PACK_TOKENS), jnp.float32, 0.5, 1.5)
    block_multiplier = jnp.exp(jax.random.uniform(random_key_list[4], (1, PACK_TOKENS // TOK_DEV), jnp.float32, -math.log(2.0), math.log(2.0)))
    block_multiplier = jnp.repeat(block_multiplier, TOK_DEV, axis=1)
    cluster_positions = jax.random.randint(random_key_list[5], (3,), 0, PACK_TOKENS)
    cluster_mask = jnp.any(jnp.arange(PACK_TOKENS, dtype=jnp.int32)[None, :] == cluster_positions[:, None], axis=0).astype(jnp.float32)
    cluster_size = jax.random.uniform(random_key_list[6], (MIXER_HEADS, 1), jnp.float32, 0.22, 0.45)
    return -(head_decay_rate * random_perturbation * block_multiplier) - cluster_mask[None, :] * cluster_size


def draw_keys(key, part):
    width = GROUPS * ATT_DIM
    first_key = jax.random.fold_in(key, 0)
    base = 3.0 * jnp.clip(jax.random.normal(first_key, (PACK_TOKENS, width), jnp.float32), -4.0, 4.0)
    return base.astype(jnp.bfloat16)


def levels(own_key, shape, pieces, least, high):
    loudness = 1.0
    for axis_at, shards_of in pieces:
        draws = jax.random.uniform(jax.random.fold_in(jax.random.fold_in(own_key, 6), axis_at), (shards_of,), jnp.float32, least / len(pieces), high / len(pieces))
        loudness = loudness * jnp.repeat(jnp.exp(draws), shape[axis_at] // shards_of).reshape((-1,) + (1,) * (len(shape) - 1 - axis_at))
    return loudness


def split_up(amount, total, bound, skew):
    weights = [(1 << 20) // math.isqrt(grade ** skew) + 1 for grade in range(2, amount + 1)]
    rest, holding = total - bound - (amount - 1), [1] * (amount - 1)
    while rest > 0:
        movable = [i for i in range(amount - 1) if holding[i] < bound]
        whole, left = sum([weights[i] for i in movable]), rest
        for i in movable:
            addition = min(bound - holding[i], max(1, left * weights[i] // whole), rest)
            holding[i] = holding[i] + addition
            rest = rest - addition
    return np.array([bound] + holding)


def uneven_parts(key, number_of, total, limit, slope):
    if number_of == 2:
        one = jax.random.randint(key, (), max(1, total - limit), min(limit, total - 1) + 1)
        return jnp.stack([one, total - one])
    sizes = jnp.asarray(split_up(number_of, total, limit, slope), jnp.int32)
    twos = (number_of - 1) // 2
    giver, taker = sizes[1:1 + 2 * twos:2], sizes[2:2 + 2 * twos:2]
    margin = jnp.minimum(giver - 1, limit - taker)
    passed = jax.random.randint(jax.random.fold_in(key, 1), (twos,), 0, 1 << 20) % (margin + 1)
    sizes = sizes.at[1:1 + 2 * twos:2].set(giver - passed).at[2:2 + 2 * twos:2].set(taker + passed)
    return sizes[jax.random.permutation(jax.random.fold_in(key, 2), number_of)]


def bell_draw(rng, dims, scale, bound, cuts=(), held_as=jnp.bfloat16):
    array = jax.random.normal(rng, dims, jnp.float32) * scale
    if len(cuts) > 0:
        array = levels(rng, dims, cuts, -0.22, 0.18) * array
    return jnp.clip(array, min=-bound, max=bound).astype(held_as)


def setup_inputs(seed: int = 0) -> dict:
    splits = jax.random.split(jax.random.key(seed), 13)
    mixer_input = draw_mixer_input(jax.random.fold_in(splits[12], 71), 0)
    gate = bell_draw(splits[1], (PACK_TOKENS, MIXER_HEADS * HEAD_DIM), 1.0, 6.0, ((0, 32), (1, 8)))
    in_b = bell_draw(splits[2], (PACK_TOKENS, GROUPS * STATE), 1.0, 6.0, ((0, 32), (1, 8)))
    in_c = bell_draw(splits[3], (PACK_TOKENS, GROUPS * STATE), STATE ** -0.5, 0.375, ((0, 32), (1, 8)))
    step_size = jnp.clip(jnp.exp(math.log(2.0) - 1.3862944 * jax.random.uniform(splits[4], (MIXER_HEADS, PACK_TOKENS), jnp.float32) ** levels(splits[4], (MIXER_HEADS, PACK_TOKENS), ((0, 8), (1, 32)), -0.2, 0.2)), 0.5, 2.0)
    log_decay = draw_log_decay(jax.random.fold_in(splits[12], 71), 0)
    skip_gain = jnp.clip(1.0 + 3.0 * jax.random.uniform(splits[6], (MIXER_HEADS,), jnp.float32) ** levels(splits[6], (MIXER_HEADS,), ((0, 8),), -0.2, 0.2), 1.0, 4.0)
    norm_gain = jnp.clip(1.0 + 0.1 * jax.random.normal(splits[7], (MIXER_HEADS * HEAD_DIM,), jnp.float32), 0.5, 1.5)
    query_weight = bell_draw(splits[8], (GROUPS, MIXER_HEADS // GROUPS * HEAD_DIM, QHEADS // GROUPS * ATT_DIM), (MIXER_HEADS // GROUPS * HEAD_DIM) ** -0.5, 0.125, ((0, 8),))
    keys = draw_keys(jax.random.fold_in(splits[12], 71), 0)
    values = bell_draw(splits[10], (PACK_TOKENS, GROUPS * ATT_DIM), 1.0, 6.0, ((0, 32), (1, 8)))
    doc_lengths = uneven_parts(splits[11], DOCS, PACK_TOKENS, MOST, 2).astype(jnp.int32)
    return dict(mixer_input=mixer_input, gate=gate, in_b=in_b, in_c=in_c, step_size=step_size, log_decay=log_decay, skip_gain=skip_gain, norm_gain=norm_gain, query_weight=query_weight, keys=keys, values=values, doc_lengths=doc_lengths)


EPSILON = 1e-05

def segment_ids(positions, doc_lengths):
    doc_starts = jnp.cumsum(doc_lengths) - doc_lengths
    hits = (doc_starts[None, :] <= positions[:, None]).astype(jnp.int32)
    return (lax.optimization_barrier(jnp.sum(hits, axis=1)) - 1).astype(jnp.int32)

def reference(mixer_input, gate, in_b, in_c, step_size, log_decay, skip_gain, norm_gain, query_weight, keys, values, doc_lengths):
    head_group = MIXER_HEADS // GROUPS
    block_total = PACK_TOKENS // TOK_DEV
    highest = lax.Precision.HIGHEST
    positions = jnp.arange(PACK_TOKENS, dtype=jnp.int32)
    doc_ids = segment_ids(positions, doc_lengths)
    row_index = jnp.arange(TOK_DEV, dtype=jnp.int32)

    def block_step(incoming, block_number):
        offset = (block_number * TOK_DEV).astype(jnp.int32)
        input_rows = lax.dynamic_slice_in_dim(mixer_input, offset, TOK_DEV, 0).astype(jnp.float32).reshape(TOK_DEV, GROUPS, head_group, HEAD_DIM)
        state_in = lax.dynamic_slice_in_dim(in_b, offset, TOK_DEV, 0).astype(jnp.float32).reshape(TOK_DEV, GROUPS, STATE)
        state_out = lax.dynamic_slice_in_dim(in_c, offset, TOK_DEV, 0).astype(jnp.float32).reshape(TOK_DEV, GROUPS, STATE)
        step_rows = lax.dynamic_slice_in_dim(step_size, offset, TOK_DEV, 1).reshape(GROUPS, head_group, TOK_DEV)
        decay_rows = lax.dynamic_slice_in_dim(log_decay, offset, TOK_DEV, 1).reshape(GROUPS, head_group, TOK_DEV)
        block_docs = lax.dynamic_slice_in_dim(doc_ids, offset, TOK_DEV, 0)
        prev_doc = segment_ids(jnp.reshape(offset - 1, (1,)).astype(jnp.int32), doc_lengths)[0]
        cum_decay = jnp.cumsum(decay_rows, axis=2)
        same_doc = (block_docs[:, None] == block_docs[None, :]) & (row_index[:, None] >= row_index[None, :])
        log_gap = cum_decay[:, :, :, None] - cum_decay[:, :, None, :]
        decay_matrix = jnp.exp(jnp.where(same_doc[None, None], log_gap, -jnp.inf))
        pair_products = jnp.einsum('tgn,sgn->gts', state_out, state_in, precision=highest)
        mixing = pair_products[:, None] * decay_matrix * step_rows[:, :, None, :]
        local_out = jnp.einsum('gjts,sgjp->tgjp', mixing, input_rows, precision=highest)
        last_doc = (block_docs == block_docs[-1]).astype(jnp.float32)
        end_weight = jnp.exp(cum_decay[:, :, -1:] - cum_decay) * last_doc[None, None, :] * step_rows
        weighted = input_rows * jnp.transpose(end_weight, (2, 0, 1))[..., None]
        local_state = jnp.einsum('sgn,sgjp->gjnp', state_in, weighted, precision=highest)
        carry_mask = (block_docs == prev_doc).astype(jnp.float32)
        carry_weight = jnp.exp(cum_decay) * carry_mask[None, None, :]
        carried_out = jnp.einsum('tgn,gjnp->tgjp', state_out, incoming, precision=highest) * jnp.transpose(carry_weight, (2, 0, 1))[..., None]
        skip_rows = skip_gain.reshape(GROUPS, head_group)[None, :, :, None] * input_rows
        mixer_rows = local_out + carried_out + skip_rows
        block_decay = jnp.exp(cum_decay[:, :, -1]) * carry_mask[-1]
        next_state = block_decay[:, :, None, None] * incoming + local_state
        return (next_state, mixer_rows.reshape(TOK_DEV, MIXER_HEADS * HEAD_DIM))
    zero_state = jnp.zeros((GROUPS, head_group, STATE, HEAD_DIM), jnp.float32)
    _, outputs = lax.scan(block_step, zero_state, jnp.arange(block_total, dtype=jnp.int32))
    mixer_full = outputs.reshape(PACK_TOKENS, MIXER_HEADS * HEAD_DIM)
    gated = mixer_full * jax.nn.silu(gate.astype(jnp.float32))
    square_sum = lax.optimization_barrier(jnp.sum(gated * gated, axis=1))
    mixer_out = (gated * lax.rsqrt(square_sum / (MIXER_HEADS * HEAD_DIM) + EPSILON)[:, None] * norm_gain[None, :]).astype(jnp.bfloat16)
    query = jnp.einsum('tgf,gfo->tgo', mixer_out.reshape(PACK_TOKENS, GROUPS, -1).astype(jnp.float32), query_weight.astype(jnp.float32))
    query = query.astype(jnp.bfloat16).reshape(PACK_TOKENS, GROUPS, QHEADS // GROUPS, ATT_DIM)
    key_heads = keys.reshape(PACK_TOKENS, GROUPS, ATT_DIM).astype(jnp.float32)
    value_heads = values.reshape(PACK_TOKENS, GROUPS, ATT_DIM).astype(jnp.float32)

    def one_item(item_number):
        block_number = item_number // GROUPS
        group_number = item_number % GROUPS
        offset = (block_number * TOK_DEV).astype(jnp.int32)
        query_rows = lax.dynamic_slice_in_dim(query, offset, TOK_DEV, 0)
        query_rows = lax.dynamic_index_in_dim(query_rows, group_number, 1, keepdims=False).astype(jnp.float32)
        key_rows = lax.dynamic_index_in_dim(key_heads, group_number, 1, keepdims=False)
        value_rows = lax.dynamic_index_in_dim(value_heads, group_number, 1, keepdims=False)
        query_docs = lax.dynamic_slice_in_dim(doc_ids, offset, TOK_DEV, 0)
        query_pos = lax.dynamic_slice_in_dim(positions, offset, TOK_DEV, 0)
        visible = (query_docs[:, None] == doc_ids[None, :]) & (positions[None, :] <= query_pos[:, None])
        scores = jnp.einsum('tqa,sa->qts', query_rows, key_rows) * ATT_DIM ** (-0.5)
        scores = jnp.where(visible[None], scores, -jnp.inf)
        best_score = lax.optimization_barrier(jnp.max(scores, axis=-1, keepdims=True))
        raw_weight = jnp.exp(scores - best_score)
        score_total = lax.optimization_barrier(jnp.sum(raw_weight, axis=-1))
        rounded = lax.optimization_barrier(raw_weight.astype(jnp.bfloat16)).astype(jnp.float32)
        summed = jnp.einsum('qts,sa->tqa', rounded, value_rows)
        return (summed / jnp.transpose(score_total)[:, :, None]).astype(jnp.bfloat16)
    results = lax.map(one_item, jnp.arange(GROUPS * block_total, dtype=jnp.int32))
    results = results.reshape(block_total, GROUPS, TOK_DEV, QHEADS // GROUPS, ATT_DIM)
    attn_out = jnp.transpose(results, (0, 2, 1, 3, 4)).reshape(PACK_TOKENS, QHEADS * ATT_DIM)
    return (mixer_out, attn_out)
```

```python
import jax
import jax.numpy as jnp
from jax import lax
from jax.sharding import PartitionSpec as P

MIXER_HEADS = 256
HEAD_DIM = 64
STATE = 256
GROUPS = 8
QHEADS = 64
ATT_DIM = 128


EPSILON = 1e-05
NEG_FILL = -1e30
BLOCK_ROWS = 1024


def segment_ids(positions, doc_lengths):
    doc_starts = jnp.cumsum(doc_lengths) - doc_lengths
    hits = (doc_starts[None, :] <= positions[:, None]).astype(jnp.int32)
    return jnp.sum(hits, axis=1) - 1


def shards(
    mixer_input,
    gate,
    in_b,
    in_c,
    step_size,
    log_decay,
    skip_gain,
    norm_gain,
    query_weight,
    keys,
    values,
    doc_lengths,
):
    highest = lax.Precision.HIGHEST
    tok_rows = mixer_input.shape[0]
    groups_dev = query_weight.shape[0]
    heads_dev = step_size.shape[0]
    head_group = heads_dev // groups_dev
    query_group = QHEADS // GROUPS
    shard_index = lax.axis_index("ctx")
    first_pos = shard_index * tok_rows
    row_index = jnp.arange(tok_rows, dtype=jnp.int32)
    own_pos = first_pos + row_index
    own_docs = segment_ids(own_pos, doc_lengths)
    prev_doc = segment_ids(jnp.reshape(first_pos - 1, (1,)), doc_lengths)[0]
    input_f32 = mixer_input.reshape(tok_rows, groups_dev, head_group, HEAD_DIM).astype(jnp.float32)
    state_in = in_b.reshape(tok_rows, groups_dev, STATE)
    state_out = in_c.reshape(tok_rows, groups_dev, STATE)
    upper_ones = (row_index[:, None] <= row_index[None, :]).astype(jnp.float32)
    cum_decay = jnp.dot(log_decay, upper_ones, precision=highest).reshape(
        groups_dev, head_group, tok_rows
    )
    step_rows = step_size.reshape(groups_dev, head_group, tok_rows)
    last_doc = (own_docs == own_docs[-1]).astype(jnp.float32)
    end_weight = jnp.exp(cum_decay[:, :, -1:] - cum_decay) * last_doc[None, None, :] * step_rows
    weighted = input_f32 * jnp.transpose(end_weight, (2, 0, 1))[..., None]
    local_state = jnp.einsum(
        "sgn,sgjp->gjnp", state_in.astype(jnp.float32), weighted, precision=highest
    )
    carry_mask = (own_docs == prev_doc).astype(jnp.float32)
    ctx_count = lax.axis_size("ctx")
    owned = heads_dev // ctx_count
    block_log = jnp.where(carry_mask[-1] > 0, cum_decay[:, :, -1], -jnp.inf).reshape(heads_dev)
    all_log = lax.all_gather(block_log, "ctx")
    mine_log = lax.dynamic_slice_in_dim(all_log, shard_index * owned, owned, 1)
    block_row = jnp.arange(ctx_count, dtype=jnp.int32)
    between = (block_row[None, :, None] < block_row[None, None, :]) & (
        block_row[None, None, :] < block_row[:, None, None]
    )
    log_span = jnp.sum(
        jnp.where(between[None], jnp.transpose(mine_log)[:, None, None, :], 0.0), axis=-1
    )
    earlier = block_row[:, None] > block_row[None, :]
    transfer = jnp.where(earlier[None], jnp.exp(log_span), 0.0)
    states_mine = lax.all_to_all(
        local_state.reshape(heads_dev, STATE * HEAD_DIM), "ctx", 0, 0, tiled=True
    ).reshape(ctx_count, owned, STATE * HEAD_DIM)
    incoming_mine = jnp.einsum("kcd,dkf->ckf", transfer, states_mine, precision=highest)
    incoming = lax.all_to_all(incoming_mine, "ctx", 0, 0, tiled=True).reshape(
        groups_dev, head_group, STATE, HEAD_DIM
    )
    same_doc = (own_docs[:, None] == own_docs[None, :]) & (row_index[:, None] >= row_index[None, :])
    log_gap = cum_decay[:, :, :, None] - cum_decay[:, :, None, :]
    decay_matrix = jnp.exp(jnp.where(same_doc[None, None], log_gap, -jnp.inf))
    pair_products = jnp.einsum(
        "tgn,sgn->gts", state_out, state_in, preferred_element_type=jnp.float32
    )
    mixing = pair_products[:, None] * decay_matrix * step_rows[:, :, None, :]
    local_out = jnp.einsum("gjts,sgjp->tgjp", mixing, input_f32, precision=highest)
    carry_weight = jnp.exp(cum_decay) * carry_mask[None, None, :]
    carried_out = (
        jnp.einsum("tgn,gjnp->tgjp", state_out.astype(jnp.float32), incoming, precision=highest)
        * jnp.transpose(carry_weight, (2, 0, 1))[..., None]
    )
    skip_rows = skip_gain.reshape(groups_dev, head_group)[None, :, :, None] * input_f32
    mixer_full = (local_out + carried_out + skip_rows).reshape(tok_rows, -1)
    gated = mixer_full * jax.nn.silu(gate.astype(jnp.float32))
    square_local = jnp.sum(gated * gated, axis=1)
    square_sum = lax.psum(square_local, "head")
    mixer_out = (
        gated
        * lax.rsqrt(square_sum / (MIXER_HEADS * HEAD_DIM) + EPSILON)[:, None]
        * norm_gain[None, :]
    ).astype(jnp.bfloat16)
    query = jnp.einsum(
        "tgf,gfo->tgo",
        mixer_out.reshape(tok_rows, groups_dev, -1),
        query_weight,
        preferred_element_type=jnp.float32,
    )
    query = query.astype(jnp.bfloat16).reshape(tok_rows, groups_dev, query_group, ATT_DIM)

    def make_visit(query_rows, query_pos):
        query_docs = segment_ids(query_pos, doc_lengths)

        def attend_block(carried, key_rows, value_rows, offset):
            key_count = key_rows.shape[0]
            key_pos = offset + jnp.arange(key_count, dtype=jnp.int32)
            key_docs = segment_ids(key_pos, doc_lengths)
            visible = (query_docs[:, None] == key_docs[None, :]) & (
                key_pos[None, :] <= query_pos[:, None]
            )
            key_heads = key_rows.reshape(key_count, groups_dev, ATT_DIM)
            value_heads = value_rows.reshape(key_count, groups_dev, ATT_DIM)
            scores = jnp.einsum(
                "tgqa,rga->gqtr", query_rows, key_heads, preferred_element_type=jnp.float32
            ) * ATT_DIM ** (-0.5)
            scores = jnp.where(visible[None, None], scores, NEG_FILL)
            best_old, total_old, accum_old = carried
            best_new = jnp.maximum(best_old, jnp.max(scores, axis=-1))
            weights = jnp.where(visible[None, None], jnp.exp(scores - best_new[..., None]), 0.0)
            rescale = jnp.exp(best_old - best_new)
            total_new = total_old * rescale + jnp.sum(weights, axis=-1)
            accum_new = accum_old * rescale[..., None] + jnp.einsum(
                "gqtr,rga->gqta",
                weights.astype(jnp.bfloat16),
                value_heads,
                preferred_element_type=jnp.float32,
            )
            return (best_new, total_new, accum_new)

        def attend_piece(carried, key_rows, value_rows):
            key_count = key_rows.shape[0]
            block_count = key_count // BLOCK_ROWS
            key_blocks = key_rows.reshape(block_count, BLOCK_ROWS, -1)
            value_blocks = value_rows.reshape(block_count, BLOCK_ROWS, -1)

            def block_turn(inner, scan_item):
                key_part, value_part, block_index = scan_item
                return (attend_block(inner, key_part, value_part, block_index * BLOCK_ROWS), None)

            carried, _ = lax.scan(
                block_turn,
                carried,
                (key_blocks, value_blocks, jnp.arange(block_count, dtype=jnp.int32)),
            )
            return carried

        def visit(carried, key_rows, value_rows, offset):
            return attend_piece(carried, key_rows, value_rows)

        return visit

    initial = (
        jnp.full((groups_dev, query_group, tok_rows), NEG_FILL, jnp.float32),
        jnp.zeros((groups_dev, query_group, tok_rows), jnp.float32),
        jnp.zeros((groups_dev, query_group, tok_rows, ATT_DIM), jnp.float32),
    )
    visit_chosen = make_visit(query, own_pos)
    final_carry = visit_chosen(
        initial,
        lax.all_gather(keys, "ctx", axis=0, tiled=True),
        lax.all_gather(values, "ctx", axis=0, tiled=True),
        jnp.int32(0),
    )
    _, score_total, accum = final_carry
    attended = accum / score_total[..., None]
    attn_out = jnp.transpose(attended, (2, 0, 1, 3)).reshape(tok_rows, -1).astype(jnp.bfloat16)
    return (mixer_out, attn_out)


def solution(mesh):
    return jax.shard_map(
        shards,
        mesh=mesh,
        in_specs=(
            P("ctx", "head"),
            P("ctx", "head"),
            P("ctx", "head"),
            P("ctx", "head"),
            P("head", "ctx"),
            P("head", "ctx"),
            P("head"),
            P("head"),
            P("head", None, None),
            P("ctx", "head"),
            P("ctx", "head"),
            P(),
        ),
        out_specs=(P("ctx", "head"), P("ctx", "head")),
        check_vma=False,
    )
```

```python
import jax
import jax.numpy as jnp
from jax import lax
from jax.sharding import PartitionSpec as P

MIXER_HEADS = 256
HEAD_DIM = 64
STATE = 256
GROUPS = 8
QHEADS = 64
ATT_DIM = 128


EPSILON = 1e-05
NEG_FILL = -1e30
BLOCK_ROWS = 1024


def segment_ids(positions, doc_lengths):
    doc_starts = jnp.cumsum(doc_lengths) - doc_lengths
    hits = (doc_starts[None, :] <= positions[:, None]).astype(jnp.int32)
    return jnp.sum(hits, axis=1) - 1


def shards(
    mixer_input,
    gate,
    in_b,
    in_c,
    step_size,
    log_decay,
    skip_gain,
    norm_gain,
    query_weight,
    keys,
    values,
    doc_lengths,
):
    highest = lax.Precision.HIGHEST
    tok_rows = mixer_input.shape[0]
    groups_dev = query_weight.shape[0]
    heads_dev = step_size.shape[0]
    head_group = heads_dev // groups_dev
    query_group = QHEADS // GROUPS
    shard_index = lax.axis_index("ctx")
    first_pos = shard_index * tok_rows
    row_index = jnp.arange(tok_rows, dtype=jnp.int32)
    own_pos = first_pos + row_index
    own_docs = segment_ids(own_pos, doc_lengths)
    prev_doc = segment_ids(jnp.reshape(first_pos - 1, (1,)), doc_lengths)[0]
    input_f32 = mixer_input.reshape(tok_rows, groups_dev, head_group, HEAD_DIM).astype(jnp.float32)
    state_in = in_b.reshape(tok_rows, groups_dev, STATE)
    state_out = in_c.reshape(tok_rows, groups_dev, STATE)
    upper_ones = (row_index[:, None] <= row_index[None, :]).astype(jnp.float32)
    cum_decay = jnp.dot(log_decay, upper_ones, precision=highest).reshape(
        groups_dev, head_group, tok_rows
    )
    step_rows = step_size.reshape(groups_dev, head_group, tok_rows)
    last_doc = (own_docs == own_docs[-1]).astype(jnp.float32)
    end_weight = jnp.exp(cum_decay[:, :, -1:] - cum_decay) * last_doc[None, None, :] * step_rows
    weighted = input_f32 * jnp.transpose(end_weight, (2, 0, 1))[..., None]
    local_state = jnp.einsum(
        "sgn,sgjp->gjnp", state_in.astype(jnp.float32), weighted, precision=highest
    )
    carry_mask = (own_docs == prev_doc).astype(jnp.float32)
    ctx_count = lax.axis_size("ctx")
    owned = heads_dev // ctx_count
    block_log = jnp.where(carry_mask[-1] > 0, cum_decay[:, :, -1], -jnp.inf).reshape(heads_dev)
    lane_rows = 8
    state_cols = STATE * HEAD_DIM // lane_rows
    log_cols = jnp.broadcast_to(block_log[:, None, None], (heads_dev, lane_rows, 128))
    payload = jnp.concatenate(
        [local_state.reshape(heads_dev, lane_rows, state_cols), log_cols], axis=2
    )
    gathered = lax.all_to_all(payload, "ctx", 0, 0, tiled=True).reshape(
        ctx_count, owned, lane_rows, state_cols + 128
    )
    states_mine = gathered[:, :, :, :state_cols]
    mine_log = gathered[:, :, 0, state_cols]
    block_row = jnp.arange(ctx_count, dtype=jnp.int32)
    between = (block_row[None, :, None] < block_row[None, None, :]) & (
        block_row[None, None, :] < block_row[:, None, None]
    )
    log_span = jnp.sum(
        jnp.where(between[None], jnp.transpose(mine_log)[:, None, None, :], 0.0), axis=-1
    )
    earlier = block_row[:, None] > block_row[None, :]
    transfer = jnp.where(earlier[None], jnp.exp(log_span), 0.0)
    incoming_mine = jnp.einsum("kcd,dkrf->ckrf", transfer, states_mine, precision=highest)
    incoming = lax.all_to_all(
        incoming_mine.reshape(ctx_count * owned, lane_rows, state_cols), "ctx", 0, 0, tiled=True
    ).reshape(groups_dev, head_group, STATE, HEAD_DIM)
    same_doc = (own_docs[:, None] == own_docs[None, :]) & (row_index[:, None] >= row_index[None, :])
    log_gap = cum_decay[:, :, :, None] - cum_decay[:, :, None, :]
    decay_matrix = jnp.exp(jnp.where(same_doc[None, None], log_gap, -jnp.inf))
    pair_products = jnp.einsum(
        "tgn,sgn->gts", state_out, state_in, preferred_element_type=jnp.float32
    )
    mixing = pair_products[:, None] * decay_matrix * step_rows[:, :, None, :]
    local_out = jnp.einsum("gjts,sgjp->tgjp", mixing, input_f32, precision=highest)
    carry_weight = jnp.exp(cum_decay) * carry_mask[None, None, :]
    carried_out = (
        jnp.einsum("tgn,gjnp->tgjp", state_out.astype(jnp.float32), incoming, precision=highest)
        * jnp.transpose(carry_weight, (2, 0, 1))[..., None]
    )
    skip_rows = skip_gain.reshape(groups_dev, head_group)[None, :, :, None] * input_f32
    mixer_full = (local_out + carried_out + skip_rows).reshape(tok_rows, -1)
    gated = mixer_full * jax.nn.silu(gate.astype(jnp.float32))
    square_local = jnp.sum(gated * gated, axis=1)
    square_sum = lax.psum(square_local, "head")
    mixer_out = (
        gated
        * lax.rsqrt(square_sum / (MIXER_HEADS * HEAD_DIM) + EPSILON)[:, None]
        * norm_gain[None, :]
    ).astype(jnp.bfloat16)
    query = jnp.einsum(
        "tgf,gfo->tgo",
        mixer_out.reshape(tok_rows, groups_dev, -1),
        query_weight,
        preferred_element_type=jnp.float32,
    )
    query = query.astype(jnp.bfloat16).reshape(tok_rows, groups_dev, query_group, ATT_DIM)

    def make_visit(query_rows, query_pos):
        query_docs = segment_ids(query_pos, doc_lengths)

        def attend_block(carried, key_rows, value_rows, offset):
            key_count = key_rows.shape[0]
            key_pos = offset + jnp.arange(key_count, dtype=jnp.int32)
            key_docs = segment_ids(key_pos, doc_lengths)
            visible = (query_docs[:, None] == key_docs[None, :]) & (
                key_pos[None, :] <= query_pos[:, None]
            )
            key_heads = key_rows.reshape(key_count, groups_dev, ATT_DIM)
            value_heads = value_rows.reshape(key_count, groups_dev, ATT_DIM)
            scores = jnp.einsum(
                "tgqa,rga->gqtr", query_rows, key_heads, preferred_element_type=jnp.float32
            ) * ATT_DIM ** (-0.5)
            scores = jnp.where(visible[None, None], scores, NEG_FILL)
            best_old, total_old, accum_old = carried
            best_new = jnp.maximum(best_old, jnp.max(scores, axis=-1))
            weights = jnp.where(visible[None, None], jnp.exp(scores - best_new[..., None]), 0.0)
            rescale = jnp.exp(best_old - best_new)
            total_new = total_old * rescale + jnp.sum(weights, axis=-1)
            accum_new = accum_old * rescale[..., None] + jnp.einsum(
                "gqtr,rga->gqta",
                weights.astype(jnp.bfloat16),
                value_heads,
                preferred_element_type=jnp.float32,
            )
            return (best_new, total_new, accum_new)

        def attend_piece(carried, key_rows, value_rows):
            key_count = key_rows.shape[0]
            block_count = key_count // BLOCK_ROWS
            key_blocks = key_rows.reshape(block_count, BLOCK_ROWS, -1)
            value_blocks = value_rows.reshape(block_count, BLOCK_ROWS, -1)

            def block_turn(inner, scan_item):
                key_part, value_part, block_index = scan_item
                return (attend_block(inner, key_part, value_part, block_index * BLOCK_ROWS), None)

            carried, _ = lax.scan(
                block_turn,
                carried,
                (key_blocks, value_blocks, jnp.arange(block_count, dtype=jnp.int32)),
            )
            return carried

        def visit(carried, key_rows, value_rows, offset):
            return attend_piece(carried, key_rows, value_rows)

        return visit

    initial = (
        jnp.full((groups_dev, query_group, tok_rows), NEG_FILL, jnp.float32),
        jnp.zeros((groups_dev, query_group, tok_rows), jnp.float32),
        jnp.zeros((groups_dev, query_group, tok_rows, ATT_DIM), jnp.float32),
    )
    visit_chosen = make_visit(query, own_pos)
    final_carry = visit_chosen(
        initial,
        lax.all_gather(keys, "ctx", axis=0, tiled=True),
        lax.all_gather(values, "ctx", axis=0, tiled=True),
        jnp.int32(0),
    )
    _, score_total, accum = final_carry
    attended = accum / score_total[..., None]
    attn_out = jnp.transpose(attended, (2, 0, 1, 3)).reshape(tok_rows, -1).astype(jnp.bfloat16)
    return (mixer_out, attn_out)


def solution(mesh):
    return jax.shard_map(
        shards,
        mesh=mesh,
        in_specs=(
            P("ctx", "head"),
            P("ctx", "head"),
            P("ctx", "head"),
            P("ctx", "head"),
            P("head", "ctx"),
            P("head", "ctx"),
            P("head"),
            P("head"),
            P("head", None, None),
            P("ctx", "head"),
            P("ctx", "head"),
            P(),
        ),
        out_specs=(P("ctx", "head"), P("ctx", "head")),
        check_vma=False,
    )
```

```python
import jax
import jax.numpy as jnp
from jax import lax
from jax.sharding import PartitionSpec as P

MIXER_HEADS = 256
HEAD_DIM = 64
STATE = 256
GROUPS = 8
QHEADS = 64
ATT_DIM = 128


EPSILON = 1e-05
NEG_FILL = -1e30
KEY_CHUNK = 256


def segment_ids(positions, doc_lengths):
    doc_starts = jnp.cumsum(doc_lengths) - doc_lengths
    hits = (doc_starts[None, :] <= positions[:, None]).astype(jnp.int32)
    return jnp.sum(hits, axis=1) - 1


def shards(
    mixer_input,
    gate,
    in_b,
    in_c,
    step_size,
    log_decay,
    skip_gain,
    norm_gain,
    query_weight,
    keys,
    values,
    doc_lengths,
):
    highest = lax.Precision.HIGHEST
    tok_rows = mixer_input.shape[0]
    groups_dev = query_weight.shape[0]
    heads_dev = step_size.shape[0]
    head_group = heads_dev // groups_dev
    query_group = QHEADS // GROUPS
    shard_index = lax.axis_index("ctx")
    first_pos = shard_index * tok_rows
    row_index = jnp.arange(tok_rows, dtype=jnp.int32)
    own_pos = first_pos + row_index
    own_docs = segment_ids(own_pos, doc_lengths)
    prev_doc = segment_ids(jnp.reshape(first_pos - 1, (1,)), doc_lengths)[0]
    input_f32 = mixer_input.reshape(tok_rows, groups_dev, head_group, HEAD_DIM).astype(jnp.float32)
    state_in = in_b.reshape(tok_rows, groups_dev, STATE)
    state_out = in_c.reshape(tok_rows, groups_dev, STATE)
    upper_ones = (row_index[:, None] <= row_index[None, :]).astype(jnp.float32)
    cum_decay = jnp.dot(log_decay, upper_ones, precision=highest).reshape(
        groups_dev, head_group, tok_rows
    )
    step_rows = step_size.reshape(groups_dev, head_group, tok_rows)
    last_doc = (own_docs == own_docs[-1]).astype(jnp.float32)
    end_weight = jnp.exp(cum_decay[:, :, -1:] - cum_decay) * last_doc[None, None, :] * step_rows
    weighted = input_f32 * jnp.transpose(end_weight, (2, 0, 1))[..., None]
    local_state = jnp.einsum(
        "sgn,sgjp->gjnp", state_in.astype(jnp.float32), weighted, precision=highest
    )
    carry_mask = (own_docs == prev_doc).astype(jnp.float32)
    ctx_count = lax.axis_size("ctx")
    owned = heads_dev // ctx_count
    block_log = jnp.where(carry_mask[-1] > 0, cum_decay[:, :, -1], -jnp.inf).reshape(heads_dev)
    lane_rows = 8
    state_cols = STATE * HEAD_DIM // lane_rows
    log_cols = jnp.broadcast_to(block_log[:, None, None], (heads_dev, lane_rows, 128))
    payload = jnp.concatenate(
        [local_state.reshape(heads_dev, lane_rows, state_cols), log_cols], axis=2
    )
    gathered = lax.all_to_all(payload, "ctx", 0, 0, tiled=True).reshape(
        ctx_count, owned, lane_rows, state_cols + 128
    )
    states_mine = gathered[:, :, :, :state_cols]
    mine_log = gathered[:, :, 0, state_cols]
    block_row = jnp.arange(ctx_count, dtype=jnp.int32)
    between = (block_row[None, :, None] < block_row[None, None, :]) & (
        block_row[None, None, :] < block_row[:, None, None]
    )
    log_span = jnp.sum(
        jnp.where(between[None], jnp.transpose(mine_log)[:, None, None, :], 0.0), axis=-1
    )
    earlier = block_row[:, None] > block_row[None, :]
    transfer = jnp.where(earlier[None], jnp.exp(log_span), 0.0)
    incoming_mine = jnp.einsum("kcd,dkrf->ckrf", transfer, states_mine, precision=highest)
    incoming = lax.all_to_all(
        incoming_mine.reshape(ctx_count * owned, lane_rows, state_cols), "ctx", 0, 0, tiled=True
    ).reshape(groups_dev, head_group, STATE, HEAD_DIM)
    same_doc = (own_docs[:, None] == own_docs[None, :]) & (row_index[:, None] >= row_index[None, :])
    log_gap = cum_decay[:, :, :, None] - cum_decay[:, :, None, :]
    decay_matrix = jnp.exp(jnp.where(same_doc[None, None], log_gap, -jnp.inf))
    pair_products = jnp.einsum(
        "tgn,sgn->gts", state_out, state_in, preferred_element_type=jnp.float32
    )
    mixing = pair_products[:, None] * decay_matrix * step_rows[:, :, None, :]
    local_out = jnp.einsum("gjts,sgjp->tgjp", mixing, input_f32, precision=highest)
    carry_weight = jnp.exp(cum_decay) * carry_mask[None, None, :]
    carried_out = (
        jnp.einsum("tgn,gjnp->tgjp", state_out.astype(jnp.float32), incoming, precision=highest)
        * jnp.transpose(carry_weight, (2, 0, 1))[..., None]
    )
    skip_rows = skip_gain.reshape(groups_dev, head_group)[None, :, :, None] * input_f32
    mixer_full = (local_out + carried_out + skip_rows).reshape(tok_rows, -1)
    gated = mixer_full * jax.nn.silu(gate.astype(jnp.float32))
    square_local = jnp.sum(gated * gated, axis=1)
    square_sum = lax.psum(square_local, "head")
    mixer_out = (
        gated
        * lax.rsqrt(square_sum / (MIXER_HEADS * HEAD_DIM) + EPSILON)[:, None]
        * norm_gain[None, :]
    ).astype(jnp.bfloat16)
    query = jnp.einsum(
        "tgf,gfo->tgo",
        mixer_out.reshape(tok_rows, groups_dev, -1),
        query_weight,
        preferred_element_type=jnp.float32,
    )
    query = query.astype(jnp.bfloat16).reshape(tok_rows, groups_dev, query_group, ATT_DIM)

    def make_visit(query_rows, query_pos):
        query_docs = segment_ids(query_pos, doc_lengths)

        def attend_block(carried, key_rows, value_rows, offset):
            key_count = key_rows.shape[0]
            key_pos = offset + jnp.arange(key_count, dtype=jnp.int32)
            key_docs = segment_ids(key_pos, doc_lengths)
            visible = (query_docs[:, None] == key_docs[None, :]) & (
                key_pos[None, :] <= query_pos[:, None]
            )
            key_heads = key_rows.reshape(key_count, groups_dev, ATT_DIM)
            value_heads = value_rows.reshape(key_count, groups_dev, ATT_DIM)
            scores = jnp.einsum(
                "tgqa,rga->gqtr", query_rows, key_heads, preferred_element_type=jnp.float32
            ) * ATT_DIM ** (-0.5)
            scores = jnp.where(visible[None, None], scores, NEG_FILL)
            best_old, total_old, accum_old = carried
            best_new = jnp.maximum(best_old, jnp.max(scores, axis=-1))
            weights = jnp.where(visible[None, None], jnp.exp(scores - best_new[..., None]), 0.0)
            rescale = jnp.exp(best_old - best_new)
            total_new = total_old * rescale + jnp.sum(weights, axis=-1)
            accum_new = accum_old * rescale[..., None] + jnp.einsum(
                "gqtr,rga->gqta",
                weights.astype(jnp.bfloat16),
                value_heads,
                preferred_element_type=jnp.float32,
            )
            return (best_new, total_new, accum_new)

        def visit(carried, kv_rows, first_chunk, chunk_count):
            def chunk_turn(turn, inner):
                offset = (first_chunk + turn) * KEY_CHUNK
                piece = lax.dynamic_slice_in_dim(kv_rows, offset, KEY_CHUNK, 0)
                key_part = piece[:, :, :ATT_DIM].reshape(KEY_CHUNK, -1)
                value_part = piece[:, :, ATT_DIM:].reshape(KEY_CHUNK, -1)
                return attend_block(inner, key_part, value_part, offset)

            return lax.fori_loop(0, chunk_count, chunk_turn, carried)

        return visit

    initial = (
        jnp.full((groups_dev, query_group, tok_rows), NEG_FILL, jnp.float32),
        jnp.zeros((groups_dev, query_group, tok_rows), jnp.float32),
        jnp.zeros((groups_dev, query_group, tok_rows, ATT_DIM), jnp.float32),
    )
    kv_local = jnp.concatenate(
        [
            keys.reshape(tok_rows, groups_dev, ATT_DIM),
            values.reshape(tok_rows, groups_dev, ATT_DIM),
        ],
        axis=2,
    )
    kv_all = lax.all_gather(kv_local, "ctx", axis=0, tiled=True)
    doc_starts = jnp.cumsum(doc_lengths) - doc_lengths
    earliest = doc_starts[own_docs[0]]
    first_chunk = earliest // KEY_CHUNK
    last_chunk = (first_pos + tok_rows - 1) // KEY_CHUNK
    visit_chosen = make_visit(query, own_pos)
    final_carry = visit_chosen(initial, kv_all, first_chunk, last_chunk - first_chunk + 1)
    _, score_total, accum = final_carry
    attended = accum / score_total[..., None]
    attn_out = jnp.transpose(attended, (2, 0, 1, 3)).reshape(tok_rows, -1).astype(jnp.bfloat16)
    return (mixer_out, attn_out)


def solution(mesh):
    return jax.shard_map(
        shards,
        mesh=mesh,
        in_specs=(
            P("ctx", "head"),
            P("ctx", "head"),
            P("ctx", "head"),
            P("ctx", "head"),
            P("head", "ctx"),
            P("head", "ctx"),
            P("head"),
            P("head"),
            P("head", None, None),
            P("ctx", "head"),
            P("ctx", "head"),
            P(),
        ),
        out_specs=(P("ctx", "head"), P("ctx", "head")),
        check_vma=False,
    )
```

```python
import jax
import jax.numpy as jnp
from jax import lax
from jax.sharding import PartitionSpec as P

MIXER_HEADS = 256
HEAD_DIM = 64
STATE = 256
GROUPS = 8
QHEADS = 64
ATT_DIM = 128


EPSILON = 1e-05
NEG_FILL = -1e30
KEY_CHUNK = 256


def segment_ids(positions, doc_lengths):
    doc_starts = jnp.cumsum(doc_lengths) - doc_lengths
    hits = (doc_starts[None, :] <= positions[:, None]).astype(jnp.int32)
    return jnp.sum(hits, axis=1) - 1


def shards(
    mixer_input,
    gate,
    in_b,
    in_c,
    step_size,
    log_decay,
    skip_gain,
    norm_gain,
    query_weight,
    keys,
    values,
    doc_lengths,
):
    highest = lax.Precision.HIGHEST
    tok_rows = mixer_input.shape[0]
    groups_dev = query_weight.shape[0]
    heads_dev = step_size.shape[0]
    head_group = heads_dev // groups_dev
    query_group = QHEADS // GROUPS
    shard_index = lax.axis_index("ctx")
    first_pos = shard_index * tok_rows
    row_index = jnp.arange(tok_rows, dtype=jnp.int32)
    own_pos = first_pos + row_index
    own_docs = segment_ids(own_pos, doc_lengths)
    prev_doc = segment_ids(jnp.reshape(first_pos - 1, (1,)), doc_lengths)[0]
    input_f32 = mixer_input.reshape(tok_rows, groups_dev, head_group, HEAD_DIM).astype(jnp.float32)
    state_in = in_b.reshape(tok_rows, groups_dev, STATE)
    state_out = in_c.reshape(tok_rows, groups_dev, STATE)
    upper_ones = (row_index[:, None] <= row_index[None, :]).astype(jnp.float32)
    cum_decay = jnp.dot(log_decay, upper_ones, precision=highest).reshape(
        groups_dev, head_group, tok_rows
    )
    step_rows = step_size.reshape(groups_dev, head_group, tok_rows)
    last_doc = (own_docs == own_docs[-1]).astype(jnp.float32)
    end_weight = jnp.exp(cum_decay[:, :, -1:] - cum_decay) * last_doc[None, None, :] * step_rows
    weighted = input_f32 * jnp.transpose(end_weight, (2, 0, 1))[..., None]
    local_state = jnp.einsum(
        "sgjp,sgn->gjpn", weighted, state_in.astype(jnp.float32), precision=highest
    )
    carry_mask = (own_docs == prev_doc).astype(jnp.float32)
    ctx_count = lax.axis_size("ctx")
    owned = heads_dev // ctx_count
    block_log = jnp.where(carry_mask[-1] > 0, cum_decay[:, :, -1], -jnp.inf).reshape(heads_dev)
    log_rows = jnp.broadcast_to(block_log[:, None, None], (heads_dev, 8, STATE))
    payload = jnp.concatenate([local_state.reshape(heads_dev, HEAD_DIM, STATE), log_rows], axis=1)
    gathered = lax.all_to_all(payload, "ctx", 0, 0, tiled=True).reshape(
        ctx_count, owned, HEAD_DIM + 8, STATE
    )
    states_mine = gathered[:, :, :HEAD_DIM, :]
    mine_log = gathered[:, :, HEAD_DIM, 0]
    block_row = jnp.arange(ctx_count, dtype=jnp.int32)
    between = (block_row[None, :, None] < block_row[None, None, :]) & (
        block_row[None, None, :] < block_row[:, None, None]
    )
    log_span = jnp.sum(
        jnp.where(between[None], jnp.transpose(mine_log)[:, None, None, :], 0.0), axis=-1
    )
    earlier = block_row[:, None] > block_row[None, :]
    transfer = jnp.where(earlier[None], jnp.exp(log_span), 0.0)
    incoming_mine = jnp.einsum("kcd,dkpn->ckpn", transfer, states_mine, precision=highest)
    incoming = lax.all_to_all(
        incoming_mine.reshape(ctx_count * owned, HEAD_DIM, STATE), "ctx", 0, 0, tiled=True
    ).reshape(groups_dev, head_group, HEAD_DIM, STATE)
    same_doc = (own_docs[:, None] == own_docs[None, :]) & (row_index[:, None] >= row_index[None, :])
    log_gap = cum_decay[:, :, :, None] - cum_decay[:, :, None, :]
    decay_matrix = jnp.exp(jnp.where(same_doc[None, None], log_gap, -jnp.inf))
    pair_products = jnp.einsum(
        "tgn,sgn->gts", state_out, state_in, preferred_element_type=jnp.float32
    )
    mixing = pair_products[:, None] * decay_matrix * step_rows[:, :, None, :]
    local_out = jnp.einsum("gjts,sgjp->tgjp", mixing, input_f32, precision=highest)
    carry_weight = jnp.exp(cum_decay) * carry_mask[None, None, :]
    carried_out = (
        jnp.einsum("tgn,gjpn->tgjp", state_out.astype(jnp.float32), incoming, precision=highest)
        * jnp.transpose(carry_weight, (2, 0, 1))[..., None]
    )
    skip_rows = skip_gain.reshape(groups_dev, head_group)[None, :, :, None] * input_f32
    mixer_full = (local_out + carried_out + skip_rows).reshape(tok_rows, -1)
    gated = mixer_full * jax.nn.silu(gate.astype(jnp.float32))
    square_local = jnp.sum(gated * gated, axis=1)
    square_sum = lax.psum(square_local, "head")
    mixer_out = (
        gated
        * lax.rsqrt(square_sum / (MIXER_HEADS * HEAD_DIM) + EPSILON)[:, None]
        * norm_gain[None, :]
    ).astype(jnp.bfloat16)
    query = jnp.einsum(
        "tgf,gfo->tgo",
        mixer_out.reshape(tok_rows, groups_dev, -1),
        query_weight,
        preferred_element_type=jnp.float32,
    )
    query = query.astype(jnp.bfloat16).reshape(tok_rows, groups_dev, query_group, ATT_DIM)

    def make_visit(query_rows, query_pos):
        query_docs = segment_ids(query_pos, doc_lengths)

        def attend_block(carried, key_rows, value_rows, offset):
            key_count = key_rows.shape[0]
            key_pos = offset + jnp.arange(key_count, dtype=jnp.int32)
            key_docs = segment_ids(key_pos, doc_lengths)
            visible = (query_docs[:, None] == key_docs[None, :]) & (
                key_pos[None, :] <= query_pos[:, None]
            )
            key_heads = key_rows.reshape(key_count, groups_dev, ATT_DIM)
            value_heads = value_rows.reshape(key_count, groups_dev, ATT_DIM)
            scores = jnp.einsum(
                "tgqa,rga->gqtr", query_rows, key_heads, preferred_element_type=jnp.float32
            ) * ATT_DIM ** (-0.5)
            scores = jnp.where(visible[None, None], scores, NEG_FILL)
            best_old, total_old, accum_old = carried
            best_new = jnp.maximum(best_old, jnp.max(scores, axis=-1))
            weights = jnp.where(visible[None, None], jnp.exp(scores - best_new[..., None]), 0.0)
            rescale = jnp.exp(best_old - best_new)
            total_new = total_old * rescale + jnp.sum(weights, axis=-1)
            accum_new = accum_old * rescale[..., None] + jnp.einsum(
                "gqtr,rga->gqta",
                weights.astype(jnp.bfloat16),
                value_heads,
                preferred_element_type=jnp.float32,
            )
            return (best_new, total_new, accum_new)

        def visit(carried, kv_rows, first_chunk, chunk_count):
            def chunk_turn(turn, inner):
                offset = (first_chunk + turn) * KEY_CHUNK
                piece = lax.dynamic_slice_in_dim(kv_rows, offset, KEY_CHUNK, 0)
                key_part = piece[:, :, :ATT_DIM].reshape(KEY_CHUNK, -1)
                value_part = piece[:, :, ATT_DIM:].reshape(KEY_CHUNK, -1)
                return attend_block(inner, key_part, value_part, offset)

            return lax.fori_loop(0, chunk_count, chunk_turn, carried)

        return visit

    initial = (
        jnp.full((groups_dev, query_group, tok_rows), NEG_FILL, jnp.float32),
        jnp.zeros((groups_dev, query_group, tok_rows), jnp.float32),
        jnp.zeros((groups_dev, query_group, tok_rows, ATT_DIM), jnp.float32),
    )
    kv_local = jnp.concatenate(
        [
            keys.reshape(tok_rows, groups_dev, ATT_DIM),
            values.reshape(tok_rows, groups_dev, ATT_DIM),
        ],
        axis=2,
    )
    kv_all = lax.all_gather(kv_local, "ctx", axis=0, tiled=True)
    doc_starts = jnp.cumsum(doc_lengths) - doc_lengths
    earliest = doc_starts[own_docs[0]]
    first_chunk = earliest // KEY_CHUNK
    last_chunk = (first_pos + tok_rows - 1) // KEY_CHUNK
    visit_chosen = make_visit(query, own_pos)
    final_carry = visit_chosen(initial, kv_all, first_chunk, last_chunk - first_chunk + 1)
    _, score_total, accum = final_carry
    attended = accum / score_total[..., None]
    attn_out = jnp.transpose(attended, (2, 0, 1, 3)).reshape(tok_rows, -1).astype(jnp.bfloat16)
    return (mixer_out, attn_out)


def solution(mesh):
    return jax.shard_map(
        shards,
        mesh=mesh,
        in_specs=(
            P("ctx", "head"),
            P("ctx", "head"),
            P("ctx", "head"),
            P("ctx", "head"),
            P("head", "ctx"),
            P("head", "ctx"),
            P("head"),
            P("head"),
            P("head", None, None),
            P("ctx", "head"),
            P("ctx", "head"),
            P(),
        ),
        out_specs=(P("ctx", "head"), P("ctx", "head")),
        check_vma=False,
    )
```

```python
import jax
import jax.numpy as jnp
from jax import lax
from jax.sharding import PartitionSpec as P

MIXER_HEADS = 256
HEAD_DIM = 64
STATE = 256
GROUPS = 8
QHEADS = 64
ATT_DIM = 128


EPSILON = 1e-05
NEG_FILL = -1e30
KEY_CHUNK = 256


def segment_ids(positions, doc_lengths):
    doc_starts = jnp.cumsum(doc_lengths) - doc_lengths
    hits = (doc_starts[None, :] <= positions[:, None]).astype(jnp.int32)
    return jnp.sum(hits, axis=1) - 1


def shards(
    mixer_input,
    gate,
    in_b,
    in_c,
    step_size,
    log_decay,
    skip_gain,
    norm_gain,
    query_weight,
    keys,
    values,
    doc_lengths,
):
    highest = lax.Precision.HIGHEST
    tok_rows = mixer_input.shape[0]
    groups_dev = query_weight.shape[0]
    heads_dev = step_size.shape[0]
    head_group = heads_dev // groups_dev
    query_group = QHEADS // GROUPS
    shard_index = lax.axis_index("ctx")
    first_pos = shard_index * tok_rows
    row_index = jnp.arange(tok_rows, dtype=jnp.int32)
    own_pos = first_pos + row_index
    own_docs = segment_ids(own_pos, doc_lengths)
    prev_doc = segment_ids(jnp.reshape(first_pos - 1, (1,)), doc_lengths)[0]
    input_f32 = mixer_input.reshape(tok_rows, groups_dev, head_group, HEAD_DIM).astype(jnp.float32)
    state_in = in_b.reshape(tok_rows, groups_dev, STATE)
    state_out = in_c.reshape(tok_rows, groups_dev, STATE)
    upper_ones = (row_index[:, None] <= row_index[None, :]).astype(jnp.float32)
    cum_decay = jnp.dot(log_decay, upper_ones, precision=highest).reshape(
        groups_dev, head_group, tok_rows
    )
    step_rows = step_size.reshape(groups_dev, head_group, tok_rows)
    last_doc = (own_docs == own_docs[-1]).astype(jnp.float32)
    end_weight = jnp.exp(cum_decay[:, :, -1:] - cum_decay) * last_doc[None, None, :] * step_rows
    weighted = input_f32 * jnp.transpose(end_weight, (2, 0, 1))[..., None]
    local_state = jnp.einsum(
        "sgjp,sgn->gjpn", weighted, state_in.astype(jnp.float32), precision=highest
    )
    carry_mask = (own_docs == prev_doc).astype(jnp.float32)
    ctx_count = lax.axis_size("ctx")
    owned = heads_dev // ctx_count
    block_log = jnp.where(carry_mask[-1] > 0, cum_decay[:, :, -1], -jnp.inf).reshape(heads_dev)
    log_rows = jnp.broadcast_to(block_log[:, None, None], (heads_dev, 8, STATE))
    payload = jnp.concatenate([local_state.reshape(heads_dev, HEAD_DIM, STATE), log_rows], axis=1)
    gathered = lax.all_to_all(payload, "ctx", 0, 0, tiled=True).reshape(
        ctx_count, owned, HEAD_DIM + 8, STATE
    )
    states_mine = gathered[:, :, :HEAD_DIM, :]
    mine_log = gathered[:, :, HEAD_DIM, 0]
    block_row = jnp.arange(ctx_count, dtype=jnp.int32)
    between = (block_row[None, :, None] < block_row[None, None, :]) & (
        block_row[None, None, :] < block_row[:, None, None]
    )
    log_span = jnp.sum(
        jnp.where(between[None], jnp.transpose(mine_log)[:, None, None, :], 0.0), axis=-1
    )
    earlier = block_row[:, None] > block_row[None, :]
    transfer = jnp.where(earlier[None], jnp.exp(log_span), 0.0)
    incoming_mine = jnp.einsum("kcd,dkpn->ckpn", transfer, states_mine, precision=highest)
    incoming = lax.all_to_all(
        incoming_mine.reshape(ctx_count * owned, HEAD_DIM, STATE), "ctx", 0, 0, tiled=True
    ).reshape(groups_dev, head_group, HEAD_DIM, STATE)
    same_doc = (own_docs[:, None] == own_docs[None, :]) & (row_index[:, None] >= row_index[None, :])
    log_gap = cum_decay[:, :, :, None] - cum_decay[:, :, None, :]
    decay_matrix = jnp.exp(jnp.where(same_doc[None, None], log_gap, -jnp.inf))
    pair_products = jnp.einsum(
        "tgn,sgn->gts", state_out, state_in, preferred_element_type=jnp.float32
    )
    mixing = pair_products[:, None] * decay_matrix * step_rows[:, :, None, :]
    local_out = jnp.einsum("gjts,sgjp->tgjp", mixing, input_f32, precision=highest)
    carry_weight = jnp.exp(cum_decay) * carry_mask[None, None, :]
    carried_out = (
        jnp.einsum("tgn,gjpn->tgjp", state_out.astype(jnp.float32), incoming, precision=highest)
        * jnp.transpose(carry_weight, (2, 0, 1))[..., None]
    )
    skip_rows = skip_gain.reshape(groups_dev, head_group)[None, :, :, None] * input_f32
    mixer_full = (local_out + carried_out + skip_rows).reshape(tok_rows, -1)
    gated = mixer_full * jax.nn.silu(gate.astype(jnp.float32))
    square_local = jnp.sum(gated * gated, axis=1)
    head_count = lax.axis_size("head")
    square_sum = square_local
    for shift in range(1, head_count):
        square_sum = square_sum + lax.ppermute(
            square_local,
            "head",
            [(source, (source + shift) % head_count) for source in range(head_count)],
        )
    mixer_out = (
        gated
        * lax.rsqrt(square_sum / (MIXER_HEADS * HEAD_DIM) + EPSILON)[:, None]
        * norm_gain[None, :]
    ).astype(jnp.bfloat16)
    query = jnp.einsum(
        "tgf,gfo->tgo",
        mixer_out.reshape(tok_rows, groups_dev, -1),
        query_weight,
        preferred_element_type=jnp.float32,
    )
    query = query.astype(jnp.bfloat16).reshape(tok_rows, groups_dev, query_group, ATT_DIM)

    def make_visit(query_rows, query_pos):
        query_docs = segment_ids(query_pos, doc_lengths)

        def attend_block(carried, key_rows, value_rows, offset):
            key_count = key_rows.shape[0]
            key_pos = offset + jnp.arange(key_count, dtype=jnp.int32)
            key_docs = segment_ids(key_pos, doc_lengths)
            visible = (query_docs[:, None] == key_docs[None, :]) & (
                key_pos[None, :] <= query_pos[:, None]
            )
            key_heads = key_rows.reshape(key_count, groups_dev, ATT_DIM)
            value_heads = value_rows.reshape(key_count, groups_dev, ATT_DIM)
            scores = jnp.einsum(
                "tgqa,rga->gqtr", query_rows, key_heads, preferred_element_type=jnp.float32
            ) * ATT_DIM ** (-0.5)
            scores = jnp.where(visible[None, None], scores, NEG_FILL)
            best_old, total_old, accum_old = carried
            best_new = jnp.maximum(best_old, jnp.max(scores, axis=-1))
            weights = jnp.where(visible[None, None], jnp.exp(scores - best_new[..., None]), 0.0)
            rescale = jnp.exp(best_old - best_new)
            total_new = total_old * rescale + jnp.sum(weights, axis=-1)
            accum_new = accum_old * rescale[..., None] + jnp.einsum(
                "gqtr,rga->gqta",
                weights.astype(jnp.bfloat16),
                value_heads,
                preferred_element_type=jnp.float32,
            )
            return (best_new, total_new, accum_new)

        def visit(carried, kv_rows, first_chunk, chunk_count):
            def chunk_turn(turn, inner):
                offset = (first_chunk + turn) * KEY_CHUNK
                piece = lax.dynamic_slice_in_dim(kv_rows, offset, KEY_CHUNK, 0)
                key_part = piece[:, :, :ATT_DIM].reshape(KEY_CHUNK, -1)
                value_part = piece[:, :, ATT_DIM:].reshape(KEY_CHUNK, -1)
                return attend_block(inner, key_part, value_part, offset)

            return lax.fori_loop(0, chunk_count, chunk_turn, carried)

        return visit

    initial = (
        jnp.full((groups_dev, query_group, tok_rows), NEG_FILL, jnp.float32),
        jnp.zeros((groups_dev, query_group, tok_rows), jnp.float32),
        jnp.zeros((groups_dev, query_group, tok_rows, ATT_DIM), jnp.float32),
    )
    kv_local = jnp.concatenate(
        [
            keys.reshape(tok_rows, groups_dev, ATT_DIM),
            values.reshape(tok_rows, groups_dev, ATT_DIM),
        ],
        axis=2,
    )
    kv_all = lax.all_gather(kv_local, "ctx", axis=0, tiled=True)
    doc_starts = jnp.cumsum(doc_lengths) - doc_lengths
    earliest = doc_starts[own_docs[0]]
    first_chunk = earliest // KEY_CHUNK
    last_chunk = (first_pos + tok_rows - 1) // KEY_CHUNK
    visit_chosen = make_visit(query, own_pos)
    final_carry = visit_chosen(initial, kv_all, first_chunk, last_chunk - first_chunk + 1)
    _, score_total, accum = final_carry
    attended = accum / score_total[..., None]
    attn_out = jnp.transpose(attended, (2, 0, 1, 3)).reshape(tok_rows, -1).astype(jnp.bfloat16)
    return (mixer_out, attn_out)


def solution(mesh):
    return jax.shard_map(
        shards,
        mesh=mesh,
        in_specs=(
            P("ctx", "head"),
            P("ctx", "head"),
            P("ctx", "head"),
            P("ctx", "head"),
            P("head", "ctx"),
            P("head", "ctx"),
            P("head"),
            P("head"),
            P("head", None, None),
            P("ctx", "head"),
            P("ctx", "head"),
            P(),
        ),
        out_specs=(P("ctx", "head"), P("ctx", "head")),
        check_vma=False,
    )
```

```python
import jax
import jax.numpy as jnp
from jax import lax
from jax.sharding import PartitionSpec as P
from jax.experimental import pallas as pl
from jax.experimental.pallas import tpu as pltpu

MIXER_HEADS = 256
HEAD_DIM = 64
STATE = 256
GROUPS = 8
QHEADS = 64
ATT_DIM = 128


EPSILON = 1e-05
NEG_FILL = -1e30
KEY_CHUNK = 256


def segment_ids(positions, doc_lengths):
    doc_starts = jnp.cumsum(doc_lengths) - doc_lengths
    hits = (doc_starts[None, :] <= positions[:, None]).astype(jnp.int32)
    return jnp.sum(hits, axis=1) - 1


def attention_kernel(chunk_ref, query_ref, kv_ref, low_ref, high_ref, out_ref):
    rows = query_ref.shape[0]
    query_rows = query_ref[...]
    low = low_ref[...]
    high = high_ref[...]

    def chunk_turn(turn, carried):
        best_old, total_old, accum_old = carried
        start = pl.multiple_of((chunk_ref[0] + turn) * KEY_CHUNK, KEY_CHUNK)
        piece = kv_ref[pl.ds(start, KEY_CHUNK), :]
        key_part = piece[:, :ATT_DIM]
        value_part = piece[:, ATT_DIM:]
        scores = lax.dot_general(
            query_rows, key_part, (((1,), (1,)), ((), ())), preferred_element_type=jnp.float32
        ) * ATT_DIM ** (-0.5)
        key_pos = start + lax.broadcasted_iota(jnp.int32, (rows, KEY_CHUNK), 1)
        visible = (key_pos >= low) & (key_pos <= high)
        scores = jnp.where(visible, scores, NEG_FILL)
        best_new = jnp.maximum(best_old, jnp.max(scores, axis=1, keepdims=True))
        weights = jnp.where(visible, jnp.exp(scores - best_new), 0.0)
        rescale = jnp.exp(best_old - best_new)
        total_new = total_old * rescale + jnp.sum(weights, axis=1, keepdims=True)
        accum_new = accum_old * rescale + jnp.dot(
            weights.astype(jnp.bfloat16), value_part, preferred_element_type=jnp.float32
        )
        return (best_new, total_new, accum_new)

    initial = (
        jnp.full((rows, 1), NEG_FILL, jnp.float32),
        jnp.zeros((rows, 1), jnp.float32),
        jnp.zeros((rows, ATT_DIM), jnp.float32),
    )
    _, total, accum = lax.fori_loop(0, chunk_ref[1], chunk_turn, initial)
    out_ref[...] = (accum / total).astype(out_ref.dtype)


def flash_attention(query_flat, kv_rows, low, high, first_chunk, chunk_count):
    rows, width = query_flat.shape
    heads = width // ATT_DIM
    chunk_info = jnp.stack([first_chunk, chunk_count]).astype(jnp.int32)
    grid_spec = pltpu.PrefetchScalarGridSpec(
        num_scalar_prefetch=1,
        grid=(heads,),
        in_specs=[
            pl.BlockSpec((rows, ATT_DIM), lambda i, info: (0, i)),
            pl.BlockSpec(kv_rows.shape, lambda i, info: (0, 0)),
            pl.BlockSpec((rows, 1), lambda i, info: (0, 0)),
            pl.BlockSpec((rows, 1), lambda i, info: (0, 0)),
        ],
        out_specs=pl.BlockSpec((rows, ATT_DIM), lambda i, info: (0, i)),
    )
    return pl.pallas_call(
        attention_kernel,
        grid_spec=grid_spec,
        out_shape=jax.ShapeDtypeStruct((rows, width), jnp.bfloat16),
    )(chunk_info, query_flat, kv_rows, low, high)


def shards(
    mixer_input,
    gate,
    in_b,
    in_c,
    step_size,
    log_decay,
    skip_gain,
    norm_gain,
    query_weight,
    keys,
    values,
    doc_lengths,
):
    highest = lax.Precision.HIGHEST
    tok_rows = mixer_input.shape[0]
    groups_dev = query_weight.shape[0]
    heads_dev = step_size.shape[0]
    head_group = heads_dev // groups_dev
    query_group = QHEADS // GROUPS
    shard_index = lax.axis_index("ctx")
    first_pos = shard_index * tok_rows
    row_index = jnp.arange(tok_rows, dtype=jnp.int32)
    own_pos = first_pos + row_index
    own_docs = segment_ids(own_pos, doc_lengths)
    prev_doc = segment_ids(jnp.reshape(first_pos - 1, (1,)), doc_lengths)[0]
    input_f32 = mixer_input.reshape(tok_rows, groups_dev, head_group, HEAD_DIM).astype(jnp.float32)
    state_in = in_b.reshape(tok_rows, groups_dev, STATE)
    state_out = in_c.reshape(tok_rows, groups_dev, STATE)
    upper_ones = (row_index[:, None] <= row_index[None, :]).astype(jnp.float32)
    cum_decay = jnp.dot(log_decay, upper_ones, precision=highest).reshape(
        groups_dev, head_group, tok_rows
    )
    step_rows = step_size.reshape(groups_dev, head_group, tok_rows)
    last_doc = (own_docs == own_docs[-1]).astype(jnp.float32)
    end_weight = jnp.exp(cum_decay[:, :, -1:] - cum_decay) * last_doc[None, None, :] * step_rows
    weighted = input_f32 * jnp.transpose(end_weight, (2, 0, 1))[..., None]
    local_state = jnp.einsum(
        "sgjp,sgn->gjpn", weighted, state_in.astype(jnp.float32), precision=highest
    )
    carry_mask = (own_docs == prev_doc).astype(jnp.float32)
    ctx_count = lax.axis_size("ctx")
    owned = heads_dev // ctx_count
    block_log = jnp.where(carry_mask[-1] > 0, cum_decay[:, :, -1], -jnp.inf).reshape(heads_dev)
    log_rows = jnp.broadcast_to(block_log[:, None, None], (heads_dev, 8, STATE))
    payload = jnp.concatenate([local_state.reshape(heads_dev, HEAD_DIM, STATE), log_rows], axis=1)
    gathered = lax.all_to_all(payload, "ctx", 0, 0, tiled=True).reshape(
        ctx_count, owned, HEAD_DIM + 8, STATE
    )
    states_mine = gathered[:, :, :HEAD_DIM, :]
    mine_log = gathered[:, :, HEAD_DIM, 0]
    block_row = jnp.arange(ctx_count, dtype=jnp.int32)
    between = (block_row[None, :, None] < block_row[None, None, :]) & (
        block_row[None, None, :] < block_row[:, None, None]
    )
    log_span = jnp.sum(
        jnp.where(between[None], jnp.transpose(mine_log)[:, None, None, :], 0.0), axis=-1
    )
    earlier = block_row[:, None] > block_row[None, :]
    transfer = jnp.where(earlier[None], jnp.exp(log_span), 0.0)
    incoming_mine = jnp.einsum("kcd,dkpn->ckpn", transfer, states_mine, precision=highest)
    incoming = lax.all_to_all(
        incoming_mine.reshape(ctx_count * owned, HEAD_DIM, STATE), "ctx", 0, 0, tiled=True
    ).reshape(groups_dev, head_group, HEAD_DIM, STATE)
    same_doc = (own_docs[:, None] == own_docs[None, :]) & (row_index[:, None] >= row_index[None, :])
    log_gap = cum_decay[:, :, :, None] - cum_decay[:, :, None, :]
    decay_matrix = jnp.exp(jnp.where(same_doc[None, None], log_gap, -jnp.inf))
    pair_products = jnp.einsum(
        "tgn,sgn->gts", state_out, state_in, preferred_element_type=jnp.float32
    )
    mixing = pair_products[:, None] * decay_matrix * step_rows[:, :, None, :]
    local_out = jnp.einsum("gjts,sgjp->tgjp", mixing, input_f32, precision=highest)
    carry_weight = jnp.exp(cum_decay) * carry_mask[None, None, :]
    carried_out = (
        jnp.einsum("tgn,gjpn->tgjp", state_out.astype(jnp.float32), incoming, precision=highest)
        * jnp.transpose(carry_weight, (2, 0, 1))[..., None]
    )
    skip_rows = skip_gain.reshape(groups_dev, head_group)[None, :, :, None] * input_f32
    mixer_full = (local_out + carried_out + skip_rows).reshape(tok_rows, -1)
    gated = mixer_full * jax.nn.silu(gate.astype(jnp.float32))
    square_local = jnp.sum(gated * gated, axis=1)
    square_sum = lax.psum(square_local, "head")
    mixer_out = (
        gated
        * lax.rsqrt(square_sum / (MIXER_HEADS * HEAD_DIM) + EPSILON)[:, None]
        * norm_gain[None, :]
    ).astype(jnp.bfloat16)
    query = jnp.einsum(
        "tgf,gfo->tgo",
        mixer_out.reshape(tok_rows, groups_dev, -1),
        query_weight,
        preferred_element_type=jnp.float32,
    )
    query = query.astype(jnp.bfloat16).reshape(tok_rows, groups_dev, query_group, ATT_DIM)

    kv_local = jnp.concatenate(
        [
            keys.reshape(tok_rows, groups_dev, ATT_DIM),
            values.reshape(tok_rows, groups_dev, ATT_DIM),
        ],
        axis=2,
    )
    kv_all = lax.all_gather(kv_local, "ctx", axis=0, tiled=True)
    doc_starts = jnp.cumsum(doc_lengths) - doc_lengths
    row_low = doc_starts[own_docs]
    first_chunk = row_low[0] // KEY_CHUNK
    last_chunk = (first_pos + tok_rows - 1) // KEY_CHUNK
    group_outs = []
    for group in range(groups_dev):
        group_outs.append(
            flash_attention(
                query[:, group].reshape(tok_rows, query_group * ATT_DIM),
                kv_all[:, group],
                row_low[:, None],
                own_pos[:, None],
                first_chunk,
                last_chunk - first_chunk + 1,
            )
        )
    attn_out = jnp.concatenate(group_outs, axis=1)
    return (mixer_out, attn_out)


def solution(mesh):
    return jax.shard_map(
        shards,
        mesh=mesh,
        in_specs=(
            P("ctx", "head"),
            P("ctx", "head"),
            P("ctx", "head"),
            P("ctx", "head"),
            P("head", "ctx"),
            P("head", "ctx"),
            P("head"),
            P("head"),
            P("head", None, None),
            P("ctx", "head"),
            P("ctx", "head"),
            P(),
        ),
        out_specs=(P("ctx", "head"), P("ctx", "head")),
        check_vma=False,
    )
```

```python
import jax
import jax.numpy as jnp
from jax import lax
from jax.sharding import PartitionSpec as P
from jax.experimental import pallas as pl
from jax.experimental.pallas import tpu as pltpu

MIXER_HEADS = 256
HEAD_DIM = 64
STATE = 256
GROUPS = 8
QHEADS = 64
ATT_DIM = 128


EPSILON = 1e-05
NEG_FILL = -1e30
KEY_CHUNK = 256


def segment_ids(positions, doc_lengths):
    doc_starts = jnp.cumsum(doc_lengths) - doc_lengths
    hits = (doc_starts[None, :] <= positions[:, None]).astype(jnp.int32)
    return jnp.sum(hits, axis=1) - 1


def attention_kernel(chunk_ref, query_ref, kv_ref, low_ref, high_ref, out_ref):
    rows = query_ref.shape[0]
    query_rows = query_ref[...]
    low = low_ref[...]
    high = high_ref[...]

    def chunk_turn(turn, carried):
        best_old, total_old, accum_old = carried
        start = pl.multiple_of((chunk_ref[0] + turn) * KEY_CHUNK, KEY_CHUNK)
        piece = kv_ref[pl.ds(start, KEY_CHUNK), :]
        key_part = piece[:, :ATT_DIM]
        value_part = piece[:, ATT_DIM:]
        scores = lax.dot_general(
            query_rows, key_part, (((1,), (1,)), ((), ())), preferred_element_type=jnp.float32
        ) * ATT_DIM ** (-0.5)
        key_pos = start + lax.broadcasted_iota(jnp.int32, (rows, KEY_CHUNK), 1)
        visible = (key_pos >= low) & (key_pos <= high)
        scores = jnp.where(visible, scores, NEG_FILL)
        best_new = jnp.maximum(best_old, jnp.max(scores, axis=1, keepdims=True))
        weights = jnp.where(visible, jnp.exp(scores - best_new), 0.0)
        rescale = jnp.exp(best_old - best_new)
        total_new = total_old * rescale + jnp.sum(weights, axis=1, keepdims=True)
        accum_new = accum_old * rescale + jnp.dot(
            weights.astype(jnp.bfloat16), value_part, preferred_element_type=jnp.float32
        )
        return (best_new, total_new, accum_new)

    initial = (
        jnp.full((rows, 1), NEG_FILL, jnp.float32),
        jnp.zeros((rows, 1), jnp.float32),
        jnp.zeros((rows, ATT_DIM), jnp.float32),
    )
    _, total, accum = lax.fori_loop(0, chunk_ref[1], chunk_turn, initial)
    out_ref[...] = (accum / total).astype(out_ref.dtype)


def flash_attention(query_flat, kv_rows, low, high, first_chunk, chunk_count):
    rows = query_flat.shape[0]
    chunk_info = jnp.stack([first_chunk, chunk_count]).astype(jnp.int32)
    grid_spec = pltpu.PrefetchScalarGridSpec(
        num_scalar_prefetch=1,
        grid=(1,),
        in_specs=[
            pl.BlockSpec(query_flat.shape, lambda i, info: (0, 0)),
            pl.BlockSpec(kv_rows.shape, lambda i, info: (0, 0)),
            pl.BlockSpec((rows, 1), lambda i, info: (0, 0)),
            pl.BlockSpec((rows, 1), lambda i, info: (0, 0)),
        ],
        out_specs=pl.BlockSpec(query_flat.shape, lambda i, info: (0, 0)),
    )
    return pl.pallas_call(
        attention_kernel,
        grid_spec=grid_spec,
        out_shape=jax.ShapeDtypeStruct(query_flat.shape, jnp.bfloat16),
    )(chunk_info, query_flat, kv_rows, low, high)


def shards(
    mixer_input,
    gate,
    in_b,
    in_c,
    step_size,
    log_decay,
    skip_gain,
    norm_gain,
    query_weight,
    keys,
    values,
    doc_lengths,
):
    highest = lax.Precision.HIGHEST
    tok_rows = mixer_input.shape[0]
    groups_dev = query_weight.shape[0]
    heads_dev = step_size.shape[0]
    head_group = heads_dev // groups_dev
    query_group = QHEADS // GROUPS
    shard_index = lax.axis_index("ctx")
    first_pos = shard_index * tok_rows
    row_index = jnp.arange(tok_rows, dtype=jnp.int32)
    own_pos = first_pos + row_index
    own_docs = segment_ids(own_pos, doc_lengths)
    prev_doc = segment_ids(jnp.reshape(first_pos - 1, (1,)), doc_lengths)[0]
    input_f32 = mixer_input.reshape(tok_rows, groups_dev, head_group, HEAD_DIM).astype(jnp.float32)
    state_in = in_b.reshape(tok_rows, groups_dev, STATE)
    state_out = in_c.reshape(tok_rows, groups_dev, STATE)
    upper_ones = (row_index[:, None] <= row_index[None, :]).astype(jnp.float32)
    cum_decay = jnp.dot(log_decay, upper_ones, precision=highest).reshape(
        groups_dev, head_group, tok_rows
    )
    step_rows = step_size.reshape(groups_dev, head_group, tok_rows)
    last_doc = (own_docs == own_docs[-1]).astype(jnp.float32)
    end_weight = jnp.exp(cum_decay[:, :, -1:] - cum_decay) * last_doc[None, None, :] * step_rows
    weighted = input_f32 * jnp.transpose(end_weight, (2, 0, 1))[..., None]
    local_state = jnp.einsum(
        "sgjp,sgn->gjpn", weighted, state_in.astype(jnp.float32), precision=highest
    )
    carry_mask = (own_docs == prev_doc).astype(jnp.float32)
    ctx_count = lax.axis_size("ctx")
    owned = heads_dev // ctx_count
    block_log = jnp.where(carry_mask[-1] > 0, cum_decay[:, :, -1], -jnp.inf).reshape(heads_dev)
    log_rows = jnp.broadcast_to(block_log[:, None, None], (heads_dev, 8, STATE))
    payload = jnp.concatenate([local_state.reshape(heads_dev, HEAD_DIM, STATE), log_rows], axis=1)
    gathered = lax.all_to_all(payload, "ctx", 0, 0, tiled=True).reshape(
        ctx_count, owned, HEAD_DIM + 8, STATE
    )
    states_mine = gathered[:, :, :HEAD_DIM, :]
    mine_log = gathered[:, :, HEAD_DIM, 0]
    block_row = jnp.arange(ctx_count, dtype=jnp.int32)
    between = (block_row[None, :, None] < block_row[None, None, :]) & (
        block_row[None, None, :] < block_row[:, None, None]
    )
    log_span = jnp.sum(
        jnp.where(between[None], jnp.transpose(mine_log)[:, None, None, :], 0.0), axis=-1
    )
    earlier = block_row[:, None] > block_row[None, :]
    transfer = jnp.where(earlier[None], jnp.exp(log_span), 0.0)
    incoming_mine = jnp.einsum("kcd,dkpn->ckpn", transfer, states_mine, precision=highest)
    incoming = lax.all_to_all(
        incoming_mine.reshape(ctx_count * owned, HEAD_DIM, STATE), "ctx", 0, 0, tiled=True
    ).reshape(groups_dev, head_group, HEAD_DIM, STATE)
    same_doc = (own_docs[:, None] == own_docs[None, :]) & (row_index[:, None] >= row_index[None, :])
    log_gap = cum_decay[:, :, :, None] - cum_decay[:, :, None, :]
    decay_matrix = jnp.exp(jnp.where(same_doc[None, None], log_gap, -jnp.inf))
    pair_products = jnp.einsum(
        "tgn,sgn->gts", state_out, state_in, preferred_element_type=jnp.float32
    )
    mixing = pair_products[:, None] * decay_matrix * step_rows[:, :, None, :]
    local_out = jnp.einsum("gjts,sgjp->tgjp", mixing, input_f32, precision=highest)
    carry_weight = jnp.exp(cum_decay) * carry_mask[None, None, :]
    carried_out = (
        jnp.einsum("tgn,gjpn->tgjp", state_out.astype(jnp.float32), incoming, precision=highest)
        * jnp.transpose(carry_weight, (2, 0, 1))[..., None]
    )
    skip_rows = skip_gain.reshape(groups_dev, head_group)[None, :, :, None] * input_f32
    mixer_full = (local_out + carried_out + skip_rows).reshape(tok_rows, -1)
    gated = mixer_full * jax.nn.silu(gate.astype(jnp.float32))
    square_local = jnp.sum(gated * gated, axis=1)
    square_sum = lax.psum(square_local, "head")
    mixer_out = (
        gated
        * lax.rsqrt(square_sum / (MIXER_HEADS * HEAD_DIM) + EPSILON)[:, None]
        * norm_gain[None, :]
    ).astype(jnp.bfloat16)
    query = jnp.einsum(
        "tgf,gfo->tgo",
        mixer_out.reshape(tok_rows, groups_dev, -1),
        query_weight,
        preferred_element_type=jnp.float32,
    )
    query = query.astype(jnp.bfloat16).reshape(tok_rows, groups_dev, query_group, ATT_DIM)

    kv_local = jnp.concatenate(
        [
            keys.reshape(tok_rows, groups_dev, ATT_DIM),
            values.reshape(tok_rows, groups_dev, ATT_DIM),
        ],
        axis=2,
    )
    kv_all = lax.all_gather(kv_local, "ctx", axis=0, tiled=True)
    doc_starts = jnp.cumsum(doc_lengths) - doc_lengths
    row_low = jnp.max(
        jnp.where(doc_starts[None, :] <= own_pos[:, None], doc_starts[None, :], 0), axis=1
    )
    first_chunk = row_low[0] // KEY_CHUNK
    last_chunk = (first_pos + tok_rows - 1) // KEY_CHUNK
    stacked_low = jnp.tile(row_low, query_group)[:, None]
    stacked_high = jnp.tile(own_pos, query_group)[:, None]
    group_outs = []
    for group in range(groups_dev):
        stacked_query = jnp.transpose(query[:, group], (1, 0, 2)).reshape(-1, ATT_DIM)
        stacked_out = flash_attention(
            stacked_query,
            kv_all[:, group],
            stacked_low,
            stacked_high,
            first_chunk,
            last_chunk - first_chunk + 1,
        )
        group_outs.append(
            jnp.transpose(stacked_out.reshape(query_group, tok_rows, ATT_DIM), (1, 0, 2))
        )
    attn_out = jnp.stack(group_outs, axis=1).reshape(tok_rows, -1)
    return (mixer_out, attn_out)


def solution(mesh):
    return jax.shard_map(
        shards,
        mesh=mesh,
        in_specs=(
            P("ctx", "head"),
            P("ctx", "head"),
            P("ctx", "head"),
            P("ctx", "head"),
            P("head", "ctx"),
            P("head", "ctx"),
            P("head"),
            P("head"),
            P("head", None, None),
            P("ctx", "head"),
            P("ctx", "head"),
            P(),
        ),
        out_specs=(P("ctx", "head"), P("ctx", "head")),
        check_vma=False,
    )
```

```python
import jax
import jax.numpy as jnp
from jax import lax
from jax.sharding import PartitionSpec as P
from jax.experimental import pallas as pl
from jax.experimental.pallas import tpu as pltpu

MIXER_HEADS = 256
HEAD_DIM = 64
STATE = 256
GROUPS = 8
QHEADS = 64
ATT_DIM = 128


EPSILON = 1e-05
NEG_FILL = -1e30
KEY_CHUNK = 256
MOST = 2176


def segment_ids(positions, doc_lengths):
    doc_starts = jnp.cumsum(doc_lengths) - doc_lengths
    hits = (doc_starts[None, :] <= positions[:, None]).astype(jnp.int32)
    return jnp.sum(hits, axis=1) - 1


def attention_kernel(chunk_ref, query_ref, kv_ref, low_ref, high_ref, out_ref):
    rows = query_ref.shape[0]
    query_rows = query_ref[...]
    low = low_ref[...]
    high = high_ref[...]

    def chunk_turn(turn, carried):
        best_old, total_old, accum_old = carried
        start = pl.multiple_of((chunk_ref[0] + turn) * KEY_CHUNK, KEY_CHUNK)
        piece = kv_ref[pl.ds(start, KEY_CHUNK), :]
        key_part = piece[:, :ATT_DIM]
        value_part = piece[:, ATT_DIM:]
        scores = lax.dot_general(
            query_rows, key_part, (((1,), (1,)), ((), ())), preferred_element_type=jnp.float32
        ) * ATT_DIM ** (-0.5)
        key_pos = chunk_ref[2] + start + lax.broadcasted_iota(jnp.int32, (rows, KEY_CHUNK), 1)
        visible = (key_pos >= low) & (key_pos <= high)
        scores = jnp.where(visible, scores, NEG_FILL)
        best_new = jnp.maximum(best_old, jnp.max(scores, axis=1, keepdims=True))
        weights = jnp.where(visible, jnp.exp(scores - best_new), 0.0)
        rescale = jnp.exp(best_old - best_new)
        total_new = total_old * rescale + jnp.sum(weights, axis=1, keepdims=True)
        accum_new = accum_old * rescale + jnp.dot(
            weights.astype(jnp.bfloat16), value_part, preferred_element_type=jnp.float32
        )
        return (best_new, total_new, accum_new)

    initial = (
        jnp.full((rows, 1), NEG_FILL, jnp.float32),
        jnp.zeros((rows, 1), jnp.float32),
        jnp.zeros((rows, ATT_DIM), jnp.float32),
    )
    _, total, accum = lax.fori_loop(0, chunk_ref[1], chunk_turn, initial)
    out_ref[...] = (accum / total).astype(out_ref.dtype)


def flash_attention(query_flat, kv_rows, low, high, first_chunk, chunk_count, base):
    rows = query_flat.shape[0]
    chunk_info = jnp.stack([first_chunk, chunk_count, base]).astype(jnp.int32)
    grid_spec = pltpu.PrefetchScalarGridSpec(
        num_scalar_prefetch=1,
        grid=(1,),
        in_specs=[
            pl.BlockSpec(query_flat.shape, lambda i, info: (0, 0)),
            pl.BlockSpec(kv_rows.shape, lambda i, info: (0, 0)),
            pl.BlockSpec((rows, 1), lambda i, info: (0, 0)),
            pl.BlockSpec((rows, 1), lambda i, info: (0, 0)),
        ],
        out_specs=pl.BlockSpec(query_flat.shape, lambda i, info: (0, 0)),
    )
    return pl.pallas_call(
        attention_kernel,
        grid_spec=grid_spec,
        out_shape=jax.ShapeDtypeStruct(query_flat.shape, jnp.bfloat16),
    )(chunk_info, query_flat, kv_rows, low, high)


def shards(
    mixer_input,
    gate,
    in_b,
    in_c,
    step_size,
    log_decay,
    skip_gain,
    norm_gain,
    query_weight,
    keys,
    values,
    doc_lengths,
):
    highest = lax.Precision.HIGHEST
    tok_rows = mixer_input.shape[0]
    groups_dev = query_weight.shape[0]
    heads_dev = step_size.shape[0]
    head_group = heads_dev // groups_dev
    query_group = QHEADS // GROUPS
    shard_index = lax.axis_index("ctx")
    first_pos = shard_index * tok_rows
    row_index = jnp.arange(tok_rows, dtype=jnp.int32)
    own_pos = first_pos + row_index
    own_docs = segment_ids(own_pos, doc_lengths)
    prev_doc = segment_ids(jnp.reshape(first_pos - 1, (1,)), doc_lengths)[0]
    input_f32 = mixer_input.reshape(tok_rows, groups_dev, head_group, HEAD_DIM).astype(jnp.float32)
    state_in = in_b.reshape(tok_rows, groups_dev, STATE)
    state_out = in_c.reshape(tok_rows, groups_dev, STATE)
    upper_ones = (row_index[:, None] <= row_index[None, :]).astype(jnp.float32)
    cum_decay = jnp.dot(log_decay, upper_ones, precision=highest).reshape(
        groups_dev, head_group, tok_rows
    )
    step_rows = step_size.reshape(groups_dev, head_group, tok_rows)
    last_doc = (own_docs == own_docs[-1]).astype(jnp.float32)
    end_weight = jnp.exp(cum_decay[:, :, -1:] - cum_decay) * last_doc[None, None, :] * step_rows
    weighted = input_f32 * jnp.transpose(end_weight, (2, 0, 1))[..., None]
    local_state = jnp.einsum(
        "sgjp,sgn->gjpn", weighted, state_in.astype(jnp.float32), precision=highest
    )
    carry_mask = (own_docs == prev_doc).astype(jnp.float32)
    ctx_count = lax.axis_size("ctx")
    owned = heads_dev // ctx_count
    block_log = jnp.where(carry_mask[-1] > 0, cum_decay[:, :, -1], -jnp.inf).reshape(heads_dev)
    log_rows = jnp.broadcast_to(block_log[:, None, None], (heads_dev, 8, STATE))
    payload = jnp.concatenate([local_state.reshape(heads_dev, HEAD_DIM, STATE), log_rows], axis=1)
    gathered = lax.all_to_all(payload, "ctx", 0, 0, tiled=True).reshape(
        ctx_count, owned, HEAD_DIM + 8, STATE
    )
    states_mine = gathered[:, :, :HEAD_DIM, :]
    mine_log = gathered[:, :, HEAD_DIM, 0]
    block_row = jnp.arange(ctx_count, dtype=jnp.int32)
    between = (block_row[None, :, None] < block_row[None, None, :]) & (
        block_row[None, None, :] < block_row[:, None, None]
    )
    log_span = jnp.sum(
        jnp.where(between[None], jnp.transpose(mine_log)[:, None, None, :], 0.0), axis=-1
    )
    earlier = block_row[:, None] > block_row[None, :]
    transfer = jnp.where(earlier[None], jnp.exp(log_span), 0.0)
    incoming_mine = jnp.einsum("kcd,dkpn->ckpn", transfer, states_mine, precision=highest)
    incoming = lax.all_to_all(
        incoming_mine.reshape(ctx_count * owned, HEAD_DIM, STATE), "ctx", 0, 0, tiled=True
    ).reshape(groups_dev, head_group, HEAD_DIM, STATE)
    same_doc = (own_docs[:, None] == own_docs[None, :]) & (row_index[:, None] >= row_index[None, :])
    log_gap = cum_decay[:, :, :, None] - cum_decay[:, :, None, :]
    decay_matrix = jnp.exp(jnp.where(same_doc[None, None], log_gap, -jnp.inf))
    pair_products = jnp.einsum(
        "tgn,sgn->gts", state_out, state_in, preferred_element_type=jnp.float32
    )
    mixing = pair_products[:, None] * decay_matrix * step_rows[:, :, None, :]
    local_out = jnp.einsum("gjts,sgjp->tgjp", mixing, input_f32, precision=highest)
    carry_weight = jnp.exp(cum_decay) * carry_mask[None, None, :]
    carried_out = (
        jnp.einsum("tgn,gjpn->tgjp", state_out.astype(jnp.float32), incoming, precision=highest)
        * jnp.transpose(carry_weight, (2, 0, 1))[..., None]
    )
    skip_rows = skip_gain.reshape(groups_dev, head_group)[None, :, :, None] * input_f32
    mixer_full = (local_out + carried_out + skip_rows).reshape(tok_rows, -1)
    gated = mixer_full * jax.nn.silu(gate.astype(jnp.float32))
    square_local = jnp.sum(gated * gated, axis=1)
    square_sum = lax.psum(square_local, "head")
    mixer_out = (
        gated
        * lax.rsqrt(square_sum / (MIXER_HEADS * HEAD_DIM) + EPSILON)[:, None]
        * norm_gain[None, :]
    ).astype(jnp.bfloat16)
    query = jnp.einsum(
        "tgf,gfo->tgo",
        mixer_out.reshape(tok_rows, groups_dev, -1),
        query_weight,
        preferred_element_type=jnp.float32,
    )
    query = query.astype(jnp.bfloat16).reshape(tok_rows, groups_dev, query_group, ATT_DIM)

    kv_local = jnp.concatenate(
        [
            keys.reshape(tok_rows, groups_dev, ATT_DIM),
            values.reshape(tok_rows, groups_dev, ATT_DIM),
        ],
        axis=2,
    )
    ctx_count = lax.axis_size("ctx")
    back = min(ctx_count - 1, -(-(MOST - 1) // tok_rows))
    pieces = [kv_local]
    for shift in range(1, back + 1):
        pieces.append(
            lax.ppermute(
                kv_local, "ctx", [(source, source + shift) for source in range(ctx_count - shift)]
            )
        )
    window_rows = (back + 1) * tok_rows
    window_pad = -window_rows % KEY_CHUNK
    kv_window = jnp.concatenate(
        [jnp.zeros((window_pad, groups_dev, 2 * ATT_DIM), kv_local.dtype)] + pieces[::-1], axis=0
    )
    window_base = first_pos - back * tok_rows - window_pad
    doc_starts = jnp.cumsum(doc_lengths) - doc_lengths
    row_low = jnp.max(
        jnp.where(doc_starts[None, :] <= own_pos[:, None], doc_starts[None, :], 0), axis=1
    )
    first_chunk = jnp.maximum(row_low[0] - window_base, 0) // KEY_CHUNK
    last_chunk = (window_rows + window_pad - 1) // KEY_CHUNK
    stacked_low = jnp.tile(row_low, query_group)[:, None]
    stacked_high = jnp.tile(own_pos, query_group)[:, None]
    group_outs = []
    for group in range(groups_dev):
        stacked_query = jnp.transpose(query[:, group], (1, 0, 2)).reshape(-1, ATT_DIM)
        stacked_out = flash_attention(
            stacked_query,
            kv_window[:, group],
            stacked_low,
            stacked_high,
            first_chunk,
            last_chunk - first_chunk + 1,
            window_base,
        )
        group_outs.append(
            jnp.transpose(stacked_out.reshape(query_group, tok_rows, ATT_DIM), (1, 0, 2))
        )
    attn_out = jnp.stack(group_outs, axis=1).reshape(tok_rows, -1)
    return (mixer_out, attn_out)


def solution(mesh):
    return jax.shard_map(
        shards,
        mesh=mesh,
        in_specs=(
            P("ctx", "head"),
            P("ctx", "head"),
            P("ctx", "head"),
            P("ctx", "head"),
            P("head", "ctx"),
            P("head", "ctx"),
            P("head"),
            P("head"),
            P("head", None, None),
            P("ctx", "head"),
            P("ctx", "head"),
            P(),
        ),
        out_specs=(P("ctx", "head"), P("ctx", "head")),
        check_vma=False,
    )
```

```python
import jax
import jax.numpy as jnp
from jax import lax
from jax.sharding import PartitionSpec as P
from jax.experimental import pallas as pl
from jax.experimental.pallas import tpu as pltpu

MIXER_HEADS = 256
HEAD_DIM = 64
STATE = 256
GROUPS = 8
QHEADS = 64
ATT_DIM = 128


EPSILON = 1e-05
NEG_FILL = -1e30
KEY_CHUNK = 256
MOST = 2176


def segment_ids(positions, doc_lengths):
    doc_starts = jnp.cumsum(doc_lengths) - doc_lengths
    hits = (doc_starts[None, :] <= positions[:, None]).astype(jnp.int32)
    return jnp.sum(hits, axis=1) - 1


def attention_kernel(chunk_ref, query_ref, kv_ref, low_ref, high_ref, out_ref):
    rows = query_ref.shape[0]
    query_rows = query_ref[...]
    low = low_ref[...]
    high = high_ref[...]

    def chunk_turn(turn, carried):
        best_old, total_old, accum_old = carried
        start = pl.multiple_of((chunk_ref[0] + turn) * KEY_CHUNK, KEY_CHUNK)
        piece = kv_ref[pl.ds(start, KEY_CHUNK), :]
        key_part = piece[:, :ATT_DIM]
        value_part = piece[:, ATT_DIM:]
        scores = lax.dot_general(
            query_rows, key_part, (((1,), (1,)), ((), ())), preferred_element_type=jnp.float32
        ) * ATT_DIM ** (-0.5)
        key_pos = chunk_ref[2] + start + lax.broadcasted_iota(jnp.int32, (rows, KEY_CHUNK), 1)
        visible = (key_pos >= low) & (key_pos <= high)
        scores = jnp.where(visible, scores, NEG_FILL)
        best_new = jnp.maximum(best_old, jnp.max(scores, axis=1, keepdims=True))
        weights = jnp.where(visible, jnp.exp(scores - best_new), 0.0)
        rescale = jnp.exp(best_old - best_new)
        total_new = total_old * rescale + jnp.sum(weights, axis=1, keepdims=True)
        accum_new = accum_old * rescale + jnp.dot(
            weights.astype(jnp.bfloat16), value_part, preferred_element_type=jnp.float32
        )
        return (best_new, total_new, accum_new)

    initial = (
        jnp.full((rows, 1), NEG_FILL, jnp.float32),
        jnp.zeros((rows, 1), jnp.float32),
        jnp.zeros((rows, ATT_DIM), jnp.float32),
    )
    _, total, accum = lax.fori_loop(0, chunk_ref[1], chunk_turn, initial)
    out_ref[...] = (accum / total).astype(out_ref.dtype)


def flash_attention(query_flat, kv_rows, low, high, first_chunk, chunk_count, base):
    rows = query_flat.shape[0]
    chunk_info = jnp.stack([first_chunk, chunk_count, base]).astype(jnp.int32)
    grid_spec = pltpu.PrefetchScalarGridSpec(
        num_scalar_prefetch=1,
        grid=(1,),
        in_specs=[
            pl.BlockSpec(query_flat.shape, lambda i, info: (0, 0)),
            pl.BlockSpec(kv_rows.shape, lambda i, info: (0, 0)),
            pl.BlockSpec((rows, 1), lambda i, info: (0, 0)),
            pl.BlockSpec((rows, 1), lambda i, info: (0, 0)),
        ],
        out_specs=pl.BlockSpec(query_flat.shape, lambda i, info: (0, 0)),
    )
    return pl.pallas_call(
        attention_kernel,
        grid_spec=grid_spec,
        out_shape=jax.ShapeDtypeStruct(query_flat.shape, jnp.bfloat16),
    )(chunk_info, query_flat, kv_rows, low, high)


def shards(
    mixer_input,
    gate,
    in_b,
    in_c,
    step_size,
    log_decay,
    skip_gain,
    norm_gain,
    query_weight,
    keys,
    values,
    doc_lengths,
):
    highest = lax.Precision.HIGHEST
    tok_rows = mixer_input.shape[0]
    groups_dev = query_weight.shape[0]
    heads_dev = step_size.shape[0]
    head_group = heads_dev // groups_dev
    query_group = QHEADS // GROUPS
    shard_index = lax.axis_index("ctx")
    first_pos = shard_index * tok_rows
    row_index = jnp.arange(tok_rows, dtype=jnp.int32)
    own_pos = first_pos + row_index
    own_docs = segment_ids(own_pos, doc_lengths)
    prev_doc = segment_ids(jnp.reshape(first_pos - 1, (1,)), doc_lengths)[0]
    input_f32 = mixer_input.reshape(tok_rows, groups_dev, head_group, HEAD_DIM).astype(jnp.float32)
    state_in = in_b.reshape(tok_rows, groups_dev, STATE)
    state_out = in_c.reshape(tok_rows, groups_dev, STATE)
    upper_ones = (row_index[:, None] <= row_index[None, :]).astype(jnp.float32)
    cum_decay = jnp.dot(log_decay, upper_ones, precision=highest).reshape(
        groups_dev, head_group, tok_rows
    )
    step_rows = step_size.reshape(groups_dev, head_group, tok_rows)
    last_doc = (own_docs == own_docs[-1]).astype(jnp.float32)
    end_weight = jnp.exp(cum_decay[:, :, -1:] - cum_decay) * last_doc[None, None, :] * step_rows
    weighted = input_f32 * jnp.transpose(end_weight, (2, 0, 1))[..., None]
    local_state = jnp.einsum(
        "sgjp,sgn->gjpn", weighted, state_in.astype(jnp.float32), precision=highest
    )
    carry_mask = (own_docs == prev_doc).astype(jnp.float32)
    ctx_count = lax.axis_size("ctx")
    owned = heads_dev // ctx_count
    block_log = jnp.where(carry_mask[-1] > 0, cum_decay[:, :, -1], -jnp.inf).reshape(heads_dev)
    log_rows = jnp.broadcast_to(block_log[:, None, None], (heads_dev, 8, STATE))
    payload = jnp.concatenate([local_state.reshape(heads_dev, HEAD_DIM, STATE), log_rows], axis=1)
    gathered = lax.all_to_all(payload, "ctx", 0, 0, tiled=True).reshape(
        ctx_count, owned, HEAD_DIM + 8, STATE
    )
    states_mine = gathered[:, :, :HEAD_DIM, :]
    mine_log = gathered[:, :, HEAD_DIM, 0]
    block_row = jnp.arange(ctx_count, dtype=jnp.int32)
    between = (block_row[None, :, None] < block_row[None, None, :]) & (
        block_row[None, None, :] < block_row[:, None, None]
    )
    log_span = jnp.sum(
        jnp.where(between[None], jnp.transpose(mine_log)[:, None, None, :], 0.0), axis=-1
    )
    earlier = block_row[:, None] > block_row[None, :]
    transfer = jnp.where(earlier[None], jnp.exp(log_span), 0.0)
    incoming_mine = jnp.einsum("kcd,dkpn->ckpn", transfer, states_mine, precision=highest)
    incoming = lax.all_to_all(
        incoming_mine.reshape(ctx_count * owned, HEAD_DIM, STATE), "ctx", 0, 0, tiled=True
    ).reshape(groups_dev, head_group, HEAD_DIM, STATE)
    same_doc = (own_docs[:, None] == own_docs[None, :]) & (row_index[:, None] >= row_index[None, :])
    log_gap = cum_decay[:, :, :, None] - cum_decay[:, :, None, :]
    decay_matrix = jnp.exp(jnp.where(same_doc[None, None], log_gap, -jnp.inf))
    pair_products = jnp.einsum(
        "tgn,sgn->gts", state_out, state_in, preferred_element_type=jnp.float32
    )
    mixing = pair_products[:, None] * decay_matrix * step_rows[:, :, None, :]
    local_out = jnp.einsum("gjts,sgjp->tgjp", mixing, input_f32, precision=highest)
    carry_weight = jnp.exp(cum_decay) * carry_mask[None, None, :]
    carried_out = (
        jnp.einsum("tgn,gjpn->tgjp", state_out.astype(jnp.float32), incoming, precision=highest)
        * jnp.transpose(carry_weight, (2, 0, 1))[..., None]
    )
    skip_rows = skip_gain.reshape(groups_dev, head_group)[None, :, :, None] * input_f32
    mixer_full = (local_out + carried_out + skip_rows).reshape(tok_rows, -1)
    gated = mixer_full * jax.nn.silu(gate.astype(jnp.float32))
    square_local = jnp.sum(gated * gated, axis=1)
    square_sum = lax.psum(square_local, "head")
    mixer_out = (
        gated
        * lax.rsqrt(square_sum / (MIXER_HEADS * HEAD_DIM) + EPSILON)[:, None]
        * norm_gain[None, :]
    ).astype(jnp.bfloat16)
    query = jnp.einsum(
        "tgf,gfo->tgo",
        mixer_out.reshape(tok_rows, groups_dev, -1),
        query_weight,
        preferred_element_type=jnp.float32,
    )
    query = query.astype(jnp.bfloat16).reshape(tok_rows, groups_dev, query_group, ATT_DIM)

    kv_local = jnp.concatenate(
        [
            keys.reshape(tok_rows, groups_dev, ATT_DIM),
            values.reshape(tok_rows, groups_dev, ATT_DIM),
        ],
        axis=2,
    )
    ctx_count = lax.axis_size("ctx")
    back = min(ctx_count - 1, -(-(MOST - 1) // tok_rows))
    held = kv_local[None]
    while held.shape[0] < back + 1:
        shift = held.shape[0]
        sent = held[held.shape[0] - min(shift, back + 1 - shift) :]
        arrived = lax.ppermute(
            sent, "ctx", [(source, source + shift) for source in range(ctx_count - shift)]
        )
        held = jnp.concatenate([arrived, held], axis=0)
    window_rows = (back + 1) * tok_rows
    window_pad = -window_rows % KEY_CHUNK
    kv_window = jnp.concatenate(
        [
            jnp.zeros((window_pad, groups_dev, 2 * ATT_DIM), kv_local.dtype),
            held.reshape(window_rows, groups_dev, 2 * ATT_DIM),
        ],
        axis=0,
    )
    window_base = first_pos - back * tok_rows - window_pad
    doc_starts = jnp.cumsum(doc_lengths) - doc_lengths
    row_low = jnp.max(
        jnp.where(doc_starts[None, :] <= own_pos[:, None], doc_starts[None, :], 0), axis=1
    )
    first_chunk = jnp.maximum(row_low[0] - window_base, 0) // KEY_CHUNK
    last_chunk = (window_rows + window_pad - 1) // KEY_CHUNK
    stacked_low = jnp.tile(row_low, query_group)[:, None]
    stacked_high = jnp.tile(own_pos, query_group)[:, None]
    group_outs = []
    for group in range(groups_dev):
        stacked_query = jnp.transpose(query[:, group], (1, 0, 2)).reshape(-1, ATT_DIM)
        stacked_out = flash_attention(
            stacked_query,
            kv_window[:, group],
            stacked_low,
            stacked_high,
            first_chunk,
            last_chunk - first_chunk + 1,
            window_base,
        )
        group_outs.append(
            jnp.transpose(stacked_out.reshape(query_group, tok_rows, ATT_DIM), (1, 0, 2))
        )
    attn_out = jnp.stack(group_outs, axis=1).reshape(tok_rows, -1)
    return (mixer_out, attn_out)


def solution(mesh):
    return jax.shard_map(
        shards,
        mesh=mesh,
        in_specs=(
            P("ctx", "head"),
            P("ctx", "head"),
            P("ctx", "head"),
            P("ctx", "head"),
            P("head", "ctx"),
            P("head", "ctx"),
            P("head"),
            P("head"),
            P("head", None, None),
            P("ctx", "head"),
            P("ctx", "head"),
            P(),
        ),
        out_specs=(P("ctx", "head"), P("ctx", "head")),
        check_vma=False,
    )
```

```python
import jax
import jax.numpy as jnp
from jax import lax
from jax.sharding import PartitionSpec as P
from jax.experimental import pallas as pl
from jax.experimental.pallas import tpu as pltpu

MIXER_HEADS = 256
HEAD_DIM = 64
STATE = 256
GROUPS = 8
QHEADS = 64
ATT_DIM = 128


EPSILON = 1e-05
NEG_FILL = -1e30
KEY_CHUNK = 256


def segment_ids(positions, doc_lengths):
    doc_starts = jnp.cumsum(doc_lengths) - doc_lengths
    hits = (doc_starts[None, :] <= positions[:, None]).astype(jnp.int32)
    return jnp.sum(hits, axis=1) - 1


def attention_kernel(chunk_ref, query_ref, kv_ref, low_ref, high_ref, out_ref):
    tokens = query_ref.shape[0]
    heads = query_ref.shape[1] // ATT_DIM
    rows = tokens * heads
    query_rows = jnp.concatenate(
        [query_ref[:, head * ATT_DIM : (head + 1) * ATT_DIM] for head in range(heads)], axis=0
    )
    low = jnp.concatenate([low_ref[...]] * heads, axis=0)
    high = jnp.concatenate([high_ref[...]] * heads, axis=0)

    def chunk_turn(turn, carried):
        best_old, total_old, accum_old = carried
        start = pl.multiple_of((chunk_ref[0] + turn) * KEY_CHUNK, KEY_CHUNK)
        piece = kv_ref[pl.ds(start, KEY_CHUNK), :]
        key_part = piece[:, :ATT_DIM]
        value_part = piece[:, ATT_DIM:]
        scores = lax.dot_general(
            query_rows, key_part, (((1,), (1,)), ((), ())), preferred_element_type=jnp.float32
        ) * ATT_DIM ** (-0.5)
        key_pos = start + lax.broadcasted_iota(jnp.int32, (rows, KEY_CHUNK), 1)
        visible = (key_pos >= low) & (key_pos <= high)
        scores = jnp.where(visible, scores, -jnp.inf)
        best_new = jnp.maximum(best_old, jnp.max(scores, axis=1, keepdims=True))
        weights = jnp.exp(scores - best_new)
        rescale = jnp.exp(best_old - best_new)
        total_new = total_old * rescale + jnp.sum(weights, axis=1, keepdims=True)
        accum_new = accum_old * rescale + jnp.dot(
            weights.astype(jnp.bfloat16), value_part, preferred_element_type=jnp.float32
        )
        return (best_new, total_new, accum_new)

    initial = (
        jnp.full((rows, 1), NEG_FILL, jnp.float32),
        jnp.zeros((rows, 1), jnp.float32),
        jnp.zeros((rows, ATT_DIM), jnp.float32),
    )
    _, total, accum = lax.fori_loop(0, chunk_ref[1], chunk_turn, initial)
    result = (accum / total).astype(out_ref.dtype)
    for head in range(heads):
        out_ref[:, head * ATT_DIM : (head + 1) * ATT_DIM] = result[
            head * tokens : (head + 1) * tokens
        ]


def flash_attention(query_rows, kv_rows, low, high, first_chunk, chunk_count):
    tokens = query_rows.shape[0]
    chunk_info = jnp.stack([first_chunk, chunk_count]).astype(jnp.int32)
    grid_spec = pltpu.PrefetchScalarGridSpec(
        num_scalar_prefetch=1,
        grid=(1,),
        in_specs=[
            pl.BlockSpec(query_rows.shape, lambda i, info: (0, 0)),
            pl.BlockSpec(kv_rows.shape, lambda i, info: (0, 0)),
            pl.BlockSpec((tokens, 1), lambda i, info: (0, 0)),
            pl.BlockSpec((tokens, 1), lambda i, info: (0, 0)),
        ],
        out_specs=pl.BlockSpec(query_rows.shape, lambda i, info: (0, 0)),
    )
    return pl.pallas_call(
        attention_kernel,
        grid_spec=grid_spec,
        out_shape=jax.ShapeDtypeStruct(query_rows.shape, jnp.bfloat16),
    )(chunk_info, query_rows, kv_rows, low, high)

def shards(
    mixer_input,
    gate,
    in_b,
    in_c,
    step_size,
    log_decay,
    skip_gain,
    norm_gain,
    query_weight,
    keys,
    values,
    doc_lengths,
):
    highest = lax.Precision.HIGHEST
    tok_rows = mixer_input.shape[0]
    groups_dev = query_weight.shape[0]
    heads_dev = step_size.shape[0]
    head_group = heads_dev // groups_dev
    query_group = QHEADS // GROUPS
    shard_index = lax.axis_index("ctx")
    first_pos = shard_index * tok_rows
    row_index = jnp.arange(tok_rows, dtype=jnp.int32)
    own_pos = first_pos + row_index
    own_docs = segment_ids(own_pos, doc_lengths)
    prev_doc = segment_ids(jnp.reshape(first_pos - 1, (1,)), doc_lengths)[0]
    input_f32 = mixer_input.reshape(tok_rows, groups_dev, head_group, HEAD_DIM).astype(jnp.float32)
    state_in = in_b.reshape(tok_rows, groups_dev, STATE)
    state_out = in_c.reshape(tok_rows, groups_dev, STATE)
    upper_ones = (row_index[:, None] <= row_index[None, :]).astype(jnp.float32)
    cum_decay = jnp.dot(log_decay, upper_ones, precision=highest).reshape(
        groups_dev, head_group, tok_rows
    )
    step_rows = step_size.reshape(groups_dev, head_group, tok_rows)
    last_doc = (own_docs == own_docs[-1]).astype(jnp.float32)
    end_weight = jnp.exp(cum_decay[:, :, -1:] - cum_decay) * last_doc[None, None, :] * step_rows
    weighted = input_f32 * jnp.transpose(end_weight, (2, 0, 1))[..., None]
    local_state = jnp.einsum(
        "sgjp,sgn->gjpn", weighted, state_in.astype(jnp.float32), precision=highest
    )
    carry_mask = (own_docs == prev_doc).astype(jnp.float32)
    ctx_count = lax.axis_size("ctx")
    owned = heads_dev // ctx_count
    block_log = jnp.where(carry_mask[-1] > 0, cum_decay[:, :, -1], -jnp.inf).reshape(heads_dev)
    log_rows = jnp.broadcast_to(block_log[:, None, None], (heads_dev, 8, STATE))
    payload = jnp.concatenate([local_state.reshape(heads_dev, HEAD_DIM, STATE), log_rows], axis=1)
    gathered = lax.all_to_all(payload, "ctx", 0, 0, tiled=True).reshape(
        ctx_count, owned, HEAD_DIM + 8, STATE
    )
    states_mine = gathered[:, :, :HEAD_DIM, :]
    mine_log = gathered[:, :, HEAD_DIM, 0]
    block_row = jnp.arange(ctx_count, dtype=jnp.int32)
    between = (block_row[None, :, None] < block_row[None, None, :]) & (
        block_row[None, None, :] < block_row[:, None, None]
    )
    log_span = jnp.sum(
        jnp.where(between[None], jnp.transpose(mine_log)[:, None, None, :], 0.0), axis=-1
    )
    earlier = block_row[:, None] > block_row[None, :]
    transfer = jnp.where(earlier[None], jnp.exp(log_span), 0.0)
    incoming_mine = jnp.einsum("kcd,dkpn->ckpn", transfer, states_mine, precision=highest)
    incoming = lax.all_to_all(
        incoming_mine.reshape(ctx_count * owned, HEAD_DIM, STATE), "ctx", 0, 0, tiled=True
    ).reshape(groups_dev, head_group, HEAD_DIM, STATE)
    same_doc = (own_docs[:, None] == own_docs[None, :]) & (row_index[:, None] >= row_index[None, :])
    log_gap = cum_decay[:, :, :, None] - cum_decay[:, :, None, :]
    decay_matrix = jnp.exp(jnp.where(same_doc[None, None], log_gap, -jnp.inf))
    pair_products = jnp.einsum(
        "tgn,sgn->gts", state_out, state_in, preferred_element_type=jnp.float32
    )
    mixing = pair_products[:, None] * decay_matrix * step_rows[:, :, None, :]
    local_out = jnp.einsum("gjts,sgjp->tgjp", mixing, input_f32, precision=highest)
    carry_weight = jnp.exp(cum_decay) * carry_mask[None, None, :]
    carried_out = (
        jnp.einsum("tgn,gjpn->tgjp", state_out.astype(jnp.float32), incoming, precision=highest)
        * jnp.transpose(carry_weight, (2, 0, 1))[..., None]
    )
    skip_rows = skip_gain.reshape(groups_dev, head_group)[None, :, :, None] * input_f32
    mixer_full = (local_out + carried_out + skip_rows).reshape(tok_rows, -1)
    gated = mixer_full * jax.nn.silu(gate.astype(jnp.float32))
    square_local = jnp.sum(gated * gated, axis=1)
    square_sum = lax.psum(square_local, "head")
    mixer_out = (
        gated
        * lax.rsqrt(square_sum / (MIXER_HEADS * HEAD_DIM) + EPSILON)[:, None]
        * norm_gain[None, :]
    ).astype(jnp.bfloat16)
    query = jnp.einsum(
        "tgf,gfo->tgo",
        mixer_out.reshape(tok_rows, groups_dev, -1),
        query_weight,
        preferred_element_type=jnp.float32,
    )
    query = query.astype(jnp.bfloat16).reshape(tok_rows, groups_dev, query_group, ATT_DIM)

    kv_local = jnp.concatenate(
        [
            keys.reshape(tok_rows, groups_dev, ATT_DIM),
            values.reshape(tok_rows, groups_dev, ATT_DIM),
        ],
        axis=2,
    )
    kv_all = lax.all_gather(kv_local, "ctx", axis=0, tiled=True)
    doc_starts = jnp.cumsum(doc_lengths) - doc_lengths
    row_low = jnp.max(
        jnp.where(doc_starts[None, :] <= own_pos[:, None], doc_starts[None, :], 0), axis=1
    )
    first_chunk = row_low[0] // KEY_CHUNK
    last_chunk = (first_pos + tok_rows - 1) // KEY_CHUNK
    group_outs = []
    for group in range(groups_dev):
        group_outs.append(
            flash_attention(
                query[:, group].reshape(tok_rows, query_group * ATT_DIM),
                kv_all[:, group],
                row_low[:, None],
                own_pos[:, None],
                first_chunk,
                last_chunk - first_chunk + 1,
            )
        )
    attn_out = jnp.concatenate(group_outs, axis=1)
    return (mixer_out, attn_out)


def solution(mesh):
    return jax.shard_map(
        shards,
        mesh=mesh,
        in_specs=(
            P("ctx", "head"),
            P("ctx", "head"),
            P("ctx", "head"),
            P("ctx", "head"),
            P("head", "ctx"),
            P("head", "ctx"),
            P("head"),
            P("head"),
            P("head", None, None),
            P("ctx", "head"),
            P("ctx", "head"),
            P(),
        ),
        out_specs=(P("ctx", "head"), P("ctx", "head")),
        check_vma=False,
    )
```

```python
import jax
import jax.numpy as jnp
from jax import lax
from jax.sharding import PartitionSpec as P
from jax.experimental import pallas as pl
from jax.experimental.pallas import tpu as pltpu

MIXER_HEADS = 256
HEAD_DIM = 64
STATE = 256
GROUPS = 8
QHEADS = 64
ATT_DIM = 128


EPSILON = 1e-05
NEG_FILL = -1e30
KEY_CHUNK = 256


def segment_ids(positions, doc_lengths):
    doc_starts = jnp.cumsum(doc_lengths) - doc_lengths
    hits = (doc_starts[None, :] <= positions[:, None]).astype(jnp.int32)
    return jnp.sum(hits, axis=1) - 1


def attention_kernel(chunk_ref, query_ref, kv_ref, low_ref, high_ref, out_ref):
    tokens = query_ref.shape[0]
    heads = query_ref.shape[1] // ATT_DIM
    rows = tokens * heads
    query_rows = jnp.concatenate(
        [query_ref[:, head * ATT_DIM : (head + 1) * ATT_DIM] for head in range(heads)], axis=0
    )
    low = jnp.concatenate([low_ref[...]] * heads, axis=0)
    high = jnp.concatenate([high_ref[...]] * heads, axis=0)

    def chunk_turn(turn, carried):
        best_old, total_old, accum_old = carried
        start = pl.multiple_of((chunk_ref[0] + turn) * KEY_CHUNK, KEY_CHUNK)
        piece = kv_ref[pl.ds(start, KEY_CHUNK), :]
        key_part = piece[:, :ATT_DIM]
        value_part = piece[:, ATT_DIM:]
        scores = lax.dot_general(
            query_rows, key_part, (((1,), (1,)), ((), ())), preferred_element_type=jnp.float32
        ) * ATT_DIM ** (-0.5)
        key_pos = start + lax.broadcasted_iota(jnp.int32, (rows, KEY_CHUNK), 1)
        visible = (key_pos >= low) & (key_pos <= high)
        scores = jnp.where(visible, scores, -jnp.inf)
        best_new = jnp.maximum(best_old, jnp.max(scores, axis=1, keepdims=True))
        weights = jnp.exp(scores - best_new)
        rescale = jnp.exp(best_old - best_new)
        total_new = total_old * rescale + jnp.sum(weights, axis=1, keepdims=True)
        accum_new = accum_old * rescale + jnp.dot(
            weights.astype(jnp.bfloat16), value_part, preferred_element_type=jnp.float32
        )
        return (best_new, total_new, accum_new)

    initial = (
        jnp.full((rows, 1), NEG_FILL, jnp.float32),
        jnp.zeros((rows, 1), jnp.float32),
        jnp.zeros((rows, ATT_DIM), jnp.float32),
    )
    _, total, accum = lax.fori_loop(0, chunk_ref[1], chunk_turn, initial)
    result = (accum / total).astype(out_ref.dtype)
    for head in range(heads):
        out_ref[:, head * ATT_DIM : (head + 1) * ATT_DIM] = result[
            head * tokens : (head + 1) * tokens
        ]


def flash_attention(query_rows, kv_rows, low, high, first_chunk, chunk_count):
    tokens = query_rows.shape[0]
    chunk_info = jnp.stack([first_chunk, chunk_count]).astype(jnp.int32)
    grid_spec = pltpu.PrefetchScalarGridSpec(
        num_scalar_prefetch=1,
        grid=(1,),
        in_specs=[
            pl.BlockSpec(query_rows.shape, lambda i, info: (0, 0)),
            pl.BlockSpec(kv_rows.shape, lambda i, info: (0, 0)),
            pl.BlockSpec((tokens, 1), lambda i, info: (0, 0)),
            pl.BlockSpec((tokens, 1), lambda i, info: (0, 0)),
        ],
        out_specs=pl.BlockSpec(query_rows.shape, lambda i, info: (0, 0)),
    )
    return pl.pallas_call(
        attention_kernel,
        grid_spec=grid_spec,
        out_shape=jax.ShapeDtypeStruct(query_rows.shape, jnp.bfloat16),
    )(chunk_info, query_rows, kv_rows, low, high)

def shards(
    mixer_input,
    gate,
    in_b,
    in_c,
    step_size,
    log_decay,
    skip_gain,
    norm_gain,
    query_weight,
    keys,
    values,
    doc_lengths,
):
    highest = lax.Precision.HIGHEST
    tok_rows = mixer_input.shape[0]
    groups_dev = query_weight.shape[0]
    heads_dev = step_size.shape[0]
    head_group = heads_dev // groups_dev
    query_group = QHEADS // GROUPS
    shard_index = lax.axis_index("ctx")
    first_pos = shard_index * tok_rows
    row_index = jnp.arange(tok_rows, dtype=jnp.int32)
    own_pos = first_pos + row_index
    own_docs = segment_ids(own_pos, doc_lengths)
    prev_doc = segment_ids(jnp.reshape(first_pos - 1, (1,)), doc_lengths)[0]
    input_f32 = mixer_input.reshape(tok_rows, groups_dev, head_group, HEAD_DIM).astype(jnp.float32)
    state_in = in_b.reshape(tok_rows, groups_dev, STATE)
    state_out = in_c.reshape(tok_rows, groups_dev, STATE)
    upper_ones = (row_index[:, None] <= row_index[None, :]).astype(jnp.float32)
    cum_decay = jnp.dot(log_decay, upper_ones, precision=highest).reshape(
        groups_dev, head_group, tok_rows
    )
    step_rows = step_size.reshape(groups_dev, head_group, tok_rows)
    last_doc = (own_docs == own_docs[-1]).astype(jnp.float32)
    end_weight = jnp.exp(cum_decay[:, :, -1:] - cum_decay) * last_doc[None, None, :] * step_rows
    weighted = input_f32 * jnp.transpose(end_weight, (2, 0, 1))[..., None]
    local_state = jnp.einsum(
        "sgjp,sgn->gjpn", weighted, state_in.astype(jnp.float32), precision=highest
    )
    carry_mask = (own_docs == prev_doc).astype(jnp.float32)
    ctx_count = lax.axis_size("ctx")
    owned = heads_dev // ctx_count
    block_log = jnp.where(carry_mask[-1] > 0, cum_decay[:, :, -1], -jnp.inf).reshape(heads_dev)
    core = shard_index % 2
    half_heads = heads_dev // 2
    pair_swap = [(source, source ^ 1) for source in range(ctx_count)]
    log_rows = jnp.broadcast_to(block_log[:, None, None], (heads_dev, 8, STATE))
    augmented = jnp.concatenate(
        [local_state.reshape(heads_dev, HEAD_DIM, STATE), log_rows], axis=1
    )
    partner = lax.ppermute(
        lax.dynamic_slice_in_dim(augmented, (1 - core) * half_heads, half_heads, 0),
        "ctx",
        pair_swap,
    )
    mine = lax.dynamic_slice_in_dim(augmented, core * half_heads, half_heads, 0)
    first_core = core == 0
    early_state = jnp.where(first_core, mine[:, :HEAD_DIM], partner[:, :HEAD_DIM])
    late_state = jnp.where(first_core, partner[:, :HEAD_DIM], mine[:, :HEAD_DIM])
    early_log = jnp.where(first_core, mine[:, HEAD_DIM, 0], partner[:, HEAD_DIM, 0])
    late_log = jnp.where(first_core, partner[:, HEAD_DIM, 0], mine[:, HEAD_DIM, 0])
    pair_state = jnp.exp(late_log)[:, None, None] * early_state + late_state
    pair_log = early_log + late_log
    splits = ctx_count // half_heads
    part_rows = HEAD_DIM // splits
    pair_rows = jnp.broadcast_to(
        jnp.repeat(pair_log, splits)[:, None, None], (ctx_count, 8, STATE)
    )
    payload = jnp.concatenate(
        [pair_state.reshape(ctx_count, part_rows, STATE), pair_rows], axis=1
    )
    pair_count = ctx_count // 2
    gathered = lax.all_to_all(payload, "ctx", 0, 0, tiled=True).reshape(
        pair_count, 2, part_rows + 8, STATE
    )
    states_mine = gathered[:, :, :part_rows, :]
    mine_log = gathered[:, :, part_rows, 0]
    block_row = jnp.arange(pair_count, dtype=jnp.int32)
    between = (block_row[None, :, None] < block_row[None, None, :]) & (
        block_row[None, None, :] < block_row[:, None, None]
    )
    log_span = jnp.sum(
        jnp.where(between[None], jnp.transpose(mine_log)[:, None, None, :], 0.0), axis=-1
    )
    earlier = block_row[:, None] > block_row[None, :]
    transfer = jnp.where(earlier[None], jnp.exp(log_span), 0.0)
    incoming_mine = jnp.einsum("ukd,dupn->kupn", transfer, states_mine, precision=highest)
    pair_incoming = lax.all_to_all(
        incoming_mine.reshape(ctx_count, part_rows, STATE), "ctx", 0, 0, tiled=True
    ).reshape(half_heads, HEAD_DIM, STATE)
    after_early = jnp.exp(early_log)[:, None, None] * pair_incoming + early_state
    swapped = lax.ppermute(
        jnp.where(first_core, after_early, pair_incoming), "ctx", pair_swap
    )
    kept = jnp.where(first_core, pair_incoming, after_early)
    incoming = jnp.where(
        first_core,
        jnp.concatenate([kept, swapped], axis=0),
        jnp.concatenate([swapped, kept], axis=0),
    ).reshape(groups_dev, head_group, HEAD_DIM, STATE)
    same_doc = (own_docs[:, None] == own_docs[None, :]) & (row_index[:, None] >= row_index[None, :])
    log_gap = cum_decay[:, :, :, None] - cum_decay[:, :, None, :]
    decay_matrix = jnp.exp(jnp.where(same_doc[None, None], log_gap, -jnp.inf))
    pair_products = jnp.einsum(
        "tgn,sgn->gts", state_out, state_in, preferred_element_type=jnp.float32
    )
    mixing = pair_products[:, None] * decay_matrix * step_rows[:, :, None, :]
    local_out = jnp.einsum("gjts,sgjp->tgjp", mixing, input_f32, precision=highest)
    carry_weight = jnp.exp(cum_decay) * carry_mask[None, None, :]
    carried_out = (
        jnp.einsum("tgn,gjpn->tgjp", state_out.astype(jnp.float32), incoming, precision=highest)
        * jnp.transpose(carry_weight, (2, 0, 1))[..., None]
    )
    skip_rows = skip_gain.reshape(groups_dev, head_group)[None, :, :, None] * input_f32
    mixer_full = (local_out + carried_out + skip_rows).reshape(tok_rows, -1)
    gated = mixer_full * jax.nn.silu(gate.astype(jnp.float32))
    square_local = jnp.sum(gated * gated, axis=1)
    square_sum = lax.psum(square_local, "head")
    mixer_out = (
        gated
        * lax.rsqrt(square_sum / (MIXER_HEADS * HEAD_DIM) + EPSILON)[:, None]
        * norm_gain[None, :]
    ).astype(jnp.bfloat16)
    query = jnp.einsum(
        "tgf,gfo->tgo",
        mixer_out.reshape(tok_rows, groups_dev, -1),
        query_weight,
        preferred_element_type=jnp.float32,
    )
    query = query.astype(jnp.bfloat16).reshape(tok_rows, groups_dev, query_group, ATT_DIM)

    kv_local = jnp.concatenate(
        [
            keys.reshape(tok_rows, groups_dev, ATT_DIM),
            values.reshape(tok_rows, groups_dev, ATT_DIM),
        ],
        axis=2,
    )
    kv_all = lax.all_gather(kv_local, "ctx", axis=0, tiled=True)
    doc_starts = jnp.cumsum(doc_lengths) - doc_lengths
    row_low = jnp.max(
        jnp.where(doc_starts[None, :] <= own_pos[:, None], doc_starts[None, :], 0), axis=1
    )
    first_chunk = row_low[0] // KEY_CHUNK
    last_chunk = (first_pos + tok_rows - 1) // KEY_CHUNK
    group_outs = []
    for group in range(groups_dev):
        group_outs.append(
            flash_attention(
                query[:, group].reshape(tok_rows, query_group * ATT_DIM),
                kv_all[:, group],
                row_low[:, None],
                own_pos[:, None],
                first_chunk,
                last_chunk - first_chunk + 1,
            )
        )
    attn_out = jnp.concatenate(group_outs, axis=1)
    return (mixer_out, attn_out)


def solution(mesh):
    return jax.shard_map(
        shards,
        mesh=mesh,
        in_specs=(
            P("ctx", "head"),
            P("ctx", "head"),
            P("ctx", "head"),
            P("ctx", "head"),
            P("head", "ctx"),
            P("head", "ctx"),
            P("head"),
            P("head"),
            P("head", None, None),
            P("ctx", "head"),
            P("ctx", "head"),
            P(),
        ),
        out_specs=(P("ctx", "head"), P("ctx", "head")),
        check_vma=False,
    )
```

```python
import jax
import jax.numpy as jnp
from jax import lax
from jax.sharding import PartitionSpec as P
from jax.experimental import pallas as pl
from jax.experimental.pallas import tpu as pltpu

MIXER_HEADS = 256
HEAD_DIM = 64
STATE = 256
GROUPS = 8
QHEADS = 64
ATT_DIM = 128


EPSILON = 1e-05
NEG_FILL = -1e30
KEY_CHUNK = 256


def segment_ids(positions, doc_lengths):
    doc_starts = jnp.cumsum(doc_lengths) - doc_lengths
    hits = (doc_starts[None, :] <= positions[:, None]).astype(jnp.int32)
    return jnp.sum(hits, axis=1) - 1


def attention_kernel(chunk_ref, query_ref, kv_ref, low_ref, high_ref, out_ref):
    tokens = query_ref.shape[0]
    heads = query_ref.shape[1] // ATT_DIM
    rows = tokens * heads
    query_rows = jnp.concatenate(
        [query_ref[:, head * ATT_DIM : (head + 1) * ATT_DIM] for head in range(heads)], axis=0
    )
    low = jnp.concatenate([low_ref[...]] * heads, axis=0)
    high = jnp.concatenate([high_ref[...]] * heads, axis=0)

    def chunk_turn(turn, carried):
        best_old, total_old, accum_old = carried
        start = pl.multiple_of((chunk_ref[0] + turn) * KEY_CHUNK, KEY_CHUNK)
        piece = kv_ref[pl.ds(start, KEY_CHUNK), :]
        key_part = piece[:, :ATT_DIM]
        value_part = piece[:, ATT_DIM:]
        scores = lax.dot_general(
            query_rows, key_part, (((1,), (1,)), ((), ())), preferred_element_type=jnp.float32
        ) * ATT_DIM ** (-0.5)
        key_pos = start + lax.broadcasted_iota(jnp.int32, (rows, KEY_CHUNK), 1)
        visible = (key_pos >= low) & (key_pos <= high)
        scores = jnp.where(visible, scores, -jnp.inf)
        best_new = jnp.maximum(best_old, jnp.max(scores, axis=1, keepdims=True))
        weights = jnp.exp(scores - best_new)
        rescale = jnp.exp(best_old - best_new)
        total_new = total_old * rescale + jnp.sum(weights, axis=1, keepdims=True)
        accum_new = accum_old * rescale + jnp.dot(
            weights.astype(jnp.bfloat16), value_part, preferred_element_type=jnp.float32
        )
        return (best_new, total_new, accum_new)

    initial = (
        jnp.full((rows, 1), NEG_FILL, jnp.float32),
        jnp.zeros((rows, 1), jnp.float32),
        jnp.zeros((rows, ATT_DIM), jnp.float32),
    )
    _, total, accum = lax.fori_loop(0, chunk_ref[1], chunk_turn, initial)
    result = (accum / total).astype(out_ref.dtype)
    for head in range(heads):
        out_ref[:, head * ATT_DIM : (head + 1) * ATT_DIM] = result[
            head * tokens : (head + 1) * tokens
        ]


def flash_attention(query_rows, kv_rows, low, high, first_chunk, chunk_count):
    tokens = query_rows.shape[0]
    chunk_info = jnp.stack([first_chunk, chunk_count]).astype(jnp.int32)
    grid_spec = pltpu.PrefetchScalarGridSpec(
        num_scalar_prefetch=1,
        grid=(1,),
        in_specs=[
            pl.BlockSpec(query_rows.shape, lambda i, info: (0, 0)),
            pl.BlockSpec(kv_rows.shape, lambda i, info: (0, 0)),
            pl.BlockSpec((tokens, 1), lambda i, info: (0, 0)),
            pl.BlockSpec((tokens, 1), lambda i, info: (0, 0)),
        ],
        out_specs=pl.BlockSpec(query_rows.shape, lambda i, info: (0, 0)),
    )
    return pl.pallas_call(
        attention_kernel,
        grid_spec=grid_spec,
        out_shape=jax.ShapeDtypeStruct(query_rows.shape, jnp.bfloat16),
    )(chunk_info, query_rows, kv_rows, low, high)

def shards(
    mixer_input,
    gate,
    in_b,
    in_c,
    step_size,
    log_decay,
    skip_gain,
    norm_gain,
    query_weight,
    keys,
    values,
    doc_lengths,
):
    highest = lax.Precision.HIGHEST
    tok_rows = mixer_input.shape[0]
    groups_dev = query_weight.shape[0]
    heads_dev = step_size.shape[0]
    head_group = heads_dev // groups_dev
    query_group = QHEADS // GROUPS
    shard_index = lax.axis_index("ctx")
    first_pos = shard_index * tok_rows
    row_index = jnp.arange(tok_rows, dtype=jnp.int32)
    own_pos = first_pos + row_index
    own_docs = segment_ids(own_pos, doc_lengths)
    prev_doc = segment_ids(jnp.reshape(first_pos - 1, (1,)), doc_lengths)[0]
    input_f32 = mixer_input.reshape(tok_rows, groups_dev, head_group, HEAD_DIM).astype(jnp.float32)
    state_in = in_b.reshape(tok_rows, groups_dev, STATE)
    state_out = in_c.reshape(tok_rows, groups_dev, STATE)
    upper_ones = (row_index[:, None] <= row_index[None, :]).astype(jnp.float32)
    cum_decay = jnp.dot(log_decay, upper_ones, precision=highest).reshape(
        groups_dev, head_group, tok_rows
    )
    step_rows = step_size.reshape(groups_dev, head_group, tok_rows)
    last_doc = (own_docs == own_docs[-1]).astype(jnp.float32)
    end_weight = jnp.exp(cum_decay[:, :, -1:] - cum_decay) * last_doc[None, None, :] * step_rows
    weighted = input_f32 * jnp.transpose(end_weight, (2, 0, 1))[..., None]
    local_state = jnp.einsum(
        "sgjp,sgn->gjpn", weighted, state_in.astype(jnp.float32), precision=highest
    )
    carry_mask = (own_docs == prev_doc).astype(jnp.float32)
    ctx_count = lax.axis_size("ctx")
    owned = heads_dev // ctx_count
    kv_local = jnp.concatenate(
        [
            keys.reshape(tok_rows, groups_dev, ATT_DIM),
            values.reshape(tok_rows, groups_dev, ATT_DIM),
        ],
        axis=2,
    )
    kv_all = lax.all_gather(kv_local, "ctx", axis=0, tiled=True)
    block_log = jnp.where(carry_mask[-1] > 0, cum_decay[:, :, -1], -jnp.inf).reshape(heads_dev)
    core = shard_index % 2
    half_heads = heads_dev // 2
    pair_swap = [(source, source ^ 1) for source in range(ctx_count)]
    log_rows = jnp.broadcast_to(block_log[:, None, None], (heads_dev, 8, STATE))
    augmented = jnp.concatenate(
        [local_state.reshape(heads_dev, HEAD_DIM, STATE), log_rows], axis=1
    )
    partner = lax.ppermute(
        lax.dynamic_slice_in_dim(augmented, (1 - core) * half_heads, half_heads, 0),
        "ctx",
        pair_swap,
    )
    mine = lax.dynamic_slice_in_dim(augmented, core * half_heads, half_heads, 0)
    first_core = core == 0
    early_state = jnp.where(first_core, mine[:, :HEAD_DIM], partner[:, :HEAD_DIM])
    late_state = jnp.where(first_core, partner[:, :HEAD_DIM], mine[:, :HEAD_DIM])
    early_log = jnp.where(first_core, mine[:, HEAD_DIM, 0], partner[:, HEAD_DIM, 0])
    late_log = jnp.where(first_core, partner[:, HEAD_DIM, 0], mine[:, HEAD_DIM, 0])
    pair_state = jnp.exp(late_log)[:, None, None] * early_state + late_state
    pair_log = early_log + late_log
    splits = ctx_count // half_heads
    part_rows = HEAD_DIM // splits
    pair_rows = jnp.broadcast_to(
        jnp.repeat(pair_log, splits)[:, None, None], (ctx_count, 8, STATE)
    )
    payload = jnp.concatenate(
        [pair_state.reshape(ctx_count, part_rows, STATE), pair_rows], axis=1
    )
    pair_count = ctx_count // 2
    gathered = lax.all_to_all(payload, "ctx", 0, 0, tiled=True).reshape(
        pair_count, 2, part_rows + 8, STATE
    )
    states_mine = gathered[:, :, :part_rows, :]
    mine_log = gathered[:, :, part_rows, 0]
    block_row = jnp.arange(pair_count, dtype=jnp.int32)
    between = (block_row[None, :, None] < block_row[None, None, :]) & (
        block_row[None, None, :] < block_row[:, None, None]
    )
    log_span = jnp.sum(
        jnp.where(between[None], jnp.transpose(mine_log)[:, None, None, :], 0.0), axis=-1
    )
    earlier = block_row[:, None] > block_row[None, :]
    transfer = jnp.where(earlier[None], jnp.exp(log_span), 0.0)
    incoming_mine = jnp.einsum("ukd,dupn->kupn", transfer, states_mine, precision=highest)
    pair_incoming = lax.all_to_all(
        incoming_mine.reshape(ctx_count, part_rows, STATE), "ctx", 0, 0, tiled=True
    ).reshape(half_heads, HEAD_DIM, STATE)
    kv_all, pair_incoming = lax.optimization_barrier((kv_all, pair_incoming))
    after_early = jnp.exp(early_log)[:, None, None] * pair_incoming + early_state
    swapped = lax.ppermute(
        jnp.where(first_core, after_early, pair_incoming), "ctx", pair_swap
    )
    kept = jnp.where(first_core, pair_incoming, after_early)
    incoming = jnp.where(
        first_core,
        jnp.concatenate([kept, swapped], axis=0),
        jnp.concatenate([swapped, kept], axis=0),
    ).reshape(groups_dev, head_group, HEAD_DIM, STATE)
    same_doc = (own_docs[:, None] == own_docs[None, :]) & (row_index[:, None] >= row_index[None, :])
    log_gap = cum_decay[:, :, :, None] - cum_decay[:, :, None, :]
    decay_matrix = jnp.exp(jnp.where(same_doc[None, None], log_gap, -jnp.inf))
    pair_products = jnp.einsum(
        "tgn,sgn->gts", state_out, state_in, preferred_element_type=jnp.float32
    )
    mixing = pair_products[:, None] * decay_matrix * step_rows[:, :, None, :]
    local_out = jnp.einsum("gjts,sgjp->tgjp", mixing, input_f32, precision=highest)
    carry_weight = jnp.exp(cum_decay) * carry_mask[None, None, :]
    carried_out = (
        jnp.einsum("tgn,gjpn->tgjp", state_out.astype(jnp.float32), incoming, precision=highest)
        * jnp.transpose(carry_weight, (2, 0, 1))[..., None]
    )
    skip_rows = skip_gain.reshape(groups_dev, head_group)[None, :, :, None] * input_f32
    mixer_full = (local_out + carried_out + skip_rows).reshape(tok_rows, -1)
    gated = mixer_full * jax.nn.silu(gate.astype(jnp.float32))
    square_local = jnp.sum(gated * gated, axis=1)
    square_sum = lax.psum(square_local, "head")
    mixer_out = (
        gated
        * lax.rsqrt(square_sum / (MIXER_HEADS * HEAD_DIM) + EPSILON)[:, None]
        * norm_gain[None, :]
    ).astype(jnp.bfloat16)
    query = jnp.einsum(
        "tgf,gfo->tgo",
        mixer_out.reshape(tok_rows, groups_dev, -1),
        query_weight,
        preferred_element_type=jnp.float32,
    )
    query = query.astype(jnp.bfloat16).reshape(tok_rows, groups_dev, query_group, ATT_DIM)

    doc_starts = jnp.cumsum(doc_lengths) - doc_lengths
    row_low = jnp.max(
        jnp.where(doc_starts[None, :] <= own_pos[:, None], doc_starts[None, :], 0), axis=1
    )
    first_chunk = row_low[0] // KEY_CHUNK
    last_chunk = (first_pos + tok_rows - 1) // KEY_CHUNK
    group_outs = []
    for group in range(groups_dev):
        group_outs.append(
            flash_attention(
                query[:, group].reshape(tok_rows, query_group * ATT_DIM),
                kv_all[:, group],
                row_low[:, None],
                own_pos[:, None],
                first_chunk,
                last_chunk - first_chunk + 1,
            )
        )
    attn_out = jnp.concatenate(group_outs, axis=1)
    return (mixer_out, attn_out)


def solution(mesh):
    return jax.shard_map(
        shards,
        mesh=mesh,
        in_specs=(
            P("ctx", "head"),
            P("ctx", "head"),
            P("ctx", "head"),
            P("ctx", "head"),
            P("head", "ctx"),
            P("head", "ctx"),
            P("head"),
            P("head"),
            P("head", None, None),
            P("ctx", "head"),
            P("ctx", "head"),
            P(),
        ),
        out_specs=(P("ctx", "head"), P("ctx", "head")),
        check_vma=False,
    )
```

```python
import jax
import jax.numpy as jnp
from jax import lax
from jax.sharding import PartitionSpec as P
from jax.experimental import pallas as pl
from jax.experimental.pallas import tpu as pltpu

MIXER_HEADS = 256
HEAD_DIM = 64
STATE = 256
GROUPS = 8
QHEADS = 64
ATT_DIM = 128


EPSILON = 1e-05
NEG_FILL = -1e30
KEY_CHUNK = 256


def segment_ids(positions, doc_lengths):
    doc_starts = jnp.cumsum(doc_lengths) - doc_lengths
    hits = (doc_starts[None, :] <= positions[:, None]).astype(jnp.int32)
    return jnp.sum(hits, axis=1) - 1


def attention_kernel(chunk_ref, query_ref, kv_ref, low_ref, high_ref, out_ref):
    tokens = query_ref.shape[0]
    heads = query_ref.shape[1] // ATT_DIM
    rows = tokens * heads
    query_rows = jnp.concatenate(
        [query_ref[:, head * ATT_DIM : (head + 1) * ATT_DIM] for head in range(heads)], axis=0
    )
    low = jnp.concatenate([low_ref[...]] * heads, axis=0)
    high = jnp.concatenate([high_ref[...]] * heads, axis=0)

    def chunk_turn(turn, carried):
        best_old, total_old, accum_old = carried
        start = pl.multiple_of((chunk_ref[0] + turn) * KEY_CHUNK, KEY_CHUNK)
        piece = kv_ref[pl.ds(start, KEY_CHUNK), :]
        key_part = piece[:, :ATT_DIM]
        value_part = piece[:, ATT_DIM:]
        scores = lax.dot_general(
            query_rows, key_part, (((1,), (1,)), ((), ())), preferred_element_type=jnp.float32
        ) * ATT_DIM ** (-0.5)
        key_pos = start + lax.broadcasted_iota(jnp.int32, (rows, KEY_CHUNK), 1)
        visible = (key_pos >= low) & (key_pos <= high)
        scores = jnp.where(visible, scores, -jnp.inf)
        best_new = jnp.maximum(best_old, jnp.max(scores, axis=1, keepdims=True))
        weights = jnp.exp(scores - best_new)
        rescale = jnp.exp(best_old - best_new)
        total_new = total_old * rescale + jnp.sum(weights, axis=1, keepdims=True)
        accum_new = accum_old * rescale + jnp.dot(
            weights.astype(jnp.bfloat16), value_part, preferred_element_type=jnp.float32
        )
        return (best_new, total_new, accum_new)

    initial = (
        jnp.full((rows, 1), NEG_FILL, jnp.float32),
        jnp.zeros((rows, 1), jnp.float32),
        jnp.zeros((rows, ATT_DIM), jnp.float32),
    )
    _, total, accum = lax.fori_loop(0, chunk_ref[1], chunk_turn, initial)
    result = (accum / total).astype(out_ref.dtype)
    for head in range(heads):
        out_ref[:, head * ATT_DIM : (head + 1) * ATT_DIM] = result[
            head * tokens : (head + 1) * tokens
        ]


def flash_attention(query_rows, kv_rows, low, high, first_chunk, chunk_count):
    tokens = query_rows.shape[0]
    chunk_info = jnp.stack([first_chunk, chunk_count]).astype(jnp.int32)
    grid_spec = pltpu.PrefetchScalarGridSpec(
        num_scalar_prefetch=1,
        grid=(1,),
        in_specs=[
            pl.BlockSpec(query_rows.shape, lambda i, info: (0, 0)),
            pl.BlockSpec(kv_rows.shape, lambda i, info: (0, 0)),
            pl.BlockSpec((tokens, 1), lambda i, info: (0, 0)),
            pl.BlockSpec((tokens, 1), lambda i, info: (0, 0)),
        ],
        out_specs=pl.BlockSpec(query_rows.shape, lambda i, info: (0, 0)),
    )
    return pl.pallas_call(
        attention_kernel,
        grid_spec=grid_spec,
        out_shape=jax.ShapeDtypeStruct(query_rows.shape, jnp.bfloat16),
    )(chunk_info, query_rows, kv_rows, low, high)

def shards(
    mixer_input,
    gate,
    in_b,
    in_c,
    step_size,
    log_decay,
    skip_gain,
    norm_gain,
    query_weight,
    keys,
    values,
    doc_lengths,
):
    highest = lax.Precision.HIGHEST
    tok_rows = mixer_input.shape[0]
    groups_dev = query_weight.shape[0]
    heads_dev = step_size.shape[0]
    head_group = heads_dev // groups_dev
    query_group = QHEADS // GROUPS
    shard_index = lax.axis_index("ctx")
    first_pos = shard_index * tok_rows
    row_index = jnp.arange(tok_rows, dtype=jnp.int32)
    own_pos = first_pos + row_index
    own_docs = segment_ids(own_pos, doc_lengths)
    prev_doc = segment_ids(jnp.reshape(first_pos - 1, (1,)), doc_lengths)[0]
    input_f32 = mixer_input.reshape(tok_rows, groups_dev, head_group, HEAD_DIM).astype(jnp.float32)
    state_in = in_b.reshape(tok_rows, groups_dev, STATE)
    state_out = in_c.reshape(tok_rows, groups_dev, STATE)
    upper_ones = (row_index[:, None] <= row_index[None, :]).astype(jnp.float32)
    cum_decay = jnp.dot(log_decay, upper_ones, precision=highest).reshape(
        groups_dev, head_group, tok_rows
    )
    step_rows = step_size.reshape(groups_dev, head_group, tok_rows)
    last_doc = (own_docs == own_docs[-1]).astype(jnp.float32)
    end_weight = jnp.exp(cum_decay[:, :, -1:] - cum_decay) * last_doc[None, None, :] * step_rows
    weighted = input_f32 * jnp.transpose(end_weight, (2, 0, 1))[..., None]
    local_state = jnp.einsum(
        "sgjp,sgn->gjpn", weighted, state_in.astype(jnp.float32), precision=highest
    )
    carry_mask = (own_docs == prev_doc).astype(jnp.float32)
    ctx_count = lax.axis_size("ctx")
    owned = heads_dev // ctx_count
    block_log = jnp.where(carry_mask[-1] > 0, cum_decay[:, :, -1], -jnp.inf).reshape(heads_dev)
    core = shard_index % 2
    half_heads = heads_dev // 2
    pair_swap = [(source, source ^ 1) for source in range(ctx_count)]
    log_rows = jnp.broadcast_to(block_log[:, None, None], (heads_dev, 8, STATE))
    augmented = jnp.concatenate(
        [local_state.reshape(heads_dev, HEAD_DIM, STATE), log_rows], axis=1
    )
    partner = lax.ppermute(
        lax.dynamic_slice_in_dim(augmented, (1 - core) * half_heads, half_heads, 0),
        "ctx",
        pair_swap,
    )
    mine = lax.dynamic_slice_in_dim(augmented, core * half_heads, half_heads, 0)
    first_core = core == 0
    early_state = jnp.where(first_core, mine[:, :HEAD_DIM], partner[:, :HEAD_DIM])
    late_state = jnp.where(first_core, partner[:, :HEAD_DIM], mine[:, :HEAD_DIM])
    early_log = jnp.where(first_core, mine[:, HEAD_DIM, 0], partner[:, HEAD_DIM, 0])
    late_log = jnp.where(first_core, partner[:, HEAD_DIM, 0], mine[:, HEAD_DIM, 0])
    pair_state = jnp.exp(late_log)[:, None, None] * early_state + late_state
    pair_log = early_log + late_log
    splits = ctx_count // half_heads
    part_rows = HEAD_DIM // splits
    pair_rows = jnp.broadcast_to(
        jnp.repeat(pair_log, splits)[:, None, None], (ctx_count, 8, STATE)
    )
    payload = jnp.concatenate(
        [pair_state.reshape(ctx_count, part_rows, STATE), pair_rows], axis=1
    )
    pair_count = ctx_count // 2
    gathered = lax.all_to_all(payload, "ctx", 0, 0, tiled=True).reshape(
        pair_count, 2, part_rows + 8, STATE
    )
    states_mine = gathered[:, :, :part_rows, :]
    mine_log = gathered[:, :, part_rows, 0]
    block_row = jnp.arange(pair_count, dtype=jnp.int32)
    between = (block_row[None, :, None] < block_row[None, None, :]) & (
        block_row[None, None, :] < block_row[:, None, None]
    )
    log_span = jnp.sum(
        jnp.where(between[None], jnp.transpose(mine_log)[:, None, None, :], 0.0), axis=-1
    )
    earlier = block_row[:, None] > block_row[None, :]
    transfer = jnp.where(earlier[None], jnp.exp(log_span), 0.0)
    incoming_mine = jnp.einsum("ukd,dupn->kupn", transfer, states_mine, precision=highest)
    pair_incoming = lax.all_to_all(
        incoming_mine.reshape(ctx_count, part_rows, STATE), "ctx", 0, 0, tiled=True
    ).reshape(half_heads, HEAD_DIM, STATE)
    after_early = jnp.exp(early_log)[:, None, None] * pair_incoming + early_state
    swapped = lax.ppermute(
        jnp.where(first_core, after_early, pair_incoming), "ctx", pair_swap
    )
    kept = jnp.where(first_core, pair_incoming, after_early)
    incoming = jnp.where(
        first_core,
        jnp.concatenate([kept, swapped], axis=0),
        jnp.concatenate([swapped, kept], axis=0),
    ).reshape(groups_dev, head_group, HEAD_DIM, STATE)
    kv_local = jnp.concatenate(
        [
            keys.reshape(tok_rows, groups_dev, ATT_DIM),
            values.reshape(tok_rows, groups_dev, ATT_DIM),
        ],
        axis=2,
    )
    kv_local, incoming = lax.optimization_barrier((kv_local, incoming))
    same_doc = (own_docs[:, None] == own_docs[None, :]) & (row_index[:, None] >= row_index[None, :])
    log_gap = cum_decay[:, :, :, None] - cum_decay[:, :, None, :]
    decay_matrix = jnp.exp(jnp.where(same_doc[None, None], log_gap, -jnp.inf))
    pair_products = jnp.einsum(
        "tgn,sgn->gts", state_out, state_in, preferred_element_type=jnp.float32
    )
    mixing = pair_products[:, None] * decay_matrix * step_rows[:, :, None, :]
    local_out = jnp.einsum("gjts,sgjp->tgjp", mixing, input_f32, precision=highest)
    carry_weight = jnp.exp(cum_decay) * carry_mask[None, None, :]
    carried_out = (
        jnp.einsum("tgn,gjpn->tgjp", state_out.astype(jnp.float32), incoming, precision=highest)
        * jnp.transpose(carry_weight, (2, 0, 1))[..., None]
    )
    skip_rows = skip_gain.reshape(groups_dev, head_group)[None, :, :, None] * input_f32
    mixer_full = (local_out + carried_out + skip_rows).reshape(tok_rows, -1)
    gated = mixer_full * jax.nn.silu(gate.astype(jnp.float32))
    square_local = jnp.sum(gated * gated, axis=1)
    square_sum = lax.psum(square_local, "head")
    mixer_out = (
        gated
        * lax.rsqrt(square_sum / (MIXER_HEADS * HEAD_DIM) + EPSILON)[:, None]
        * norm_gain[None, :]
    ).astype(jnp.bfloat16)
    query = jnp.einsum(
        "tgf,gfo->tgo",
        mixer_out.reshape(tok_rows, groups_dev, -1),
        query_weight,
        preferred_element_type=jnp.float32,
    )
    query = query.astype(jnp.bfloat16).reshape(tok_rows, groups_dev, query_group, ATT_DIM)

    kv_all = lax.all_gather(kv_local, "ctx", axis=0, tiled=True)
    doc_starts = jnp.cumsum(doc_lengths) - doc_lengths
    row_low = jnp.max(
        jnp.where(doc_starts[None, :] <= own_pos[:, None], doc_starts[None, :], 0), axis=1
    )
    first_chunk = row_low[0] // KEY_CHUNK
    last_chunk = (first_pos + tok_rows - 1) // KEY_CHUNK
    group_outs = []
    for group in range(groups_dev):
        group_outs.append(
            flash_attention(
                query[:, group].reshape(tok_rows, query_group * ATT_DIM),
                kv_all[:, group],
                row_low[:, None],
                own_pos[:, None],
                first_chunk,
                last_chunk - first_chunk + 1,
            )
        )
    attn_out = jnp.concatenate(group_outs, axis=1)
    return (mixer_out, attn_out)


def solution(mesh):
    return jax.shard_map(
        shards,
        mesh=mesh,
        in_specs=(
            P("ctx", "head"),
            P("ctx", "head"),
            P("ctx", "head"),
            P("ctx", "head"),
            P("head", "ctx"),
            P("head", "ctx"),
            P("head"),
            P("head"),
            P("head", None, None),
            P("ctx", "head"),
            P("ctx", "head"),
            P(),
        ),
        out_specs=(P("ctx", "head"), P("ctx", "head")),
        check_vma=False,
    )
```

```python
import jax
import jax.numpy as jnp
from jax import lax
from jax.sharding import PartitionSpec as P
from jax.experimental import pallas as pl
from jax.experimental.pallas import tpu as pltpu

MIXER_HEADS = 256
HEAD_DIM = 64
STATE = 256
GROUPS = 8
QHEADS = 64
ATT_DIM = 128


EPSILON = 1e-05
NEG_FILL = -1e30
KEY_CHUNK = 256


def segment_ids(positions, doc_lengths):
    doc_starts = jnp.cumsum(doc_lengths) - doc_lengths
    hits = (doc_starts[None, :] <= positions[:, None]).astype(jnp.int32)
    return jnp.sum(hits, axis=1) - 1


def attention_kernel(chunk_ref, query_ref, kv_ref, low_ref, high_ref, out_ref):
    tokens = query_ref.shape[0]
    heads = query_ref.shape[1] // ATT_DIM
    rows = tokens * heads
    query_rows = jnp.concatenate(
        [query_ref[:, head * ATT_DIM : (head + 1) * ATT_DIM] for head in range(heads)], axis=0
    )
    low = jnp.concatenate([low_ref[...]] * heads, axis=0)
    high = jnp.concatenate([high_ref[...]] * heads, axis=0)

    def make_turn(base, masked):
        def chunk_turn(turn, carried):
            best_old, total_old, accum_old = carried
            start = pl.multiple_of((base + turn) * KEY_CHUNK, KEY_CHUNK)
            piece = kv_ref[pl.ds(start, KEY_CHUNK), :]
            key_part = piece[:, :ATT_DIM]
            value_part = piece[:, ATT_DIM:]
            scores = lax.dot_general(
                query_rows, key_part, (((1,), (1,)), ((), ())), preferred_element_type=jnp.float32
            ) * ATT_DIM ** (-0.5)
            if masked:
                key_pos = start + lax.broadcasted_iota(jnp.int32, (rows, KEY_CHUNK), 1)
                visible = (key_pos >= low) & (key_pos <= high)
                scores = jnp.where(visible, scores, -jnp.inf)
            best_new = jnp.maximum(best_old, jnp.max(scores, axis=1, keepdims=True))
            weights = jnp.exp(scores - best_new)
            rescale = jnp.exp(best_old - best_new)
            total_new = total_old * rescale + jnp.sum(weights, axis=1, keepdims=True)
            accum_new = accum_old * rescale + jnp.dot(
                weights.astype(jnp.bfloat16), value_part, preferred_element_type=jnp.float32
            )
            return (best_new, total_new, accum_new)

        return chunk_turn

    carried = (
        jnp.full((rows, 1), NEG_FILL, jnp.float32),
        jnp.zeros((rows, 1), jnp.float32),
        jnp.zeros((rows, ATT_DIM), jnp.float32),
    )
    carried = lax.fori_loop(0, chunk_ref[1], make_turn(chunk_ref[0], True), carried)
    carried = lax.fori_loop(0, chunk_ref[3], make_turn(chunk_ref[2], False), carried)
    carried = lax.fori_loop(0, chunk_ref[5], make_turn(chunk_ref[4], True), carried)
    _, total, accum = carried
    result = (accum / total).astype(out_ref.dtype)
    for head in range(heads):
        out_ref[:, head * ATT_DIM : (head + 1) * ATT_DIM] = result[
            head * tokens : (head + 1) * tokens
        ]


def flash_attention(query_rows, kv_rows, low, high, first_chunk, chunk_count):
    tokens = query_rows.shape[0]
    last_chunk = first_chunk + chunk_count - 1
    inner_first = jnp.maximum(first_chunk, -(-jnp.max(low) // KEY_CHUNK))
    inner_last = jnp.minimum(last_chunk, (jnp.min(high) + 1) // KEY_CHUNK - 1)
    inner_count = jnp.maximum(inner_last - inner_first + 1, 0)
    has_inner = inner_count > 0
    front_count = jnp.where(has_inner, inner_first - first_chunk, chunk_count)
    back_first = jnp.where(has_inner, inner_last + 1, last_chunk + 1)
    back_count = last_chunk - back_first + 1
    chunk_info = jnp.stack(
        [first_chunk, front_count, inner_first, inner_count, back_first, back_count]
    ).astype(jnp.int32)
    grid_spec = pltpu.PrefetchScalarGridSpec(
        num_scalar_prefetch=1,
        grid=(1,),
        in_specs=[
            pl.BlockSpec(query_rows.shape, lambda i, info: (0, 0)),
            pl.BlockSpec(kv_rows.shape, lambda i, info: (0, 0)),
            pl.BlockSpec((tokens, 1), lambda i, info: (0, 0)),
            pl.BlockSpec((tokens, 1), lambda i, info: (0, 0)),
        ],
        out_specs=pl.BlockSpec(query_rows.shape, lambda i, info: (0, 0)),
    )
    return pl.pallas_call(
        attention_kernel,
        grid_spec=grid_spec,
        out_shape=jax.ShapeDtypeStruct(query_rows.shape, jnp.bfloat16),
    )(chunk_info, query_rows, kv_rows, low, high)

def shards(
    mixer_input,
    gate,
    in_b,
    in_c,
    step_size,
    log_decay,
    skip_gain,
    norm_gain,
    query_weight,
    keys,
    values,
    doc_lengths,
):
    highest = lax.Precision.HIGHEST
    tok_rows = mixer_input.shape[0]
    groups_dev = query_weight.shape[0]
    heads_dev = step_size.shape[0]
    head_group = heads_dev // groups_dev
    query_group = QHEADS // GROUPS
    shard_index = lax.axis_index("ctx")
    first_pos = shard_index * tok_rows
    row_index = jnp.arange(tok_rows, dtype=jnp.int32)
    own_pos = first_pos + row_index
    own_docs = segment_ids(own_pos, doc_lengths)
    prev_doc = segment_ids(jnp.reshape(first_pos - 1, (1,)), doc_lengths)[0]
    input_f32 = mixer_input.reshape(tok_rows, groups_dev, head_group, HEAD_DIM).astype(jnp.float32)
    state_in = in_b.reshape(tok_rows, groups_dev, STATE)
    state_out = in_c.reshape(tok_rows, groups_dev, STATE)
    upper_ones = (row_index[:, None] <= row_index[None, :]).astype(jnp.float32)
    cum_decay = jnp.dot(log_decay, upper_ones, precision=highest).reshape(
        groups_dev, head_group, tok_rows
    )
    step_rows = step_size.reshape(groups_dev, head_group, tok_rows)
    last_doc = (own_docs == own_docs[-1]).astype(jnp.float32)
    end_weight = jnp.exp(cum_decay[:, :, -1:] - cum_decay) * last_doc[None, None, :] * step_rows
    weighted = input_f32 * jnp.transpose(end_weight, (2, 0, 1))[..., None]
    local_state = jnp.einsum(
        "sgjp,sgn->gjpn", weighted, state_in.astype(jnp.float32), precision=highest
    )
    carry_mask = (own_docs == prev_doc).astype(jnp.float32)
    ctx_count = lax.axis_size("ctx")
    owned = heads_dev // ctx_count
    block_log = jnp.where(carry_mask[-1] > 0, cum_decay[:, :, -1], -jnp.inf).reshape(heads_dev)
    core = shard_index % 2
    half_heads = heads_dev // 2
    pair_swap = [(source, source ^ 1) for source in range(ctx_count)]
    log_rows = jnp.broadcast_to(block_log[:, None, None], (heads_dev, 8, STATE))
    augmented = jnp.concatenate(
        [local_state.reshape(heads_dev, HEAD_DIM, STATE), log_rows], axis=1
    )
    partner = lax.ppermute(
        lax.dynamic_slice_in_dim(augmented, (1 - core) * half_heads, half_heads, 0),
        "ctx",
        pair_swap,
    )
    mine = lax.dynamic_slice_in_dim(augmented, core * half_heads, half_heads, 0)
    first_core = core == 0
    early_state = jnp.where(first_core, mine[:, :HEAD_DIM], partner[:, :HEAD_DIM])
    late_state = jnp.where(first_core, partner[:, :HEAD_DIM], mine[:, :HEAD_DIM])
    early_log = jnp.where(first_core, mine[:, HEAD_DIM, 0], partner[:, HEAD_DIM, 0])
    late_log = jnp.where(first_core, partner[:, HEAD_DIM, 0], mine[:, HEAD_DIM, 0])
    pair_state = jnp.exp(late_log)[:, None, None] * early_state + late_state
    pair_log = early_log + late_log
    splits = ctx_count // half_heads
    part_rows = HEAD_DIM // splits
    pair_rows = jnp.broadcast_to(
        jnp.repeat(pair_log, splits)[:, None, None], (ctx_count, 8, STATE)
    )
    payload = jnp.concatenate(
        [pair_state.reshape(ctx_count, part_rows, STATE), pair_rows], axis=1
    )
    pair_count = ctx_count // 2
    gathered = lax.all_to_all(payload, "ctx", 0, 0, tiled=True).reshape(
        pair_count, 2, part_rows + 8, STATE
    )
    states_mine = gathered[:, :, :part_rows, :]
    mine_log = gathered[:, :, part_rows, 0]
    block_row = jnp.arange(pair_count, dtype=jnp.int32)
    between = (block_row[None, :, None] < block_row[None, None, :]) & (
        block_row[None, None, :] < block_row[:, None, None]
    )
    log_span = jnp.sum(
        jnp.where(between[None], jnp.transpose(mine_log)[:, None, None, :], 0.0), axis=-1
    )
    earlier = block_row[:, None] > block_row[None, :]
    transfer = jnp.where(earlier[None], jnp.exp(log_span), 0.0)
    incoming_mine = jnp.einsum("ukd,dupn->kupn", transfer, states_mine, precision=highest)
    pair_incoming = lax.all_to_all(
        incoming_mine.reshape(ctx_count, part_rows, STATE), "ctx", 0, 0, tiled=True
    ).reshape(half_heads, HEAD_DIM, STATE)
    after_early = jnp.exp(early_log)[:, None, None] * pair_incoming + early_state
    swapped = lax.ppermute(
        jnp.where(first_core, after_early, pair_incoming), "ctx", pair_swap
    )
    kept = jnp.where(first_core, pair_incoming, after_early)
    incoming = jnp.where(
        first_core,
        jnp.concatenate([kept, swapped], axis=0),
        jnp.concatenate([swapped, kept], axis=0),
    ).reshape(groups_dev, head_group, HEAD_DIM, STATE)
    same_doc = (own_docs[:, None] == own_docs[None, :]) & (row_index[:, None] >= row_index[None, :])
    log_gap = cum_decay[:, :, :, None] - cum_decay[:, :, None, :]
    decay_matrix = jnp.exp(jnp.where(same_doc[None, None], log_gap, -jnp.inf))
    pair_products = jnp.einsum(
        "tgn,sgn->gts", state_out, state_in, preferred_element_type=jnp.float32
    )
    mixing = pair_products[:, None] * decay_matrix * step_rows[:, :, None, :]
    local_out = jnp.einsum("gjts,sgjp->tgjp", mixing, input_f32, precision=highest)
    carry_weight = jnp.exp(cum_decay) * carry_mask[None, None, :]
    carried_out = (
        jnp.einsum("tgn,gjpn->tgjp", state_out.astype(jnp.float32), incoming, precision=highest)
        * jnp.transpose(carry_weight, (2, 0, 1))[..., None]
    )
    skip_rows = skip_gain.reshape(groups_dev, head_group)[None, :, :, None] * input_f32
    mixer_full = (local_out + carried_out + skip_rows).reshape(tok_rows, -1)
    gated = mixer_full * jax.nn.silu(gate.astype(jnp.float32))
    square_local = jnp.sum(gated * gated, axis=1)
    square_sum = lax.psum(square_local, "head")
    mixer_out = (
        gated
        * lax.rsqrt(square_sum / (MIXER_HEADS * HEAD_DIM) + EPSILON)[:, None]
        * norm_gain[None, :]
    ).astype(jnp.bfloat16)
    query = jnp.einsum(
        "tgf,gfo->tgo",
        mixer_out.reshape(tok_rows, groups_dev, -1),
        query_weight,
        preferred_element_type=jnp.float32,
    )
    query = query.astype(jnp.bfloat16).reshape(tok_rows, groups_dev, query_group, ATT_DIM)

    kv_local = jnp.concatenate(
        [
            keys.reshape(tok_rows, groups_dev, ATT_DIM),
            values.reshape(tok_rows, groups_dev, ATT_DIM),
        ],
        axis=2,
    )
    kv_all = lax.all_gather(kv_local, "ctx", axis=0, tiled=True)
    doc_starts = jnp.cumsum(doc_lengths) - doc_lengths
    row_low = jnp.max(
        jnp.where(doc_starts[None, :] <= own_pos[:, None], doc_starts[None, :], 0), axis=1
    )
    first_chunk = row_low[0] // KEY_CHUNK
    last_chunk = (first_pos + tok_rows - 1) // KEY_CHUNK
    group_outs = []
    for group in range(groups_dev):
        group_outs.append(
            flash_attention(
                query[:, group].reshape(tok_rows, query_group * ATT_DIM),
                kv_all[:, group],
                row_low[:, None],
                own_pos[:, None],
                first_chunk,
                last_chunk - first_chunk + 1,
            )
        )
    attn_out = jnp.concatenate(group_outs, axis=1)
    return (mixer_out, attn_out)


def solution(mesh):
    return jax.shard_map(
        shards,
        mesh=mesh,
        in_specs=(
            P("ctx", "head"),
            P("ctx", "head"),
            P("ctx", "head"),
            P("ctx", "head"),
            P("head", "ctx"),
            P("head", "ctx"),
            P("head"),
            P("head"),
            P("head", None, None),
            P("ctx", "head"),
            P("ctx", "head"),
            P(),
        ),
        out_specs=(P("ctx", "head"), P("ctx", "head")),
        check_vma=False,
    )
```

```python
import jax
import jax.numpy as jnp
from jax import lax
from jax.sharding import PartitionSpec as P
from jax.experimental import pallas as pl
from jax.experimental.pallas import tpu as pltpu

MIXER_HEADS = 256
HEAD_DIM = 64
STATE = 256
GROUPS = 8
QHEADS = 64
ATT_DIM = 128


EPSILON = 1e-05
NEG_FILL = -1e30
KEY_CHUNK = 256


def segment_ids(positions, doc_lengths):
    doc_starts = jnp.cumsum(doc_lengths) - doc_lengths
    hits = (doc_starts[None, :] <= positions[:, None]).astype(jnp.int32)
    return jnp.sum(hits, axis=1) - 1


def attention_kernel(chunk_ref, query_ref, kv_ref, low_ref, high_ref, out_ref):
    tokens = query_ref.shape[0]
    heads = query_ref.shape[1] // ATT_DIM
    rows = tokens * heads
    query_rows = jnp.concatenate(
        [query_ref[:, head * ATT_DIM : (head + 1) * ATT_DIM] for head in range(heads)], axis=0
    )
    low = jnp.concatenate([low_ref[...]] * heads, axis=0)
    high = jnp.concatenate([high_ref[...]] * heads, axis=0)

    def chunk_turn(turn, carried):
        best_old, total_old, accum_old = carried
        start = pl.multiple_of((chunk_ref[0] + turn) * KEY_CHUNK, KEY_CHUNK)
        piece = kv_ref[pl.ds(start, KEY_CHUNK), :]
        key_part = piece[:, :ATT_DIM]
        value_part = piece[:, ATT_DIM:]
        scores = lax.dot_general(
            query_rows, key_part, (((1,), (1,)), ((), ())), preferred_element_type=jnp.float32
        ) * ATT_DIM ** (-0.5)
        key_pos = start + lax.broadcasted_iota(jnp.int32, (rows, KEY_CHUNK), 1)
        visible = (key_pos >= low) & (key_pos <= high)
        scores = jnp.where(visible, scores, -jnp.inf)
        best_new = jnp.maximum(best_old, jnp.max(scores, axis=1, keepdims=True))
        weights = jnp.exp(scores - best_new)
        rescale = jnp.exp(best_old - best_new)
        total_new = total_old * rescale + jnp.sum(weights, axis=1, keepdims=True)
        accum_new = accum_old * rescale + jnp.dot(
            weights.astype(jnp.bfloat16), value_part, preferred_element_type=jnp.float32
        )
        return (best_new, total_new, accum_new)

    initial = (
        jnp.full((rows, 1), NEG_FILL, jnp.float32),
        jnp.zeros((rows, 1), jnp.float32),
        jnp.zeros((rows, ATT_DIM), jnp.float32),
    )
    _, total, accum = lax.fori_loop(0, chunk_ref[1], chunk_turn, initial)
    result = (accum / total).astype(out_ref.dtype)
    for head in range(heads):
        out_ref[:, head * ATT_DIM : (head + 1) * ATT_DIM] = result[
            head * tokens : (head + 1) * tokens
        ]


def flash_attention(query_rows, kv_rows, low, high, first_chunk, chunk_count):
    tokens = query_rows.shape[0]
    chunk_info = jnp.stack([first_chunk, chunk_count]).astype(jnp.int32)
    grid_spec = pltpu.PrefetchScalarGridSpec(
        num_scalar_prefetch=1,
        grid=(1,),
        in_specs=[
            pl.BlockSpec(query_rows.shape, lambda i, info: (0, 0)),
            pl.BlockSpec(kv_rows.shape, lambda i, info: (0, 0)),
            pl.BlockSpec((tokens, 1), lambda i, info: (0, 0)),
            pl.BlockSpec((tokens, 1), lambda i, info: (0, 0)),
        ],
        out_specs=pl.BlockSpec(query_rows.shape, lambda i, info: (0, 0)),
    )
    return pl.pallas_call(
        attention_kernel,
        grid_spec=grid_spec,
        out_shape=jax.ShapeDtypeStruct(query_rows.shape, jnp.bfloat16),
    )(chunk_info, query_rows, kv_rows, low, high)

def shards(
    mixer_input,
    gate,
    in_b,
    in_c,
    step_size,
    log_decay,
    skip_gain,
    norm_gain,
    query_weight,
    keys,
    values,
    doc_lengths,
):
    highest = lax.Precision.HIGHEST
    tok_rows = mixer_input.shape[0]
    groups_dev = query_weight.shape[0]
    heads_dev = step_size.shape[0]
    head_group = heads_dev // groups_dev
    query_group = QHEADS // GROUPS
    shard_index = lax.axis_index("ctx")
    first_pos = shard_index * tok_rows
    row_index = jnp.arange(tok_rows, dtype=jnp.int32)
    own_pos = first_pos + row_index
    own_docs = segment_ids(own_pos, doc_lengths)
    prev_doc = segment_ids(jnp.reshape(first_pos - 1, (1,)), doc_lengths)[0]
    input_f32 = mixer_input.reshape(tok_rows, groups_dev, head_group, HEAD_DIM).astype(jnp.float32)
    state_in = in_b.reshape(tok_rows, groups_dev, STATE)
    state_out = in_c.reshape(tok_rows, groups_dev, STATE)
    upper_ones = (row_index[:, None] <= row_index[None, :]).astype(jnp.float32)
    cum_decay = jnp.dot(log_decay, upper_ones, precision=highest).reshape(
        groups_dev, head_group, tok_rows
    )
    step_rows = step_size.reshape(groups_dev, head_group, tok_rows)
    last_doc = (own_docs == own_docs[-1]).astype(jnp.float32)
    end_weight = jnp.exp(cum_decay[:, :, -1:] - cum_decay) * last_doc[None, None, :] * step_rows
    weighted = input_f32 * jnp.transpose(end_weight, (2, 0, 1))[..., None]
    local_state = jnp.einsum(
        "sgjp,sgn->gjpn", weighted, state_in.astype(jnp.float32), precision=highest
    )
    carry_mask = (own_docs == prev_doc).astype(jnp.float32)
    ctx_count = lax.axis_size("ctx")
    owned = heads_dev // ctx_count
    block_log = jnp.where(carry_mask[-1] > 0, cum_decay[:, :, -1], -jnp.inf).reshape(heads_dev)
    core = shard_index % 2
    half_heads = heads_dev // 2
    pair_swap = [(source, source ^ 1) for source in range(ctx_count)]
    log_rows = jnp.broadcast_to(block_log[:, None, None], (heads_dev, 8, STATE))
    augmented = jnp.concatenate(
        [local_state.reshape(heads_dev, HEAD_DIM, STATE), log_rows], axis=1
    )
    partner = lax.ppermute(
        lax.dynamic_slice_in_dim(augmented, (1 - core) * half_heads, half_heads, 0),
        "ctx",
        pair_swap,
    )
    mine = lax.dynamic_slice_in_dim(augmented, core * half_heads, half_heads, 0)
    first_core = core == 0
    early_state = jnp.where(first_core, mine[:, :HEAD_DIM], partner[:, :HEAD_DIM])
    late_state = jnp.where(first_core, partner[:, :HEAD_DIM], mine[:, :HEAD_DIM])
    early_log = jnp.where(first_core, mine[:, HEAD_DIM, 0], partner[:, HEAD_DIM, 0])
    late_log = jnp.where(first_core, partner[:, HEAD_DIM, 0], mine[:, HEAD_DIM, 0])
    pair_state = jnp.exp(late_log)[:, None, None] * early_state + late_state
    pair_log = early_log + late_log
    splits = ctx_count // half_heads
    part_rows = HEAD_DIM // splits
    pair_rows = jnp.broadcast_to(
        jnp.repeat(pair_log, splits)[:, None, None], (ctx_count, 8, STATE)
    )
    payload = jnp.concatenate(
        [pair_state.reshape(ctx_count, part_rows, STATE), pair_rows], axis=1
    )
    pair_count = ctx_count // 2
    gathered = lax.all_to_all(payload, "ctx", 0, 0, tiled=True).reshape(
        pair_count, 2, part_rows + 8, STATE
    )
    same_doc = (own_docs[:, None] == own_docs[None, :]) & (row_index[:, None] >= row_index[None, :])
    log_gap = cum_decay[:, :, :, None] - cum_decay[:, :, None, :]
    decay_matrix = jnp.exp(jnp.where(same_doc[None, None], log_gap, -jnp.inf))
    pair_products = jnp.einsum(
        "tgn,sgn->gts", state_out, state_in, preferred_element_type=jnp.float32
    )
    mixing = pair_products[:, None] * decay_matrix * step_rows[:, :, None, :]
    local_out = jnp.einsum("gjts,sgjp->tgjp", mixing, input_f32, precision=highest)
    gathered, local_out = lax.optimization_barrier((gathered, local_out))
    states_mine = gathered[:, :, :part_rows, :]
    mine_log = gathered[:, :, part_rows, 0]
    block_row = jnp.arange(pair_count, dtype=jnp.int32)
    between = (block_row[None, :, None] < block_row[None, None, :]) & (
        block_row[None, None, :] < block_row[:, None, None]
    )
    log_span = jnp.sum(
        jnp.where(between[None], jnp.transpose(mine_log)[:, None, None, :], 0.0), axis=-1
    )
    earlier = block_row[:, None] > block_row[None, :]
    transfer = jnp.where(earlier[None], jnp.exp(log_span), 0.0)
    incoming_mine = jnp.einsum("ukd,dupn->kupn", transfer, states_mine, precision=highest)
    pair_incoming = lax.all_to_all(
        incoming_mine.reshape(ctx_count, part_rows, STATE), "ctx", 0, 0, tiled=True
    ).reshape(half_heads, HEAD_DIM, STATE)
    after_early = jnp.exp(early_log)[:, None, None] * pair_incoming + early_state
    swapped = lax.ppermute(
        jnp.where(first_core, after_early, pair_incoming), "ctx", pair_swap
    )
    kept = jnp.where(first_core, pair_incoming, after_early)
    incoming = jnp.where(
        first_core,
        jnp.concatenate([kept, swapped], axis=0),
        jnp.concatenate([swapped, kept], axis=0),
    ).reshape(groups_dev, head_group, HEAD_DIM, STATE)
    carry_weight = jnp.exp(cum_decay) * carry_mask[None, None, :]
    carried_out = (
        jnp.einsum("tgn,gjpn->tgjp", state_out.astype(jnp.float32), incoming, precision=highest)
        * jnp.transpose(carry_weight, (2, 0, 1))[..., None]
    )
    skip_rows = skip_gain.reshape(groups_dev, head_group)[None, :, :, None] * input_f32
    mixer_full = (local_out + carried_out + skip_rows).reshape(tok_rows, -1)
    gated = mixer_full * jax.nn.silu(gate.astype(jnp.float32))
    square_local = jnp.sum(gated * gated, axis=1)
    square_sum = lax.psum(square_local, "head")
    mixer_out = (
        gated
        * lax.rsqrt(square_sum / (MIXER_HEADS * HEAD_DIM) + EPSILON)[:, None]
        * norm_gain[None, :]
    ).astype(jnp.bfloat16)
    query = jnp.einsum(
        "tgf,gfo->tgo",
        mixer_out.reshape(tok_rows, groups_dev, -1),
        query_weight,
        preferred_element_type=jnp.float32,
    )
    query = query.astype(jnp.bfloat16).reshape(tok_rows, groups_dev, query_group, ATT_DIM)

    kv_local = jnp.concatenate(
        [
            keys.reshape(tok_rows, groups_dev, ATT_DIM),
            values.reshape(tok_rows, groups_dev, ATT_DIM),
        ],
        axis=2,
    )
    kv_all = lax.all_gather(kv_local, "ctx", axis=0, tiled=True)
    doc_starts = jnp.cumsum(doc_lengths) - doc_lengths
    row_low = jnp.max(
        jnp.where(doc_starts[None, :] <= own_pos[:, None], doc_starts[None, :], 0), axis=1
    )
    first_chunk = row_low[0] // KEY_CHUNK
    last_chunk = (first_pos + tok_rows - 1) // KEY_CHUNK
    group_outs = []
    for group in range(groups_dev):
        group_outs.append(
            flash_attention(
                query[:, group].reshape(tok_rows, query_group * ATT_DIM),
                kv_all[:, group],
                row_low[:, None],
                own_pos[:, None],
                first_chunk,
                last_chunk - first_chunk + 1,
            )
        )
    attn_out = jnp.concatenate(group_outs, axis=1)
    return (mixer_out, attn_out)


def solution(mesh):
    return jax.shard_map(
        shards,
        mesh=mesh,
        in_specs=(
            P("ctx", "head"),
            P("ctx", "head"),
            P("ctx", "head"),
            P("ctx", "head"),
            P("head", "ctx"),
            P("head", "ctx"),
            P("head"),
            P("head"),
            P("head", None, None),
            P("ctx", "head"),
            P("ctx", "head"),
            P(),
        ),
        out_specs=(P("ctx", "head"), P("ctx", "head")),
        check_vma=False,
    )
```

```python
import jax
import jax.numpy as jnp
from jax import lax
from jax.sharding import PartitionSpec as P
from jax.experimental import pallas as pl
from jax.experimental.pallas import tpu as pltpu

MIXER_HEADS = 256
HEAD_DIM = 64
STATE = 256
GROUPS = 8
QHEADS = 64
ATT_DIM = 128


EPSILON = 1e-05
NEG_FILL = -1e30
KEY_CHUNK = 256


def segment_ids(positions, doc_lengths):
    doc_starts = jnp.cumsum(doc_lengths) - doc_lengths
    hits = (doc_starts[None, :] <= positions[:, None]).astype(jnp.int32)
    return jnp.sum(hits, axis=1) - 1


def attention_kernel(chunk_ref, query_ref, kv_ref, low_ref, high_ref, out_ref):
    tokens = query_ref.shape[0]
    heads = query_ref.shape[1] // ATT_DIM
    rows = tokens * heads
    query_rows = jnp.concatenate(
        [query_ref[:, head * ATT_DIM : (head + 1) * ATT_DIM] for head in range(heads)], axis=0
    )
    low = jnp.concatenate([low_ref[...]] * heads, axis=0)
    high = jnp.concatenate([high_ref[...]] * heads, axis=0)

    def chunk_turn(turn, carried):
        best_old, total_old, accum_old = carried
        start = pl.multiple_of((chunk_ref[0] + turn) * KEY_CHUNK, KEY_CHUNK)
        piece = kv_ref[pl.ds(start, KEY_CHUNK), :]
        key_part = piece[:, :ATT_DIM]
        value_part = piece[:, ATT_DIM:]
        scores = lax.dot_general(
            query_rows, key_part, (((1,), (1,)), ((), ())), preferred_element_type=jnp.float32
        ) * ATT_DIM ** (-0.5)
        key_pos = start + lax.broadcasted_iota(jnp.int32, (rows, KEY_CHUNK), 1)
        visible = (key_pos >= low) & (key_pos <= high)
        scores = jnp.where(visible, scores, -jnp.inf)
        best_new = jnp.maximum(best_old, jnp.max(scores, axis=1, keepdims=True))
        weights = jnp.exp(scores - best_new)
        rescale = jnp.exp(best_old - best_new)
        total_new = total_old * rescale + jnp.sum(weights, axis=1, keepdims=True)
        accum_new = accum_old * rescale + jnp.dot(
            weights.astype(jnp.bfloat16), value_part, preferred_element_type=jnp.float32
        )
        return (best_new, total_new, accum_new)

    initial = (
        jnp.full((rows, 1), NEG_FILL, jnp.float32),
        jnp.zeros((rows, 1), jnp.float32),
        jnp.zeros((rows, ATT_DIM), jnp.float32),
    )
    _, total, accum = lax.fori_loop(0, chunk_ref[1], chunk_turn, initial)
    result = (accum / total).astype(out_ref.dtype)
    for head in range(heads):
        out_ref[:, head * ATT_DIM : (head + 1) * ATT_DIM] = result[
            head * tokens : (head + 1) * tokens
        ]


def flash_attention(query_rows, kv_rows, low, high, first_chunk, chunk_count):
    tokens = query_rows.shape[0]
    chunk_info = jnp.stack([first_chunk, chunk_count]).astype(jnp.int32)
    grid_spec = pltpu.PrefetchScalarGridSpec(
        num_scalar_prefetch=1,
        grid=(1,),
        in_specs=[
            pl.BlockSpec(query_rows.shape, lambda i, info: (0, 0)),
            pl.BlockSpec(kv_rows.shape, lambda i, info: (0, 0)),
            pl.BlockSpec((tokens, 1), lambda i, info: (0, 0)),
            pl.BlockSpec((tokens, 1), lambda i, info: (0, 0)),
        ],
        out_specs=pl.BlockSpec(query_rows.shape, lambda i, info: (0, 0)),
    )
    return pl.pallas_call(
        attention_kernel,
        grid_spec=grid_spec,
        out_shape=jax.ShapeDtypeStruct(query_rows.shape, jnp.bfloat16),
    )(chunk_info, query_rows, kv_rows, low, high)

def shards(
    mixer_input,
    gate,
    in_b,
    in_c,
    step_size,
    log_decay,
    skip_gain,
    norm_gain,
    query_weight,
    keys,
    values,
    doc_lengths,
):
    highest = lax.Precision.HIGHEST
    tok_rows = mixer_input.shape[0]
    groups_dev = query_weight.shape[0]
    heads_dev = step_size.shape[0]
    head_group = heads_dev // groups_dev
    query_group = QHEADS // GROUPS
    shard_index = lax.axis_index("ctx")
    first_pos = shard_index * tok_rows
    row_index = jnp.arange(tok_rows, dtype=jnp.int32)
    own_pos = first_pos + row_index
    own_docs = segment_ids(own_pos, doc_lengths)
    prev_doc = segment_ids(jnp.reshape(first_pos - 1, (1,)), doc_lengths)[0]
    input_f32 = mixer_input.reshape(tok_rows, groups_dev, head_group, HEAD_DIM).astype(jnp.float32)
    state_in = in_b.reshape(tok_rows, groups_dev, STATE)
    state_out = in_c.reshape(tok_rows, groups_dev, STATE)
    upper_ones = (row_index[:, None] <= row_index[None, :]).astype(jnp.float32)
    cum_decay = jnp.dot(log_decay, upper_ones, precision=highest).reshape(
        groups_dev, head_group, tok_rows
    )
    step_rows = step_size.reshape(groups_dev, head_group, tok_rows)
    last_doc = (own_docs == own_docs[-1]).astype(jnp.float32)
    end_weight = jnp.exp(cum_decay[:, :, -1:] - cum_decay) * last_doc[None, None, :] * step_rows
    weighted = input_f32 * jnp.transpose(end_weight, (2, 0, 1))[..., None]
    local_state = jnp.einsum(
        "sgjp,sgn->gjpn", weighted, state_in.astype(jnp.float32), precision=highest
    )
    carry_mask = (own_docs == prev_doc).astype(jnp.float32)
    ctx_count = lax.axis_size("ctx")
    owned = heads_dev // ctx_count
    block_log = jnp.where(carry_mask[-1] > 0, cum_decay[:, :, -1], -jnp.inf).reshape(heads_dev)
    core = shard_index % 2
    half_heads = heads_dev // 2
    pair_swap = [(source, source ^ 1) for source in range(ctx_count)]
    log_rows = jnp.broadcast_to(block_log[:, None, None], (heads_dev, 8, STATE))
    augmented = jnp.concatenate(
        [local_state.reshape(heads_dev, HEAD_DIM, STATE), log_rows], axis=1
    )
    partner = lax.ppermute(
        lax.dynamic_slice_in_dim(augmented, (1 - core) * half_heads, half_heads, 0),
        "ctx",
        pair_swap,
    )
    mine = lax.dynamic_slice_in_dim(augmented, core * half_heads, half_heads, 0)
    first_core = core == 0
    early_state = jnp.where(first_core, mine[:, :HEAD_DIM], partner[:, :HEAD_DIM])
    late_state = jnp.where(first_core, partner[:, :HEAD_DIM], mine[:, :HEAD_DIM])
    early_log = jnp.where(first_core, mine[:, HEAD_DIM, 0], partner[:, HEAD_DIM, 0])
    late_log = jnp.where(first_core, partner[:, HEAD_DIM, 0], mine[:, HEAD_DIM, 0])
    pair_state = jnp.exp(late_log)[:, None, None] * early_state + late_state
    pair_log = early_log + late_log
    splits = ctx_count // half_heads
    part_rows = HEAD_DIM // splits
    pair_rows = jnp.broadcast_to(
        jnp.repeat(pair_log, splits)[:, None, None], (ctx_count, 8, STATE)
    )
    payload = jnp.concatenate(
        [pair_state.reshape(ctx_count, part_rows, STATE), pair_rows], axis=1
    )
    pair_count = ctx_count // 2
    gathered = lax.all_to_all(payload, "ctx", 0, 0, tiled=True).reshape(
        pair_count, 2, part_rows + 8, STATE
    )
    same_doc = (own_docs[:, None] == own_docs[None, :]) & (row_index[:, None] >= row_index[None, :])
    log_gap = cum_decay[:, :, :, None] - cum_decay[:, :, None, :]
    decay_matrix = jnp.exp(jnp.where(same_doc[None, None], log_gap, -jnp.inf))
    pair_products = jnp.einsum(
        "tgn,sgn->gts", state_out, state_in, preferred_element_type=jnp.float32
    )
    mixing = pair_products[:, None] * decay_matrix * step_rows[:, :, None, :]
    local_out = jnp.einsum("gjts,sgjp->tgjp", mixing, input_f32, precision=highest)
    gathered, local_out = lax.optimization_barrier((gathered, local_out))
    states_mine = gathered[:, :, :part_rows, :]
    mine_log = gathered[:, :, part_rows, 0]
    block_row = jnp.arange(pair_count, dtype=jnp.int32)
    between = (block_row[None, :, None] < block_row[None, None, :]) & (
        block_row[None, None, :] < block_row[:, None, None]
    )
    log_span = jnp.sum(
        jnp.where(between[None], jnp.transpose(mine_log)[:, None, None, :], 0.0), axis=-1
    )
    earlier = block_row[:, None] > block_row[None, :]
    transfer = jnp.where(earlier[None], jnp.exp(log_span), 0.0)
    incoming_mine = jnp.einsum("ukd,dupn->kupn", transfer, states_mine, precision=highest)
    pair_incoming = lax.all_to_all(
        incoming_mine.reshape(ctx_count, part_rows, STATE), "ctx", 0, 0, tiled=True
    ).reshape(half_heads, HEAD_DIM, STATE)
    after_early = jnp.exp(early_log)[:, None, None] * pair_incoming + early_state
    swapped = lax.ppermute(
        jnp.where(first_core, after_early, pair_incoming), "ctx", pair_swap
    )
    kept = jnp.where(first_core, pair_incoming, after_early)
    incoming = lax.dynamic_slice_in_dim(
        jnp.concatenate([swapped, kept, swapped], axis=0), (1 - core) * half_heads, heads_dev, 0
    ).reshape(groups_dev, head_group, HEAD_DIM, STATE)
    carry_weight = jnp.exp(cum_decay) * carry_mask[None, None, :]
    carried_out = (
        jnp.einsum("tgn,gjpn->tgjp", state_out.astype(jnp.float32), incoming, precision=highest)
        * jnp.transpose(carry_weight, (2, 0, 1))[..., None]
    )
    skip_rows = skip_gain.reshape(groups_dev, head_group)[None, :, :, None] * input_f32
    mixer_full = (local_out + carried_out + skip_rows).reshape(tok_rows, -1)
    gated = mixer_full * jax.nn.silu(gate.astype(jnp.float32))
    square_local = jnp.sum(gated * gated, axis=1)
    square_sum = lax.psum(square_local, "head")
    mixer_out = (
        gated
        * lax.rsqrt(square_sum / (MIXER_HEADS * HEAD_DIM) + EPSILON)[:, None]
        * norm_gain[None, :]
    ).astype(jnp.bfloat16)
    query = jnp.einsum(
        "tgf,gfo->tgo",
        mixer_out.reshape(tok_rows, groups_dev, -1),
        query_weight,
        preferred_element_type=jnp.float32,
    )
    query = query.astype(jnp.bfloat16).reshape(tok_rows, groups_dev, query_group, ATT_DIM)

    kv_local = jnp.concatenate(
        [
            keys.reshape(tok_rows, groups_dev, ATT_DIM),
            values.reshape(tok_rows, groups_dev, ATT_DIM),
        ],
        axis=2,
    )
    kv_all = lax.all_gather(kv_local, "ctx", axis=0, tiled=True)
    doc_starts = jnp.cumsum(doc_lengths) - doc_lengths
    row_low = jnp.max(
        jnp.where(doc_starts[None, :] <= own_pos[:, None], doc_starts[None, :], 0), axis=1
    )
    first_chunk = row_low[0] // KEY_CHUNK
    last_chunk = (first_pos + tok_rows - 1) // KEY_CHUNK
    group_outs = []
    for group in range(groups_dev):
        group_outs.append(
            flash_attention(
                query[:, group].reshape(tok_rows, query_group * ATT_DIM),
                kv_all[:, group],
                row_low[:, None],
                own_pos[:, None],
                first_chunk,
                last_chunk - first_chunk + 1,
            )
        )
    attn_out = jnp.concatenate(group_outs, axis=1)
    return (mixer_out, attn_out)


def solution(mesh):
    return jax.shard_map(
        shards,
        mesh=mesh,
        in_specs=(
            P("ctx", "head"),
            P("ctx", "head"),
            P("ctx", "head"),
            P("ctx", "head"),
            P("head", "ctx"),
            P("head", "ctx"),
            P("head"),
            P("head"),
            P("head", None, None),
            P("ctx", "head"),
            P("ctx", "head"),
            P(),
        ),
        out_specs=(P("ctx", "head"), P("ctx", "head")),
        check_vma=False,
    )
```

```python
import jax
import jax.numpy as jnp
from jax import lax
from jax.sharding import PartitionSpec as P
from jax.experimental import pallas as pl
from jax.experimental.pallas import tpu as pltpu

MIXER_HEADS = 256
HEAD_DIM = 64
STATE = 256
GROUPS = 8
QHEADS = 64
ATT_DIM = 128


EPSILON = 1e-05
NEG_FILL = -1e30
KEY_CHUNK = 512


def segment_ids(positions, doc_lengths):
    doc_starts = jnp.cumsum(doc_lengths) - doc_lengths
    hits = (doc_starts[None, :] <= positions[:, None]).astype(jnp.int32)
    return jnp.sum(hits, axis=1) - 1


def attention_kernel(chunk_ref, query_ref, kv_ref, low_ref, high_ref, out_ref):
    tokens = query_ref.shape[0]
    heads = query_ref.shape[1] // ATT_DIM
    rows = tokens * heads
    query_rows = jnp.concatenate(
        [query_ref[:, head * ATT_DIM : (head + 1) * ATT_DIM] for head in range(heads)], axis=0
    )
    low = jnp.concatenate([low_ref[...]] * heads, axis=0)
    high = jnp.concatenate([high_ref[...]] * heads, axis=0)

    def chunk_turn(turn, carried):
        best_old, total_old, accum_old = carried
        start = pl.multiple_of((chunk_ref[0] + turn) * KEY_CHUNK, KEY_CHUNK)
        piece = kv_ref[pl.ds(start, KEY_CHUNK), :]
        key_part = piece[:, :ATT_DIM]
        value_part = piece[:, ATT_DIM:]
        scores = lax.dot_general(
            query_rows, key_part, (((1,), (1,)), ((), ())), preferred_element_type=jnp.float32
        ) * ATT_DIM ** (-0.5)
        key_pos = start + lax.broadcasted_iota(jnp.int32, (rows, KEY_CHUNK), 1)
        visible = (key_pos >= low) & (key_pos <= high)
        scores = jnp.where(visible, scores, -jnp.inf)
        best_new = jnp.maximum(best_old, jnp.max(scores, axis=1, keepdims=True))
        weights = jnp.exp(scores - best_new)
        rescale = jnp.exp(best_old - best_new)
        total_new = total_old * rescale + jnp.sum(weights, axis=1, keepdims=True)
        accum_new = accum_old * rescale + jnp.dot(
            weights.astype(jnp.bfloat16), value_part, preferred_element_type=jnp.float32
        )
        return (best_new, total_new, accum_new)

    initial = (
        jnp.full((rows, 1), NEG_FILL, jnp.float32),
        jnp.zeros((rows, 1), jnp.float32),
        jnp.zeros((rows, ATT_DIM), jnp.float32),
    )
    _, total, accum = lax.fori_loop(0, chunk_ref[1], chunk_turn, initial)
    result = (accum / total).astype(out_ref.dtype)
    for head in range(heads):
        out_ref[:, head * ATT_DIM : (head + 1) * ATT_DIM] = result[
            head * tokens : (head + 1) * tokens
        ]


def flash_attention(query_rows, kv_rows, low, high, first_chunk, chunk_count):
    tokens = query_rows.shape[0]
    chunk_info = jnp.stack([first_chunk, chunk_count]).astype(jnp.int32)
    grid_spec = pltpu.PrefetchScalarGridSpec(
        num_scalar_prefetch=1,
        grid=(1,),
        in_specs=[
            pl.BlockSpec(query_rows.shape, lambda i, info: (0, 0)),
            pl.BlockSpec(kv_rows.shape, lambda i, info: (0, 0)),
            pl.BlockSpec((tokens, 1), lambda i, info: (0, 0)),
            pl.BlockSpec((tokens, 1), lambda i, info: (0, 0)),
        ],
        out_specs=pl.BlockSpec(query_rows.shape, lambda i, info: (0, 0)),
    )
    return pl.pallas_call(
        attention_kernel,
        grid_spec=grid_spec,
        out_shape=jax.ShapeDtypeStruct(query_rows.shape, jnp.bfloat16),
    )(chunk_info, query_rows, kv_rows, low, high)

def shards(
    mixer_input,
    gate,
    in_b,
    in_c,
    step_size,
    log_decay,
    skip_gain,
    norm_gain,
    query_weight,
    keys,
    values,
    doc_lengths,
):
    highest = lax.Precision.HIGHEST
    tok_rows = mixer_input.shape[0]
    groups_dev = query_weight.shape[0]
    heads_dev = step_size.shape[0]
    head_group = heads_dev // groups_dev
    query_group = QHEADS // GROUPS
    shard_index = lax.axis_index("ctx")
    first_pos = shard_index * tok_rows
    row_index = jnp.arange(tok_rows, dtype=jnp.int32)
    own_pos = first_pos + row_index
    own_docs = segment_ids(own_pos, doc_lengths)
    prev_doc = segment_ids(jnp.reshape(first_pos - 1, (1,)), doc_lengths)[0]
    input_f32 = mixer_input.reshape(tok_rows, groups_dev, head_group, HEAD_DIM).astype(jnp.float32)
    state_in = in_b.reshape(tok_rows, groups_dev, STATE)
    state_out = in_c.reshape(tok_rows, groups_dev, STATE)
    upper_ones = (row_index[:, None] <= row_index[None, :]).astype(jnp.float32)
    cum_decay = jnp.dot(log_decay, upper_ones, precision=highest).reshape(
        groups_dev, head_group, tok_rows
    )
    step_rows = step_size.reshape(groups_dev, head_group, tok_rows)
    last_doc = (own_docs == own_docs[-1]).astype(jnp.float32)
    end_weight = jnp.exp(cum_decay[:, :, -1:] - cum_decay) * last_doc[None, None, :] * step_rows
    weighted = input_f32 * jnp.transpose(end_weight, (2, 0, 1))[..., None]
    local_state = jnp.einsum(
        "sgjp,sgn->gjpn", weighted, state_in.astype(jnp.float32), precision=highest
    )
    carry_mask = (own_docs == prev_doc).astype(jnp.float32)
    ctx_count = lax.axis_size("ctx")
    owned = heads_dev // ctx_count
    block_log = jnp.where(carry_mask[-1] > 0, cum_decay[:, :, -1], -jnp.inf).reshape(heads_dev)
    core = shard_index % 2
    half_heads = heads_dev // 2
    pair_swap = [(source, source ^ 1) for source in range(ctx_count)]
    log_rows = jnp.broadcast_to(block_log[:, None, None], (heads_dev, 8, STATE))
    augmented = jnp.concatenate(
        [local_state.reshape(heads_dev, HEAD_DIM, STATE), log_rows], axis=1
    )
    partner = lax.ppermute(
        lax.dynamic_slice_in_dim(augmented, (1 - core) * half_heads, half_heads, 0),
        "ctx",
        pair_swap,
    )
    mine = lax.dynamic_slice_in_dim(augmented, core * half_heads, half_heads, 0)
    first_core = core == 0
    early_state = jnp.where(first_core, mine[:, :HEAD_DIM], partner[:, :HEAD_DIM])
    late_state = jnp.where(first_core, partner[:, :HEAD_DIM], mine[:, :HEAD_DIM])
    early_log = jnp.where(first_core, mine[:, HEAD_DIM, 0], partner[:, HEAD_DIM, 0])
    late_log = jnp.where(first_core, partner[:, HEAD_DIM, 0], mine[:, HEAD_DIM, 0])
    pair_state = jnp.exp(late_log)[:, None, None] * early_state + late_state
    pair_log = early_log + late_log
    splits = ctx_count // half_heads
    part_rows = HEAD_DIM // splits
    pair_rows = jnp.broadcast_to(
        jnp.repeat(pair_log, splits)[:, None, None], (ctx_count, 8, STATE)
    )
    payload = jnp.concatenate(
        [pair_state.reshape(ctx_count, part_rows, STATE), pair_rows], axis=1
    )
    pair_count = ctx_count // 2
    gathered = lax.all_to_all(payload, "ctx", 0, 0, tiled=True).reshape(
        pair_count, 2, part_rows + 8, STATE
    )
    same_doc = (own_docs[:, None] == own_docs[None, :]) & (row_index[:, None] >= row_index[None, :])
    log_gap = cum_decay[:, :, :, None] - cum_decay[:, :, None, :]
    decay_matrix = jnp.exp(jnp.where(same_doc[None, None], log_gap, -jnp.inf))
    pair_products = jnp.einsum(
        "tgn,sgn->gts", state_out, state_in, preferred_element_type=jnp.float32
    )
    mixing = pair_products[:, None] * decay_matrix * step_rows[:, :, None, :]
    local_out = jnp.einsum("gjts,sgjp->tgjp", mixing, input_f32, precision=highest)
    gathered, local_out = lax.optimization_barrier((gathered, local_out))
    states_mine = gathered[:, :, :part_rows, :]
    mine_log = gathered[:, :, part_rows, 0]
    block_row = jnp.arange(pair_count, dtype=jnp.int32)
    between = (block_row[None, :, None] < block_row[None, None, :]) & (
        block_row[None, None, :] < block_row[:, None, None]
    )
    log_span = jnp.sum(
        jnp.where(between[None], jnp.transpose(mine_log)[:, None, None, :], 0.0), axis=-1
    )
    earlier = block_row[:, None] > block_row[None, :]
    transfer = jnp.where(earlier[None], jnp.exp(log_span), 0.0)
    incoming_mine = jnp.einsum("ukd,dupn->kupn", transfer, states_mine, precision=highest)
    pair_incoming = lax.all_to_all(
        incoming_mine.reshape(ctx_count, part_rows, STATE), "ctx", 0, 0, tiled=True
    ).reshape(half_heads, HEAD_DIM, STATE)
    after_early = jnp.exp(early_log)[:, None, None] * pair_incoming + early_state
    swapped = lax.ppermute(
        jnp.where(first_core, after_early, pair_incoming), "ctx", pair_swap
    )
    kept = jnp.where(first_core, pair_incoming, after_early)
    incoming = jnp.where(
        first_core,
        jnp.concatenate([kept, swapped], axis=0),
        jnp.concatenate([swapped, kept], axis=0),
    ).reshape(groups_dev, head_group, HEAD_DIM, STATE)
    carry_weight = jnp.exp(cum_decay) * carry_mask[None, None, :]
    carried_out = (
        jnp.einsum("tgn,gjpn->tgjp", state_out.astype(jnp.float32), incoming, precision=highest)
        * jnp.transpose(carry_weight, (2, 0, 1))[..., None]
    )
    skip_rows = skip_gain.reshape(groups_dev, head_group)[None, :, :, None] * input_f32
    mixer_full = (local_out + carried_out + skip_rows).reshape(tok_rows, -1)
    gated = mixer_full * jax.nn.silu(gate.astype(jnp.float32))
    square_local = jnp.sum(gated * gated, axis=1)
    square_sum = lax.psum(square_local, "head")
    mixer_out = (
        gated
        * lax.rsqrt(square_sum / (MIXER_HEADS * HEAD_DIM) + EPSILON)[:, None]
        * norm_gain[None, :]
    ).astype(jnp.bfloat16)
    query = jnp.einsum(
        "tgf,gfo->tgo",
        mixer_out.reshape(tok_rows, groups_dev, -1),
        query_weight,
        preferred_element_type=jnp.float32,
    )
    query = query.astype(jnp.bfloat16).reshape(tok_rows, groups_dev, query_group, ATT_DIM)

    kv_local = jnp.concatenate(
        [
            keys.reshape(tok_rows, groups_dev, ATT_DIM),
            values.reshape(tok_rows, groups_dev, ATT_DIM),
        ],
        axis=2,
    )
    kv_all = lax.all_gather(kv_local, "ctx", axis=0, tiled=True)
    doc_starts = jnp.cumsum(doc_lengths) - doc_lengths
    row_low = jnp.max(
        jnp.where(doc_starts[None, :] <= own_pos[:, None], doc_starts[None, :], 0), axis=1
    )
    first_chunk = row_low[0] // KEY_CHUNK
    last_chunk = (first_pos + tok_rows - 1) // KEY_CHUNK
    group_outs = []
    for group in range(groups_dev):
        group_outs.append(
            flash_attention(
                query[:, group].reshape(tok_rows, query_group * ATT_DIM),
                kv_all[:, group],
                row_low[:, None],
                own_pos[:, None],
                first_chunk,
                last_chunk - first_chunk + 1,
            )
        )
    attn_out = jnp.concatenate(group_outs, axis=1)
    return (mixer_out, attn_out)


def solution(mesh):
    return jax.shard_map(
        shards,
        mesh=mesh,
        in_specs=(
            P("ctx", "head"),
            P("ctx", "head"),
            P("ctx", "head"),
            P("ctx", "head"),
            P("head", "ctx"),
            P("head", "ctx"),
            P("head"),
            P("head"),
            P("head", None, None),
            P("ctx", "head"),
            P("ctx", "head"),
            P(),
        ),
        out_specs=(P("ctx", "head"), P("ctx", "head")),
        check_vma=False,
    )
```
